32 devices in a mesh: head: 4 (over x, core), tok: 8 (over z, y).
Axes of the slice: x: 2, y: 2, z: 4, core: 2. Of those that a mesh axis runs over, the one named last changes fastest.
Arguments:
- tokens: bfloat16 [8, 512, 2048], P('tok', 'head'), may hold values from -6 to 6
- cache_len: int32 [8], P('tok'), may hold values from 64 to 4096, as said below
- attn_gain: float32 [2048], replicated, may hold values from 0.5 to 1.5
- w_qkv: bfloat16 [2048, 6144], P(None, 'head'), may hold values from -0.25 to 0.25
- k_cache: bfloat16 [8, 4096, 2048], P('tok', None, 'head'), may hold values from -8 to 8
- v_cache: bfloat16 [8, 4096, 2048], P('tok', None, 'head'), may hold values from -6 to 6
- w_out: bfloat16 [2048, 2048], P('head'), may hold values from -0.125 to 0.125
- moe_gain: float32 [2048], replicated, may hold values from 0.5 to 1.5
- w_shared: bfloat16 [2048, 2, 2816], P(None, None, 'head'), may hold values from -0.125 to 0.125
- w_shared_down: bfloat16 [2816, 2048], P('head'), may hold values from -0.109375 to 0.109375
- expert_ids: int32 [8, 512, 6], P('tok', 'head'), may hold values from 0 to 63, all different within a row; in each aligned block of 128 rows (0 to 127, 128 to 255, ..., all dimensions but the last counted through in order) at most 24 rows name the same one
- expert_weights: float32 [8, 512, 6], P('tok', 'head'), may hold values from 0.05 to 0.5
- expert_slot: int32 [64], replicated, may hold values from 0 to 63, each once
- w_expert: bfloat16 [2048, 2, 90112], P(None, None, ('head', 'tok')), may hold values from -0.125 to 0.125
- w_expert_down: bfloat16 [90112, 2048], P(('head', 'tok')), may hold values from -0.15625 to 0.15625
Outputs:
- layer_out: bfloat16 [8, 512, 2048], P('tok', 'head')
The draws below stay inside these ranges and needn't reach their ends.
Inputs may be any that keep to these rules, and one draw needn't show every extreme that they name: `cache_len`: Heavy-tailed over requests; some request has exactly 4096 cached tokens and some other exactly 64. `expert_ids`: each token names 6 different experts. Rows are taken in order over requests then new tokens; in each aligned block of 128 rows no expert is named by more than 24 rows, and in some block an expert is named by exactly 24. `expert_slot`: A permutation of the experts.
All inputs are finite; a program needn't handle non-finite values.
Results may differ from the reference program's by a relative error of at most 0.014.
Values may be sent and summed in bfloat16 or wider, within the bound.
No kernel may reach another device: no remote copies, remote signals or barrier semaphores. Data moves between devices by JAX's collectives and lax.ppermute only.
A program may use at most 256 MiB of HBM per device.

```python
import math
import jax
import jax.numpy as jnp
import numpy as np
from jax import lax

D = 2048
H = 16
HD = 128
E = 64
F = 1408
TOP = 6
SH = 2816
NEW_TOK = 512
CACHE = 4096
R = 8
QROWS = 128
CAP = 24
SPLIT = 1
N_HEAD = 4


def draw_cache_len(key, part):
    key_div, key_first, key_second = jax.random.split(jax.random.fold_in(key, 17), 3)
    divisor = jax.random.randint(key_div, (R,), 1, 65)
    first = jax.random.randint(key_first, (), 0, R)
    second = (first + jax.random.randint(key_second, (), 1, R)) % R
    places = jnp.arange(R, dtype=jnp.int32)
    divisor = jnp.where(places == first, 1, divisor)
    divisor = jnp.where(places == second, 64, divisor)
    return (CACHE // divisor).astype(jnp.int32)


def draw_tokens(key, part):
    shape = (R, NEW_TOK, D)
    key_base = jax.random.fold_in(key, 2)
    base = jnp.clip(jax.random.normal(key_base, shape, jnp.float32), -6.0, 6.0)
    return base.astype(jnp.bfloat16)


def draw_w_qkv(key, part):
    key_base = jax.random.fold_in(key, 1)
    spread = D ** (-0.5)
    shape = (D, 3 * H * HD)
    base = jnp.clip(jax.random.normal(key_base, shape, jnp.float32), -6.0, 6.0) * spread
    return base.astype(jnp.bfloat16)


def draw_k_cache(key, part):
    shape = (R, CACHE, H * HD)
    key_base = jax.random.fold_in(key, 3)
    base = jnp.clip(jax.random.normal(key_base, shape, jnp.float32), -8.0, 8.0)
    return base.astype(jnp.bfloat16)


def steps_of(stream_key, extent, pieces, least, high):
    loudness, own = 1.0, jax.random.fold_in(stream_key, 6)
    for axis_at, parts in pieces:
        draws = jnp.exp(jax.random.uniform(jax.random.fold_in(own, axis_at), (parts,), jnp.float32, least / len(pieces), high / len(pieces)))
        loudness = loudness * jnp.repeat(draws, extent[axis_at] // parts).reshape([-1 if axis == axis_at else 1 for axis in range(len(extent))])
    return loudness


def deal_out(rng, own, number, rows, count, top, most, skew):
    ranking = jax.random.permutation(rng, count)
    crowded, ordinary = shares(count, rows * top, most, skew, True), shares(count, rows * top, most, skew, False)
    places = jnp.arange(count)

    def named(lengths, rotation):
        used = int((lengths > 0).sum())
        fixed = max(1, used // 4)
        moved = fixed + (places - fixed + rotation * (used - fixed)) % max(1, count - fixed)
        return jnp.zeros((count,), jnp.int32).at[ranking[jnp.where(places < fixed, places, moved)]].set(jnp.asarray(lengths, jnp.int32))

    lengths = jnp.where(number % 4 == 0, named(crowded, number // 4), named(ordinary, number - number // 4 - 1))
    mixed = jax.random.permutation(jax.random.fold_in(own, 3), count)
    giver, sink = mixed[0:count // 2 * 2:2], mixed[1:count // 2 * 2:2]
    margin = jnp.minimum(lengths[giver] - 1, most - lengths[sink]) // 2
    margin = jnp.where((giver == ranking[0]) | (sink == ranking[0]) | (lengths[sink] == 0), 0, jnp.maximum(margin, 0))
    moved = jax.random.randint(jax.random.fold_in(own, 4), (count // 2,), 0, 1 << 20) % (margin + 1)
    lengths = lengths.at[giver].add(-moved).at[sink].add(moved)
    labels = jnp.searchsorted(jnp.cumsum(lengths), jnp.arange(rows * top), side="right").astype(jnp.int32)
    table = labels.reshape(top, rows).T
    table = table[jax.random.permutation(jax.random.fold_in(own, 1), rows)]
    rotation = jax.random.randint(jax.random.fold_in(own, 2), (rows, 1), 0, top)
    return jnp.take_along_axis(table, (jnp.arange(top)[None, :] + rotation) % top, axis=1)


def shares(count, total, most, slope, full):
    loads = [(1 << 20) // math.isqrt(rank ** slope) + 1 for rank in range(1, count + 1)]
    largest = most if full else min(most, max(-(-total // count), total * loads[0] // sum(loads)))
    least = 1 if total - largest >= count - 1 else 0
    given, surplus = [largest] + [least] * (count - 1), total - largest - least * (count - 1)
    while surplus > 0:
        free = [i for i in range(1, count) if given[i] < largest] or [i for i in range(1, count) if given[i] < most]
        mass, remaining = sum([loads[i] for i in free]), surplus
        for i in free:
            more = min(most - given[i], max(1, remaining * loads[i] // mass), surplus)
            given[i] = given[i] + more
            surplus = surplus - more
    return np.array(given)


def gaussian(stream_key, dims, width, limit, shards=(), kind=jnp.bfloat16):
    loudness = steps_of(stream_key, dims, shards, -0.22, 0.18) if shards else 1.0
    values = jax.random.normal(stream_key, dims, jnp.float32) * width * loudness
    return jnp.minimum(jnp.maximum(values, -limit), limit).astype(kind)


def setup_inputs(seed: int = 0) -> dict:
    seeds = jax.random.split(jax.random.key(seed), 16)
    tokens = draw_tokens(jax.random.fold_in(seeds[15], 71), 0)
    cache_len = draw_cache_len(jax.random.fold_in(seeds[15], 71), 0)
    attn_gain = jnp.clip(1.0 + 0.1 * jax.random.normal(seeds[2], (D,), jnp.float32), 0.5, 1.5)
    w_qkv = draw_w_qkv(jax.random.fold_in(seeds[15], 71), 0)
    k_cache = draw_k_cache(jax.random.fold_in(seeds[15], 71), 0)
    v_cache = gaussian(seeds[5], (R, CACHE, H * HD), 1.0, 6.0, ((0, 8), (2, 4)))
    w_out = gaussian(seeds[6], (H * HD, D), (H * HD) ** -0.5, 0.125, ((0, 4),))
    moe_gain = jnp.clip(1.0 + 0.1 * jax.random.normal(seeds[7], (D,), jnp.float32), 0.5, 1.5)
    w_shared = gaussian(seeds[8], (D, 2, SH), D ** -0.5, 0.125, ((2, 4),))
    w_shared_down = gaussian(seeds[9], (SH, D), SH ** -0.5, 0.109375, ((0, 4),))
    expert_ids_keys = jax.random.split(jax.random.fold_in(seeds[10], 1), R * NEW_TOK // QROWS)
    expert_ids_turns = jax.random.permutation(jax.random.fold_in(seeds[10], 3), R * NEW_TOK // QROWS)
    expert_ids = jax.vmap(lambda own, number: deal_out(jax.random.fold_in(seeds[10], 2), own, number, QROWS, E, TOP, CAP, 1))(expert_ids_keys, expert_ids_turns).reshape((R, NEW_TOK, TOP))
    expert_weights = jnp.clip(jnp.exp(math.log(0.5) - 2.3025851 * jax.random.uniform(seeds[11], (R, NEW_TOK, TOP), jnp.float32) ** steps_of(seeds[11], (R, NEW_TOK, TOP), ((0, 8), (1, 4)), -0.2, 0.2)), 0.05, 0.5)
    expert_slot = jax.random.permutation(seeds[12], E).astype(jnp.int32)
    w_expert = gaussian(seeds[13], (D, 2, E * F), D ** -0.5, 0.125, ((2, 32),))
    w_expert_down = gaussian(seeds[14], (E * F, D), F ** -0.5, 0.15625, ((0, 32),))
    return {"tokens": tokens, "cache_len": cache_len, "attn_gain": attn_gain, "w_qkv": w_qkv, "k_cache": k_cache, "v_cache": v_cache, "w_out": w_out, "moe_gain": moe_gain, "w_shared": w_shared, "w_shared_down": w_shared_down, "expert_ids": expert_ids, "expert_weights": expert_weights, "expert_slot": expert_slot, "w_expert": w_expert, "w_expert_down": w_expert_down}


EPS = 1e-06
NEG_BIG = -1e+30

def normalize(values, gain_vector):
    wide = values.astype(jnp.float32)
    factor = lax.rsqrt(lax.optimization_barrier(jnp.mean(wide * wide, axis=-1, keepdims=True)) + EPS)
    return (wide * factor * gain_vector).astype(jnp.bfloat16)

def rotary(vectors, positions):
    half_dim = vectors.shape[-1] // 2
    freqs = 10000.0 ** (-jnp.arange(half_dim, dtype=jnp.float32) / half_dim)
    angles = positions.astype(jnp.float32)[:, None] * freqs[None, :]
    cosine = jnp.cos(angles)[:, None, :]
    sine_part = jnp.sin(angles)[:, None, :]
    lower = vectors[..., :half_dim]
    upper = vectors[..., half_dim:]
    return jnp.concatenate([lower * cosine - upper * sine_part, upper * cosine + lower * sine_part], axis=-1)

def attend(queries, keys_new, values_new, keys_old, values_old, length):
    factor = 1.0 / math.sqrt(queries.shape[-1])
    score_old = jnp.dot(queries, keys_old.T, preferred_element_type=jnp.float32) * factor
    score_new = jnp.dot(queries, keys_new.T, preferred_element_type=jnp.float32) * factor
    old_slots = jnp.arange(keys_old.shape[0], dtype=jnp.int32)
    live_old = (old_slots < length)[None, :]
    new_slots = jnp.arange(queries.shape[0], dtype=jnp.int32)
    live_new = new_slots[None, :] <= new_slots[:, None]
    row_max = jnp.maximum(lax.optimization_barrier(jnp.max(jnp.where(live_old, score_old, NEG_BIG), axis=1)), lax.optimization_barrier(jnp.max(jnp.where(live_new, score_new, NEG_BIG), axis=1)))
    prob_old = jnp.where(live_old, jnp.exp(score_old - row_max[:, None]), 0.0)
    prob_new = jnp.where(live_new, jnp.exp(score_new - row_max[:, None]), 0.0)
    denom = lax.optimization_barrier(jnp.sum(prob_old, axis=1)) + lax.optimization_barrier(jnp.sum(prob_new, axis=1))
    weighted = jnp.dot(prob_old.astype(jnp.bfloat16), values_old, preferred_element_type=jnp.float32)
    weighted = weighted + jnp.dot(prob_new.astype(jnp.bfloat16), values_new, preferred_element_type=jnp.float32)
    return (weighted / denom[:, None]).astype(jnp.bfloat16)

def rounded_sum(left, right, groups):
    inner = left.shape[1] // groups
    result = jnp.zeros((left.shape[0], right.shape[1]), jnp.float32)
    for group in range(groups):
        partial_sum = jnp.dot(left[:, group * inner:(group + 1) * inner], right[group * inner:(group + 1) * inner], preferred_element_type=jnp.float32)
        result = result + lax.optimization_barrier(partial_sum.astype(jnp.bfloat16)).astype(jnp.float32)
    return result

def reference(tokens, cache_len, attn_gain, w_qkv, k_cache, v_cache, w_out, moe_gain, w_shared, w_shared_down, expert_ids, expert_weights, expert_slot, w_expert, w_expert_down):

    def one_request(inputs):
        hidden_in, length, keys_old, values_old = inputs
        normed = normalize(hidden_in, attn_gain)
        qkv = jnp.dot(normed, w_qkv, preferred_element_type=jnp.float32).reshape(NEW_TOK, H, 3, HD)
        positions = length + jnp.arange(NEW_TOK, dtype=jnp.int32)
        queries = rotary(qkv[:, :, 0], positions).astype(jnp.bfloat16)
        keys_new = rotary(qkv[:, :, 1], positions).astype(jnp.bfloat16)
        values_new = qkv[:, :, 2].astype(jnp.bfloat16)
        keys_old = keys_old.reshape(CACHE, H, HD)
        values_old = values_old.reshape(CACHE, H, HD)
        heads_out = jax.vmap(attend, in_axes=(1, 1, 1, 1, 1, None), out_axes=1)(queries, keys_new, values_new, keys_old, values_old, length)
        return heads_out.reshape(NEW_TOK, H * HD)
    attn_heads = lax.map(one_request, (tokens, cache_len, k_cache, v_cache))
    token_count = R * NEW_TOK
    attn_proj = rounded_sum(attn_heads.reshape(token_count, H * HD), w_out, N_HEAD)
    middle = (tokens.reshape(token_count, D).astype(jnp.float32) + attn_proj).astype(jnp.bfloat16)
    normed_mid = normalize(middle, moe_gain)
    shared_gate = jnp.dot(normed_mid, w_shared[:, 0, :], preferred_element_type=jnp.float32)
    shared_up = jnp.dot(normed_mid, w_shared[:, 1, :], preferred_element_type=jnp.float32)
    shared_hidden = (jax.nn.silu(shared_gate) * shared_up).astype(jnp.bfloat16)
    shared_out = rounded_sum(shared_hidden, w_shared_down, N_HEAD)
    flat_ids = expert_ids.reshape(-1)
    flat_weights = expert_weights.reshape(-1)
    owners = jnp.arange(token_count * TOP, dtype=jnp.int32) // TOP
    most_rows = R * N_HEAD * CAP

    def one_expert(expert, routed):
        selected = flat_ids == expert
        ranks = jnp.cumsum(selected.astype(jnp.int32)) - 1
        target = jnp.where(selected, ranks, most_rows)
        row_index = jnp.zeros((most_rows,), jnp.int32).at[target].set(owners, mode='drop')
        row_weight = jnp.zeros((most_rows,), jnp.float32).at[target].set(flat_weights, mode='drop')
        place = expert_slot[expert]
        w_pair = lax.dynamic_slice_in_dim(w_expert, place * F, F, 2)
        w_down = lax.dynamic_slice_in_dim(w_expert_down, place * F, F, 0)
        rows_in = normed_mid[row_index]
        gate_part = jnp.dot(rows_in, w_pair[:, 0, :], preferred_element_type=jnp.float32)
        up_part = jnp.dot(rows_in, w_pair[:, 1, :], preferred_element_type=jnp.float32)
        hidden_part = (jax.nn.silu(gate_part) * up_part).astype(jnp.bfloat16)
        expert_out = rounded_sum(hidden_part, w_down, SPLIT)
        return routed.at[row_index].add(row_weight[:, None] * expert_out)
    routed_out = lax.fori_loop(0, E, one_expert, jnp.zeros((token_count, D), jnp.float32))
    layer_out = (middle.astype(jnp.float32) + shared_out + routed_out).astype(jnp.bfloat16)
    return layer_out.reshape(R, NEW_TOK, D)
```

```python
import math

import jax
import jax.numpy as jnp
from jax import lax
from jax.sharding import PartitionSpec as P

HD = 128
E = 64
TOP = 6


EPS = 1e-06
NEG_BIG = -1e30
CHUNKS = 2


def normalize(values, gain_vector):
    wide = values.astype(jnp.float32)
    factor = lax.rsqrt(jnp.mean(wide * wide, axis=-1, keepdims=True) + EPS)
    return (wide * factor * gain_vector).astype(jnp.bfloat16)


def rotary(vectors, positions):
    half_dim = vectors.shape[-1] // 2
    freqs = 10000.0 ** (-jnp.arange(half_dim, dtype=jnp.float32) / half_dim)
    angles = positions.astype(jnp.float32)[:, None] * freqs[None, :]
    cosine = jnp.cos(angles)[:, None, :]
    sine_part = jnp.sin(angles)[:, None, :]
    lower = vectors[..., :half_dim]
    upper = vectors[..., half_dim:]
    return jnp.concatenate(
        [lower * cosine - upper * sine_part, upper * cosine + lower * sine_part], axis=-1
    )


def attend(queries, keys_new, values_new, keys_old, values_old, length):
    factor = 1.0 / math.sqrt(queries.shape[-1])
    score_old = jnp.dot(queries, keys_old.T, preferred_element_type=jnp.float32) * factor
    score_new = jnp.dot(queries, keys_new.T, preferred_element_type=jnp.float32) * factor
    old_slots = jnp.arange(keys_old.shape[0], dtype=jnp.int32)
    live_old = (old_slots < length)[None, :]
    new_slots = jnp.arange(queries.shape[0], dtype=jnp.int32)
    live_new = new_slots[None, :] <= new_slots[:, None]
    row_max = jnp.maximum(
        jnp.max(jnp.where(live_old, score_old, NEG_BIG), axis=1),
        jnp.max(jnp.where(live_new, score_new, NEG_BIG), axis=1),
    )
    prob_old = jnp.where(live_old, jnp.exp(score_old - row_max[:, None]), 0.0)
    prob_new = jnp.where(live_new, jnp.exp(score_new - row_max[:, None]), 0.0)
    denom = jnp.sum(prob_old, axis=1) + jnp.sum(prob_new, axis=1)
    weighted = jnp.dot(
        prob_old.astype(jnp.bfloat16), values_old, preferred_element_type=jnp.float32
    )
    weighted = weighted + jnp.dot(
        prob_new.astype(jnp.bfloat16), values_new, preferred_element_type=jnp.float32
    )
    return (weighted / denom[:, None]).astype(jnp.bfloat16)


def body(
    tokens,
    cache_len,
    attn_gain,
    w_qkv,
    k_cache,
    v_cache,
    w_out,
    moe_gain,
    w_shared,
    w_shared_down,
    expert_ids,
    expert_weights,
    expert_slot,
    w_expert,
    w_expert_down,
):
    req_local, qrows, width = tokens.shape
    head_count = lax.axis_size("head")
    tok_count = lax.axis_size("tok")
    new_len = qrows * head_count
    head_local = w_out.shape[0] // HD
    cache_rows = k_cache.shape[1]
    normed = normalize(lax.all_gather(tokens, "head", axis=1, tiled=True), attn_gain)
    qkv = jnp.einsum("rcd,dk->rck", normed, w_qkv, preferred_element_type=jnp.float32)
    parts = qkv.reshape(req_local, new_len, head_local, 3, HD)
    length = cache_len[0]
    positions = length + jnp.arange(new_len, dtype=jnp.int32)
    queries = rotary(parts[0, :, :, 0], positions).astype(jnp.bfloat16)
    keys_new = rotary(parts[0, :, :, 1], positions).astype(jnp.bfloat16)
    values_new = parts[0, :, :, 2].astype(jnp.bfloat16)
    keys_old = k_cache[0].reshape(cache_rows, head_local, HD)
    values_old = v_cache[0].reshape(cache_rows, head_local, HD)
    attention_heads_out = jax.vmap(attend, in_axes=(1, 1, 1, 1, 1, None), out_axes=1)(
        queries, keys_new, values_new, keys_old, values_old, length
    )
    outputs = [attention_heads_out.reshape(new_len, head_local * HD)]
    heads_out = jnp.stack(outputs, axis=1)
    row_block = heads_out
    attn_rows = lax.psum_scatter(
        jnp.einsum("crk,kd->crd", row_block, w_out, preferred_element_type=jnp.float32).astype(
            jnp.bfloat16
        ),
        "head",
        scatter_dimension=0,
        tiled=True,
    ).astype(jnp.float32)
    middle = (tokens.astype(jnp.float32) + jnp.transpose(attn_rows, (1, 0, 2))).astype(jnp.bfloat16)
    normed_mid = normalize(middle, moe_gain)
    gate_up = jnp.einsum(
        "rcd,djz->jcrz",
        lax.all_gather(normed_mid, "head", axis=1, tiled=True),
        w_shared,
        preferred_element_type=jnp.float32,
    )
    hidden_rows = (jax.nn.silu(gate_up[0]) * gate_up[1]).astype(jnp.bfloat16)
    row_block = hidden_rows
    shared_rows = lax.psum_scatter(
        jnp.einsum(
            "crz,zd->crd", row_block, w_shared_down, preferred_element_type=jnp.float32
        ).astype(jnp.bfloat16),
        "head",
        scatter_dimension=0,
        tiled=True,
    ).astype(jnp.float32)
    capacity = 2 * qrows * TOP // E
    slots = req_local * capacity
    local_rows = req_local * qrows
    flat_ids = expert_ids.reshape(req_local, qrows * TOP)
    hits = (flat_ids[:, :, None] == jnp.arange(E, dtype=jnp.int32)[None, None, :]).astype(jnp.int32)
    ranks = jnp.sum((jnp.cumsum(hits, axis=1) - 1) * hits, axis=2)
    slot_of = ranks + jnp.arange(req_local, dtype=jnp.int32)[:, None] * capacity
    place_of = jnp.sum(hits * expert_slot[None, None, :], axis=2)
    target = (place_of * slots + slot_of).reshape(local_rows, TOP)
    columns = jnp.arange(E * slots, dtype=jnp.int32)
    matches = (target[:, :, None] == columns[None, None, :]).astype(jnp.float32)
    placement = jnp.sum(matches, axis=1).astype(jnp.bfloat16)
    routing_matrix = jnp.sum(matches * expert_weights.reshape(local_rows, TOP)[:, :, None], axis=1)
    flat_mid = normed_mid.reshape(local_rows, width)
    outgoing = lax.dot_general(
        placement, flat_mid, (((0,), (0,)), ((), ())), preferred_element_type=jnp.float32
    ).astype(jnp.bfloat16)
    devices = head_count * tok_count
    per_device = max(1, E // devices)
    copies = max(1, devices // E)
    outgoing = outgoing.reshape(E, 1, slots, width)
    if copies > 1:
        outgoing = jnp.broadcast_to(outgoing, (E, copies, slots, width))
    outgoing = outgoing.reshape(devices, per_device, slots, width)
    unit_count = w_expert.shape[2] // per_device
    w_down = w_expert_down.reshape(per_device, unit_count, width)
    chunks = CHUNKS if slots % CHUNKS == 0 else 1
    step = slots // chunks
    received = [
        lax.all_to_all(
            outgoing[:, :, c * step : (c + 1) * step],
            ("head", "tok"),
            split_axis=0,
            concat_axis=0,
            tiled=True,
        )
        for c in range(chunks)
    ]
    received[0], shared_rows = lax.optimization_barrier((received[0], shared_rows))
    returned_parts = []
    for c in range(chunks):
        expert_parts = []
        for e in range(per_device):
            w_pair = w_expert[:, :, e * unit_count : (e + 1) * unit_count]
            gate_up = jnp.einsum(
                "gsd,dju->jgsu", received[c][:, e], w_pair, preferred_element_type=jnp.float32
            )
            hidden_part = (jax.nn.silu(gate_up[0]) * gate_up[1]).astype(jnp.bfloat16)
            expert_parts.append(
                jnp.einsum(
                    "gsu,ud->gsd", hidden_part, w_down[e], preferred_element_type=jnp.float32
                ).astype(jnp.bfloat16)
            )
        partial_out = jnp.stack(expert_parts, axis=1)
        returned_parts.append(
            lax.all_to_all(partial_out, ("head", "tok"), split_axis=0, concat_axis=0, tiled=True)
        )
    returned = jnp.concatenate(returned_parts, axis=2)
    summed = jnp.sum(returned.reshape(E, copies, slots, width).astype(jnp.float32), axis=1)
    routed = jnp.dot(
        routing_matrix,
        summed.reshape(E * slots, width),
        precision=lax.Precision.HIGHEST,
        preferred_element_type=jnp.float32,
    )
    routed = routed.reshape(req_local, qrows, width)
    layer_out = middle.astype(jnp.float32) + jnp.transpose(shared_rows, (1, 0, 2)) + routed
    return layer_out.astype(jnp.bfloat16)


def solution(mesh):
    return jax.shard_map(
        body,
        mesh=mesh,
        in_specs=(
            P("tok", "head", None),
            P("tok"),
            P(),
            P(None, "head"),
            P("tok", None, "head"),
            P("tok", None, "head"),
            P("head", None),
            P(),
            P(None, None, "head"),
            P("head", None),
            P("tok", "head", None),
            P("tok", "head", None),
            P(),
            P(None, None, ("head", "tok")),
            P(("head", "tok"), None),
        ),
        out_specs=P("tok", "head", None),
        check_vma=False,
    )
```

```python
import math

import jax
import jax.numpy as jnp
from jax import lax
from jax.experimental import pallas as pl
from jax.experimental.pallas import tpu as pltpu
from jax.sharding import PartitionSpec as P

HD = 128
E = 64
TOP = 6


EPS = 1e-06
NEG_BIG = -1e30
CHUNKS = 2


def normalize(values, gain_vector):
    wide = values.astype(jnp.float32)
    factor = lax.rsqrt(jnp.mean(wide * wide, axis=-1, keepdims=True) + EPS)
    return (wide * factor * gain_vector).astype(jnp.bfloat16)


def rotary(vectors, positions):
    half_dim = vectors.shape[-1] // 2
    freqs = 10000.0 ** (-jnp.arange(half_dim, dtype=jnp.float32) / half_dim)
    angles = positions.astype(jnp.float32)[:, None] * freqs[None, :]
    cosine = jnp.cos(angles)[:, None, :]
    sine_part = jnp.sin(angles)[:, None, :]
    lower = vectors[..., :half_dim]
    upper = vectors[..., half_dim:]
    return jnp.concatenate(
        [lower * cosine - upper * sine_part, upper * cosine + lower * sine_part], axis=-1
    )


def attend(queries, keys_new, values_new, keys_old, values_old, length):
    factor = 1.0 / math.sqrt(queries.shape[-1])
    score_old = jnp.dot(queries, keys_old.T, preferred_element_type=jnp.float32) * factor
    score_new = jnp.dot(queries, keys_new.T, preferred_element_type=jnp.float32) * factor
    old_slots = jnp.arange(keys_old.shape[0], dtype=jnp.int32)
    live_old = (old_slots < length)[None, :]
    new_slots = jnp.arange(queries.shape[0], dtype=jnp.int32)
    live_new = new_slots[None, :] <= new_slots[:, None]
    row_max = jnp.maximum(
        jnp.max(jnp.where(live_old, score_old, NEG_BIG), axis=1),
        jnp.max(jnp.where(live_new, score_new, NEG_BIG), axis=1),
    )
    prob_old = jnp.where(live_old, jnp.exp(score_old - row_max[:, None]), 0.0)
    prob_new = jnp.where(live_new, jnp.exp(score_new - row_max[:, None]), 0.0)
    denom = jnp.sum(prob_old, axis=1) + jnp.sum(prob_new, axis=1)
    weighted = jnp.dot(
        prob_old.astype(jnp.bfloat16), values_old, preferred_element_type=jnp.float32
    )
    weighted = weighted + jnp.dot(
        prob_new.astype(jnp.bfloat16), values_new, preferred_element_type=jnp.float32
    )
    return (weighted / denom[:, None]).astype(jnp.bfloat16)


def attention_kernel(len_ref, q_ref, kn_ref, vn_ref, ko_ref, vo_ref, o_ref):
    rows = q_ref.shape[0]
    new_len = kn_ref.shape[0]
    cache_rows = ko_ref.shape[1]
    length = len_ref[0]
    start = pl.program_id(1) * rows
    factor = 1.0 / math.sqrt(q_ref.shape[-1])
    contract = (((1,), (1,)), ((), ()))
    queries = q_ref[...]
    score_old = (
        lax.dot_general(queries, ko_ref[0], contract, preferred_element_type=jnp.float32) * factor
    )
    score_new = (
        lax.dot_general(queries, kn_ref[...], contract, preferred_element_type=jnp.float32)
        * factor
    )
    live_old = lax.broadcasted_iota(jnp.int32, (rows, cache_rows), 1) < length
    new_cols = lax.broadcasted_iota(jnp.int32, (rows, new_len), 1)
    new_rows = lax.broadcasted_iota(jnp.int32, (rows, new_len), 0) + start
    live_new = new_cols <= new_rows
    row_max = jnp.maximum(
        jnp.max(jnp.where(live_old, score_old, NEG_BIG), axis=1, keepdims=True),
        jnp.max(jnp.where(live_new, score_new, NEG_BIG), axis=1, keepdims=True),
    )
    prob_old = jnp.where(live_old, jnp.exp(score_old - row_max), 0.0)
    prob_new = jnp.where(live_new, jnp.exp(score_new - row_max), 0.0)
    denom = jnp.sum(prob_old, axis=1, keepdims=True) + jnp.sum(prob_new, axis=1, keepdims=True)
    weighted = jnp.dot(
        prob_old.astype(jnp.bfloat16), vo_ref[0], preferred_element_type=jnp.float32
    )
    weighted = weighted + jnp.dot(
        prob_new.astype(jnp.bfloat16), vn_ref[...], preferred_element_type=jnp.float32
    )
    o_ref[...] = (weighted / denom).astype(o_ref.dtype)


def attention(length, queries, keys_new, values_new, k_cache, v_cache):
    new_len, columns = queries.shape
    cache_rows = k_cache.shape[1]
    heads = columns // HD
    rows = min(128, new_len)
    grid_spec = pltpu.PrefetchScalarGridSpec(
        num_scalar_prefetch=1,
        grid=(heads, new_len // rows),
        in_specs=[
            pl.BlockSpec((rows, HD), lambda h, i, n: (i, h)),
            pl.BlockSpec((new_len, HD), lambda h, i, n: (0, h)),
            pl.BlockSpec((new_len, HD), lambda h, i, n: (0, h)),
            pl.BlockSpec((1, cache_rows, HD), lambda h, i, n: (0, 0, h)),
            pl.BlockSpec((1, cache_rows, HD), lambda h, i, n: (0, 0, h)),
        ],
        out_specs=pl.BlockSpec((rows, HD), lambda h, i, n: (i, h)),
    )
    return pl.pallas_call(
        attention_kernel,
        grid_spec=grid_spec,
        out_shape=jax.ShapeDtypeStruct((new_len, columns), jnp.bfloat16),
        name="cached_attention",
    )(length, queries, keys_new, values_new, k_cache, v_cache)


def body(
    tokens,
    cache_len,
    attn_gain,
    w_qkv,
    k_cache,
    v_cache,
    w_out,
    moe_gain,
    w_shared,
    w_shared_down,
    expert_ids,
    expert_weights,
    expert_slot,
    w_expert,
    w_expert_down,
):
    req_local, qrows, width = tokens.shape
    head_count = lax.axis_size("head")
    tok_count = lax.axis_size("tok")
    new_len = qrows * head_count
    head_local = w_out.shape[0] // HD
    cache_rows = k_cache.shape[1]
    normed = normalize(lax.all_gather(tokens, "head", axis=1, tiled=True), attn_gain)
    qkv = jnp.einsum("rcd,dk->rck", normed, w_qkv, preferred_element_type=jnp.float32)
    parts = qkv.reshape(req_local, new_len, head_local, 3, HD)
    length = cache_len[0]
    positions = length + jnp.arange(new_len, dtype=jnp.int32)
    queries = rotary(parts[0, :, :, 0], positions).astype(jnp.bfloat16)
    keys_new = rotary(parts[0, :, :, 1], positions).astype(jnp.bfloat16)
    values_new = parts[0, :, :, 2].astype(jnp.bfloat16)
    flat = (new_len, head_local * HD)
    outputs = [
        attention(
            cache_len,
            queries.reshape(flat),
            keys_new.reshape(flat),
            values_new.reshape(flat),
            k_cache,
            v_cache,
        )
    ]
    heads_out = jnp.stack(outputs, axis=1)
    row_block = heads_out
    attn_rows = lax.psum_scatter(
        jnp.einsum("crk,kd->crd", row_block, w_out, preferred_element_type=jnp.float32).astype(
            jnp.bfloat16
        ),
        "head",
        scatter_dimension=0,
        tiled=True,
    ).astype(jnp.float32)
    middle = (tokens.astype(jnp.float32) + jnp.transpose(attn_rows, (1, 0, 2))).astype(jnp.bfloat16)
    normed_mid = normalize(middle, moe_gain)
    gate_up = jnp.einsum(
        "rcd,djz->jcrz",
        lax.all_gather(normed_mid, "head", axis=1, tiled=True),
        w_shared,
        preferred_element_type=jnp.float32,
    )
    hidden_rows = (jax.nn.silu(gate_up[0]) * gate_up[1]).astype(jnp.bfloat16)
    row_block = hidden_rows
    shared_rows = lax.psum_scatter(
        jnp.einsum(
            "crz,zd->crd", row_block, w_shared_down, preferred_element_type=jnp.float32
        ).astype(jnp.bfloat16),
        "head",
        scatter_dimension=0,
        tiled=True,
    ).astype(jnp.float32)
    capacity = 2 * qrows * TOP // E
    slots = req_local * capacity
    local_rows = req_local * qrows
    flat_ids = expert_ids.reshape(req_local, qrows * TOP)
    hits = (flat_ids[:, :, None] == jnp.arange(E, dtype=jnp.int32)[None, None, :]).astype(jnp.int32)
    ranks = jnp.sum((jnp.cumsum(hits, axis=1) - 1) * hits, axis=2)
    slot_of = ranks + jnp.arange(req_local, dtype=jnp.int32)[:, None] * capacity
    place_of = jnp.sum(hits * expert_slot[None, None, :], axis=2)
    target = (place_of * slots + slot_of).reshape(local_rows, TOP)
    columns = jnp.arange(E * slots, dtype=jnp.int32)
    matches = (target[:, :, None] == columns[None, None, :]).astype(jnp.float32)
    placement = jnp.sum(matches, axis=1).astype(jnp.bfloat16)
    routing_matrix = jnp.sum(matches * expert_weights.reshape(local_rows, TOP)[:, :, None], axis=1)
    flat_mid = normed_mid.reshape(local_rows, width)
    outgoing = lax.dot_general(
        placement, flat_mid, (((0,), (0,)), ((), ())), preferred_element_type=jnp.float32
    ).astype(jnp.bfloat16)
    devices = head_count * tok_count
    per_device = max(1, E // devices)
    copies = max(1, devices // E)
    outgoing = outgoing.reshape(E, 1, slots, width)
    if copies > 1:
        outgoing = jnp.broadcast_to(outgoing, (E, copies, slots, width))
    outgoing = outgoing.reshape(devices, per_device, slots, width)
    unit_count = w_expert.shape[2] // per_device
    w_down = w_expert_down.reshape(per_device, unit_count, width)
    chunks = CHUNKS if slots % CHUNKS == 0 else 1
    step = slots // chunks
    received = [
        lax.all_to_all(
            outgoing[:, :, c * step : (c + 1) * step],
            ("head", "tok"),
            split_axis=0,
            concat_axis=0,
            tiled=True,
        )
        for c in range(chunks)
    ]
    received[0], shared_rows = lax.optimization_barrier((received[0], shared_rows))
    returned_parts = []
    for c in range(chunks):
        expert_parts = []
        for e in range(per_device):
            w_pair = w_expert[:, :, e * unit_count : (e + 1) * unit_count]
            gate_up = jnp.einsum(
                "gsd,dju->jgsu", received[c][:, e], w_pair, preferred_element_type=jnp.float32
            )
            hidden_part = (jax.nn.silu(gate_up[0]) * gate_up[1]).astype(jnp.bfloat16)
            expert_parts.append(
                jnp.einsum(
                    "gsu,ud->gsd", hidden_part, w_down[e], preferred_element_type=jnp.float32
                ).astype(jnp.bfloat16)
            )
        partial_out = jnp.stack(expert_parts, axis=1)
        returned_parts.append(
            lax.all_to_all(partial_out, ("head", "tok"), split_axis=0, concat_axis=0, tiled=True)
        )
    returned = jnp.concatenate(returned_parts, axis=2)
    summed = jnp.sum(returned.reshape(E, copies, slots, width).astype(jnp.float32), axis=1)
    routed = jnp.dot(
        routing_matrix,
        summed.reshape(E * slots, width),
        precision=lax.Precision.HIGHEST,
        preferred_element_type=jnp.float32,
    )
    routed = routed.reshape(req_local, qrows, width)
    layer_out = middle.astype(jnp.float32) + jnp.transpose(shared_rows, (1, 0, 2)) + routed
    return layer_out.astype(jnp.bfloat16)


def solution(mesh):
    return jax.shard_map(
        body,
        mesh=mesh,
        in_specs=(
            P("tok", "head", None),
            P("tok"),
            P(),
            P(None, "head"),
            P("tok", None, "head"),
            P("tok", None, "head"),
            P("head", None),
            P(),
            P(None, None, "head"),
            P("head", None),
            P("tok", "head", None),
            P("tok", "head", None),
            P(),
            P(None, None, ("head", "tok")),
            P(("head", "tok"), None),
        ),
        out_specs=P("tok", "head", None),
        check_vma=False,
    )
```

```python
import math

import jax
import jax.numpy as jnp
from jax import lax
from jax.experimental import pallas as pl
from jax.experimental.pallas import tpu as pltpu
from jax.sharding import PartitionSpec as P

HD = 128
E = 64
TOP = 6


EPS = 1e-06
NEG_BIG = -1e30
CHUNKS = 2


def normalize(values, gain_vector):
    wide = values.astype(jnp.float32)
    factor = lax.rsqrt(jnp.mean(wide * wide, axis=-1, keepdims=True) + EPS)
    return (wide * factor * gain_vector).astype(jnp.bfloat16)


def rotary(vectors, positions):
    half_dim = vectors.shape[-1] // 2
    freqs = 10000.0 ** (-jnp.arange(half_dim, dtype=jnp.float32) / half_dim)
    angles = positions.astype(jnp.float32)[:, None] * freqs[None, :]
    cosine = jnp.cos(angles)[:, None, :]
    sine_part = jnp.sin(angles)[:, None, :]
    lower = vectors[..., :half_dim]
    upper = vectors[..., half_dim:]
    return jnp.concatenate(
        [lower * cosine - upper * sine_part, upper * cosine + lower * sine_part], axis=-1
    )


def attend(queries, keys_new, values_new, keys_old, values_old, length):
    factor = 1.0 / math.sqrt(queries.shape[-1])
    score_old = jnp.dot(queries, keys_old.T, preferred_element_type=jnp.float32) * factor
    score_new = jnp.dot(queries, keys_new.T, preferred_element_type=jnp.float32) * factor
    old_slots = jnp.arange(keys_old.shape[0], dtype=jnp.int32)
    live_old = (old_slots < length)[None, :]
    new_slots = jnp.arange(queries.shape[0], dtype=jnp.int32)
    live_new = new_slots[None, :] <= new_slots[:, None]
    row_max = jnp.maximum(
        jnp.max(jnp.where(live_old, score_old, NEG_BIG), axis=1),
        jnp.max(jnp.where(live_new, score_new, NEG_BIG), axis=1),
    )
    prob_old = jnp.where(live_old, jnp.exp(score_old - row_max[:, None]), 0.0)
    prob_new = jnp.where(live_new, jnp.exp(score_new - row_max[:, None]), 0.0)
    denom = jnp.sum(prob_old, axis=1) + jnp.sum(prob_new, axis=1)
    weighted = jnp.dot(
        prob_old.astype(jnp.bfloat16), values_old, preferred_element_type=jnp.float32
    )
    weighted = weighted + jnp.dot(
        prob_new.astype(jnp.bfloat16), values_new, preferred_element_type=jnp.float32
    )
    return (weighted / denom[:, None]).astype(jnp.bfloat16)


def rotate(block, cosine, sine_signed):
    half = block.shape[-1] // 2
    return block * cosine + pltpu.roll(block, half, 1) * sine_signed


def attention_kernel(
    len_ref, q_ref, kn_ref, vn_ref, cq_ref, sq_ref, ck_ref, sk_ref, ko_ref, vo_ref, o_ref
):
    rows = q_ref.shape[0]
    new_len = kn_ref.shape[0]
    cache_rows = ko_ref.shape[1]
    length = len_ref[0]
    start = pl.program_id(1) * rows
    factor = 1.0 / math.sqrt(q_ref.shape[-1])
    contract = (((1,), (1,)), ((), ()))
    queries = rotate(q_ref[...], cq_ref[...], sq_ref[...]).astype(jnp.bfloat16)
    keys_new = rotate(kn_ref[...], ck_ref[...], sk_ref[...]).astype(jnp.bfloat16)
    values_new = vn_ref[...].astype(jnp.bfloat16)
    score_old = (
        lax.dot_general(queries, ko_ref[0], contract, preferred_element_type=jnp.float32) * factor
    )
    score_new = (
        lax.dot_general(queries, keys_new, contract, preferred_element_type=jnp.float32) * factor
    )
    live_old = lax.broadcasted_iota(jnp.int32, (rows, cache_rows), 1) < length
    new_cols = lax.broadcasted_iota(jnp.int32, (rows, new_len), 1)
    new_rows = lax.broadcasted_iota(jnp.int32, (rows, new_len), 0) + start
    live_new = new_cols <= new_rows
    row_max = jnp.maximum(
        jnp.max(jnp.where(live_old, score_old, NEG_BIG), axis=1, keepdims=True),
        jnp.max(jnp.where(live_new, score_new, NEG_BIG), axis=1, keepdims=True),
    )
    prob_old = jnp.where(live_old, jnp.exp(score_old - row_max), 0.0)
    prob_new = jnp.where(live_new, jnp.exp(score_new - row_max), 0.0)
    denom = jnp.sum(prob_old, axis=1, keepdims=True) + jnp.sum(prob_new, axis=1, keepdims=True)
    weighted = jnp.dot(
        prob_old.astype(jnp.bfloat16), vo_ref[0], preferred_element_type=jnp.float32
    )
    weighted = weighted + jnp.dot(
        prob_new.astype(jnp.bfloat16), values_new, preferred_element_type=jnp.float32
    )
    o_ref[...] = (weighted / denom).astype(o_ref.dtype)


def attention(length, qkv, cosine, sine_signed, k_cache, v_cache):
    new_len = qkv.shape[0]
    cache_rows = k_cache.shape[1]
    heads = qkv.shape[1] // (3 * HD)
    rows = min(128, new_len)
    grid_spec = pltpu.PrefetchScalarGridSpec(
        num_scalar_prefetch=1,
        grid=(heads, new_len // rows),
        in_specs=[
            pl.BlockSpec((rows, HD), lambda h, i, n: (i, 3 * h)),
            pl.BlockSpec((new_len, HD), lambda h, i, n: (0, 3 * h + 1)),
            pl.BlockSpec((new_len, HD), lambda h, i, n: (0, 3 * h + 2)),
            pl.BlockSpec((rows, HD), lambda h, i, n: (i, 0)),
            pl.BlockSpec((rows, HD), lambda h, i, n: (i, 0)),
            pl.BlockSpec((new_len, HD), lambda h, i, n: (0, 0)),
            pl.BlockSpec((new_len, HD), lambda h, i, n: (0, 0)),
            pl.BlockSpec((1, cache_rows, HD), lambda h, i, n: (0, 0, h)),
            pl.BlockSpec((1, cache_rows, HD), lambda h, i, n: (0, 0, h)),
        ],
        out_specs=pl.BlockSpec((rows, HD), lambda h, i, n: (i, h)),
    )
    return pl.pallas_call(
        attention_kernel,
        grid_spec=grid_spec,
        out_shape=jax.ShapeDtypeStruct((new_len, heads * HD), jnp.bfloat16),
        name="cached_attention",
    )(length, qkv, qkv, qkv, cosine, sine_signed, cosine, sine_signed, k_cache, v_cache)


def body(
    tokens,
    cache_len,
    attn_gain,
    w_qkv,
    k_cache,
    v_cache,
    w_out,
    moe_gain,
    w_shared,
    w_shared_down,
    expert_ids,
    expert_weights,
    expert_slot,
    w_expert,
    w_expert_down,
):
    req_local, qrows, width = tokens.shape
    head_count = lax.axis_size("head")
    tok_count = lax.axis_size("tok")
    new_len = qrows * head_count
    head_local = w_out.shape[0] // HD
    cache_rows = k_cache.shape[1]
    normed = normalize(lax.all_gather(tokens, "head", axis=1, tiled=True), attn_gain)
    qkv = jnp.dot(normed[0], w_qkv, preferred_element_type=jnp.float32)
    length = cache_len[0]
    positions = length + jnp.arange(new_len, dtype=jnp.int32)
    half_dim = HD // 2
    freqs = 10000.0 ** (-jnp.arange(half_dim, dtype=jnp.float32) / half_dim)
    angles = positions.astype(jnp.float32)[:, None] * freqs[None, :]
    cosine = jnp.cos(angles)
    sine_part = jnp.sin(angles)
    cosine = jnp.concatenate([cosine, cosine], axis=1)
    sine_signed = jnp.concatenate([-sine_part, sine_part], axis=1)
    outputs = [attention(cache_len, qkv, cosine, sine_signed, k_cache, v_cache)]
    heads_out = jnp.stack(outputs, axis=1)
    row_block = heads_out
    attn_rows = lax.psum_scatter(
        jnp.einsum("crk,kd->crd", row_block, w_out, preferred_element_type=jnp.float32).astype(
            jnp.bfloat16
        ),
        "head",
        scatter_dimension=0,
        tiled=True,
    ).astype(jnp.float32)
    middle = (tokens.astype(jnp.float32) + jnp.transpose(attn_rows, (1, 0, 2))).astype(jnp.bfloat16)
    normed_mid = normalize(middle, moe_gain)
    gate_up = jnp.einsum(
        "rcd,djz->jcrz",
        lax.all_gather(normed_mid, "head", axis=1, tiled=True),
        w_shared,
        preferred_element_type=jnp.float32,
    )
    hidden_rows = (jax.nn.silu(gate_up[0]) * gate_up[1]).astype(jnp.bfloat16)
    row_block = hidden_rows
    shared_rows = lax.psum_scatter(
        jnp.einsum(
            "crz,zd->crd", row_block, w_shared_down, preferred_element_type=jnp.float32
        ).astype(jnp.bfloat16),
        "head",
        scatter_dimension=0,
        tiled=True,
    ).astype(jnp.float32)
    capacity = 2 * qrows * TOP // E
    slots = req_local * capacity
    local_rows = req_local * qrows
    flat_ids = expert_ids.reshape(req_local, qrows * TOP)
    hits = (flat_ids[:, :, None] == jnp.arange(E, dtype=jnp.int32)[None, None, :]).astype(jnp.int32)
    ranks = jnp.sum((jnp.cumsum(hits, axis=1) - 1) * hits, axis=2)
    slot_of = ranks + jnp.arange(req_local, dtype=jnp.int32)[:, None] * capacity
    place_of = jnp.sum(hits * expert_slot[None, None, :], axis=2)
    target = (place_of * slots + slot_of).reshape(local_rows, TOP)
    columns = jnp.arange(E * slots, dtype=jnp.int32)
    matches = (target[:, :, None] == columns[None, None, :]).astype(jnp.float32)
    placement = jnp.sum(matches, axis=1).astype(jnp.bfloat16)
    routing_matrix = jnp.sum(matches * expert_weights.reshape(local_rows, TOP)[:, :, None], axis=1)
    flat_mid = normed_mid.reshape(local_rows, width)
    outgoing = lax.dot_general(
        placement, flat_mid, (((0,), (0,)), ((), ())), preferred_element_type=jnp.float32
    ).astype(jnp.bfloat16)
    devices = head_count * tok_count
    per_device = max(1, E // devices)
    copies = max(1, devices // E)
    outgoing = outgoing.reshape(E, 1, slots, width)
    if copies > 1:
        outgoing = jnp.broadcast_to(outgoing, (E, copies, slots, width))
    outgoing = outgoing.reshape(devices, per_device, slots, width)
    unit_count = w_expert.shape[2] // per_device
    w_down = w_expert_down.reshape(per_device, unit_count, width)
    chunks = CHUNKS if slots % CHUNKS == 0 else 1
    step = slots // chunks
    received = [
        lax.all_to_all(
            outgoing[:, :, c * step : (c + 1) * step],
            ("head", "tok"),
            split_axis=0,
            concat_axis=0,
            tiled=True,
        )
        for c in range(chunks)
    ]
    received[0], shared_rows = lax.optimization_barrier((received[0], shared_rows))
    routing_parts = routing_matrix.reshape(local_rows, E, slots)
    routed = None
    for c in range(chunks):
        expert_parts = []
        for e in range(per_device):
            w_pair = w_expert[:, :, e * unit_count : (e + 1) * unit_count]
            gate_up = jnp.einsum(
                "gsd,dju->jgsu", received[c][:, e], w_pair, preferred_element_type=jnp.float32
            )
            hidden_part = (jax.nn.silu(gate_up[0]) * gate_up[1]).astype(jnp.bfloat16)
            expert_parts.append(
                jnp.einsum(
                    "gsu,ud->gsd", hidden_part, w_down[e], preferred_element_type=jnp.float32
                ).astype(jnp.bfloat16)
            )
        partial_out = jnp.stack(expert_parts, axis=1)
        back = lax.all_to_all(partial_out, ("head", "tok"), split_axis=0, concat_axis=0, tiled=True)
        summed = jnp.sum(back.reshape(E, copies, step, width).astype(jnp.float32), axis=1)
        part = jnp.dot(
            routing_parts[:, :, c * step : (c + 1) * step].reshape(local_rows, E * step),
            summed.reshape(E * step, width),
            precision=lax.Precision.HIGHEST,
            preferred_element_type=jnp.float32,
        )
        routed = part if routed is None else routed + part
    routed = routed.reshape(req_local, qrows, width)
    layer_out = middle.astype(jnp.float32) + jnp.transpose(shared_rows, (1, 0, 2)) + routed
    return layer_out.astype(jnp.bfloat16)


def solution(mesh):
    return jax.shard_map(
        body,
        mesh=mesh,
        in_specs=(
            P("tok", "head", None),
            P("tok"),
            P(),
            P(None, "head"),
            P("tok", None, "head"),
            P("tok", None, "head"),
            P("head", None),
            P(),
            P(None, None, "head"),
            P("head", None),
            P("tok", "head", None),
            P("tok", "head", None),
            P(),
            P(None, None, ("head", "tok")),
            P(("head", "tok"), None),
        ),
        out_specs=P("tok", "head", None),
        check_vma=False,
    )
```

```python
import math

import jax
import jax.numpy as jnp
from jax import lax
from jax.experimental import pallas as pl
from jax.experimental.pallas import tpu as pltpu
from jax.sharding import PartitionSpec as P

HD = 128
E = 64
TOP = 6


EPS = 1e-06
NEG_BIG = -1e30


def normalize(values, gain_vector):
    wide = values.astype(jnp.float32)
    factor = lax.rsqrt(jnp.mean(wide * wide, axis=-1, keepdims=True) + EPS)
    return (wide * factor * gain_vector).astype(jnp.bfloat16)


def rotary(vectors, positions):
    half_dim = vectors.shape[-1] // 2
    freqs = 10000.0 ** (-jnp.arange(half_dim, dtype=jnp.float32) / half_dim)
    angles = positions.astype(jnp.float32)[:, None] * freqs[None, :]
    cosine = jnp.cos(angles)[:, None, :]
    sine_part = jnp.sin(angles)[:, None, :]
    lower = vectors[..., :half_dim]
    upper = vectors[..., half_dim:]
    return jnp.concatenate(
        [lower * cosine - upper * sine_part, upper * cosine + lower * sine_part], axis=-1
    )


def attend(queries, keys_new, values_new, keys_old, values_old, length):
    factor = 1.0 / math.sqrt(queries.shape[-1])
    score_old = jnp.dot(queries, keys_old.T, preferred_element_type=jnp.float32) * factor
    score_new = jnp.dot(queries, keys_new.T, preferred_element_type=jnp.float32) * factor
    old_slots = jnp.arange(keys_old.shape[0], dtype=jnp.int32)
    live_old = (old_slots < length)[None, :]
    new_slots = jnp.arange(queries.shape[0], dtype=jnp.int32)
    live_new = new_slots[None, :] <= new_slots[:, None]
    row_max = jnp.maximum(
        jnp.max(jnp.where(live_old, score_old, NEG_BIG), axis=1),
        jnp.max(jnp.where(live_new, score_new, NEG_BIG), axis=1),
    )
    prob_old = jnp.where(live_old, jnp.exp(score_old - row_max[:, None]), 0.0)
    prob_new = jnp.where(live_new, jnp.exp(score_new - row_max[:, None]), 0.0)
    denom = jnp.sum(prob_old, axis=1) + jnp.sum(prob_new, axis=1)
    weighted = jnp.dot(
        prob_old.astype(jnp.bfloat16), values_old, preferred_element_type=jnp.float32
    )
    weighted = weighted + jnp.dot(
        prob_new.astype(jnp.bfloat16), values_new, preferred_element_type=jnp.float32
    )
    return (weighted / denom[:, None]).astype(jnp.bfloat16)


def rotate(block, cosine, sine_signed):
    half = block.shape[-1] // 2
    return block * cosine + pltpu.roll(block, half, 1) * sine_signed


def attention_kernel(
    len_ref, q_ref, kn_ref, vn_ref, cq_ref, sq_ref, ck_ref, sk_ref, ko_ref, vo_ref, o_ref
):
    rows = q_ref.shape[0]
    new_len = kn_ref.shape[0]
    cache_rows = ko_ref.shape[1]
    length = len_ref[0]
    start = pl.program_id(1) * rows
    factor = 1.0 / math.sqrt(q_ref.shape[-1])
    contract = (((1,), (1,)), ((), ()))
    queries = rotate(q_ref[...], cq_ref[...], sq_ref[...]).astype(jnp.bfloat16)
    keys_new = rotate(kn_ref[...], ck_ref[...], sk_ref[...]).astype(jnp.bfloat16)
    values_new = vn_ref[...].astype(jnp.bfloat16)
    score_old = (
        lax.dot_general(queries, ko_ref[0], contract, preferred_element_type=jnp.float32) * factor
    )
    score_new = (
        lax.dot_general(queries, keys_new, contract, preferred_element_type=jnp.float32) * factor
    )
    live_old = lax.broadcasted_iota(jnp.int32, (rows, cache_rows), 1) < length
    new_cols = lax.broadcasted_iota(jnp.int32, (rows, new_len), 1)
    new_rows = lax.broadcasted_iota(jnp.int32, (rows, new_len), 0) + start
    live_new = new_cols <= new_rows
    row_max = jnp.maximum(
        jnp.max(jnp.where(live_old, score_old, NEG_BIG), axis=1, keepdims=True),
        jnp.max(jnp.where(live_new, score_new, NEG_BIG), axis=1, keepdims=True),
    )
    prob_old = jnp.where(live_old, jnp.exp(score_old - row_max), 0.0)
    prob_new = jnp.where(live_new, jnp.exp(score_new - row_max), 0.0)
    denom = jnp.sum(prob_old, axis=1, keepdims=True) + jnp.sum(prob_new, axis=1, keepdims=True)
    weighted = jnp.dot(
        prob_old.astype(jnp.bfloat16), vo_ref[0], preferred_element_type=jnp.float32
    )
    weighted = weighted + jnp.dot(
        prob_new.astype(jnp.bfloat16), values_new, preferred_element_type=jnp.float32
    )
    o_ref[...] = (weighted / denom).astype(o_ref.dtype)


def attention(length, qkv, cosine, sine_signed, k_cache, v_cache):
    new_len = qkv.shape[0]
    cache_rows = k_cache.shape[1]
    heads = qkv.shape[1] // (3 * HD)
    rows = min(128, new_len)
    grid_spec = pltpu.PrefetchScalarGridSpec(
        num_scalar_prefetch=1,
        grid=(heads, new_len // rows),
        in_specs=[
            pl.BlockSpec((rows, HD), lambda h, i, n: (i, 3 * h)),
            pl.BlockSpec((new_len, HD), lambda h, i, n: (0, 3 * h + 1)),
            pl.BlockSpec((new_len, HD), lambda h, i, n: (0, 3 * h + 2)),
            pl.BlockSpec((rows, HD), lambda h, i, n: (i, 0)),
            pl.BlockSpec((rows, HD), lambda h, i, n: (i, 0)),
            pl.BlockSpec((new_len, HD), lambda h, i, n: (0, 0)),
            pl.BlockSpec((new_len, HD), lambda h, i, n: (0, 0)),
            pl.BlockSpec((1, cache_rows, HD), lambda h, i, n: (0, 0, h)),
            pl.BlockSpec((1, cache_rows, HD), lambda h, i, n: (0, 0, h)),
        ],
        out_specs=pl.BlockSpec((rows, HD), lambda h, i, n: (i, h)),
    )
    return pl.pallas_call(
        attention_kernel,
        grid_spec=grid_spec,
        out_shape=jax.ShapeDtypeStruct((new_len, heads * HD), jnp.bfloat16),
        name="cached_attention",
    )(length, qkv, qkv, qkv, cosine, sine_signed, cosine, sine_signed, k_cache, v_cache)


def body(
    tokens,
    cache_len,
    attn_gain,
    w_qkv,
    k_cache,
    v_cache,
    w_out,
    moe_gain,
    w_shared,
    w_shared_down,
    expert_ids,
    expert_weights,
    expert_slot,
    w_expert,
    w_expert_down,
):
    req_local, qrows, width = tokens.shape
    head_count = lax.axis_size("head")
    tok_count = lax.axis_size("tok")
    new_len = qrows * head_count
    head_local = w_out.shape[0] // HD
    cache_rows = k_cache.shape[1]
    normed = normalize(lax.all_gather(tokens, "head", axis=1, tiled=True), attn_gain)
    qkv = jnp.dot(normed[0], w_qkv, preferred_element_type=jnp.float32)
    length = cache_len[0]
    positions = length + jnp.arange(new_len, dtype=jnp.int32)
    half_dim = HD // 2
    freqs = 10000.0 ** (-jnp.arange(half_dim, dtype=jnp.float32) / half_dim)
    angles = positions.astype(jnp.float32)[:, None] * freqs[None, :]
    cosine = jnp.cos(angles)
    sine_part = jnp.sin(angles)
    cosine = jnp.concatenate([cosine, cosine], axis=1)
    sine_signed = jnp.concatenate([-sine_part, sine_part], axis=1)
    outputs = [attention(cache_len, qkv, cosine, sine_signed, k_cache, v_cache)]
    heads_out = jnp.stack(outputs, axis=1)
    row_block = heads_out
    attn_rows = lax.psum_scatter(
        jnp.einsum("crk,kd->crd", row_block, w_out, preferred_element_type=jnp.float32).astype(
            jnp.bfloat16
        ),
        "head",
        scatter_dimension=0,
        tiled=True,
    ).astype(jnp.float32)
    middle = (tokens.astype(jnp.float32) + jnp.transpose(attn_rows, (1, 0, 2))).astype(jnp.bfloat16)
    normed_mid = normalize(middle, moe_gain)
    gate_up = jnp.einsum(
        "rcd,djz->jcrz",
        lax.all_gather(normed_mid, "head", axis=1, tiled=True),
        w_shared,
        preferred_element_type=jnp.float32,
    )
    hidden_rows = (jax.nn.silu(gate_up[0]) * gate_up[1]).astype(jnp.bfloat16)
    row_block = hidden_rows
    shared_rows = lax.psum_scatter(
        jnp.einsum(
            "crz,zd->crd", row_block, w_shared_down, preferred_element_type=jnp.float32
        ).astype(jnp.bfloat16),
        "head",
        scatter_dimension=0,
        tiled=True,
    ).astype(jnp.float32)
    capacity = 2 * qrows * TOP // E
    slots = req_local * capacity
    local_rows = req_local * qrows
    flat_ids = expert_ids.reshape(req_local, qrows * TOP)
    hits = (flat_ids[:, :, None] == jnp.arange(E, dtype=jnp.int32)[None, None, :]).astype(jnp.int32)
    ranks = jnp.sum((jnp.cumsum(hits, axis=1) - 1) * hits, axis=2)
    slot_of = ranks + jnp.arange(req_local, dtype=jnp.int32)[:, None] * capacity
    place_of = jnp.sum(hits * expert_slot[None, None, :], axis=2)
    target = (place_of * slots + slot_of).reshape(local_rows, TOP)
    columns = jnp.arange(E * slots, dtype=jnp.int32)
    matches = (target[:, :, None] == columns[None, None, :]).astype(jnp.float32)
    placement = jnp.sum(matches, axis=1).astype(jnp.bfloat16)
    routing_matrix = jnp.sum(matches * expert_weights.reshape(local_rows, TOP)[:, :, None], axis=1)
    flat_mid = normed_mid.reshape(local_rows, width)
    outgoing = lax.dot_general(
        placement, flat_mid, (((0,), (0,)), ((), ())), preferred_element_type=jnp.float32
    ).astype(jnp.bfloat16)
    devices = head_count * tok_count
    per_device = max(1, E // devices)
    copies = max(1, devices // E)
    outgoing = outgoing.reshape(E, 1, slots, width)
    if copies > 1:
        outgoing = jnp.broadcast_to(outgoing, (E, copies, slots, width))
    outgoing = outgoing.reshape(devices, per_device, slots, width)
    unit_count = w_expert.shape[2] // per_device
    w_down = w_expert_down.reshape(per_device, unit_count, width)
    groups = E // per_device
    received = [
        lax.all_to_all(outgoing[:, c], ("head", "tok"), split_axis=0, concat_axis=0, tiled=True)
        for c in range(per_device)
    ]
    received[0], shared_rows = lax.optimization_barrier((received[0], shared_rows))
    routing_parts = routing_matrix.reshape(local_rows, groups, per_device, slots)
    routed = None
    for c in range(per_device):
        w_pair = w_expert[:, :, c * unit_count : (c + 1) * unit_count]
        gate_up = jnp.einsum(
            "gsd,dju->jgsu", received[c], w_pair, preferred_element_type=jnp.float32
        )
        hidden_part = (jax.nn.silu(gate_up[0]) * gate_up[1]).astype(jnp.bfloat16)
        expert_part = jnp.einsum(
            "gsu,ud->gsd", hidden_part, w_down[c], preferred_element_type=jnp.float32
        ).astype(jnp.bfloat16)
        back = lax.all_to_all(expert_part, ("head", "tok"), split_axis=0, concat_axis=0, tiled=True)
        summed = jnp.sum(back.reshape(groups, copies, slots, width).astype(jnp.float32), axis=1)
        part = jnp.dot(
            routing_parts[:, :, c].reshape(local_rows, groups * slots),
            summed.reshape(groups * slots, width),
            precision=lax.Precision.HIGHEST,
            preferred_element_type=jnp.float32,
        )
        routed = part if routed is None else routed + part
    routed = routed.reshape(req_local, qrows, width)
    layer_out = middle.astype(jnp.float32) + jnp.transpose(shared_rows, (1, 0, 2)) + routed
    return layer_out.astype(jnp.bfloat16)


def solution(mesh):
    return jax.shard_map(
        body,
        mesh=mesh,
        in_specs=(
            P("tok", "head", None),
            P("tok"),
            P(),
            P(None, "head"),
            P("tok", None, "head"),
            P("tok", None, "head"),
            P("head", None),
            P(),
            P(None, None, "head"),
            P("head", None),
            P("tok", "head", None),
            P("tok", "head", None),
            P(),
            P(None, None, ("head", "tok")),
            P(("head", "tok"), None),
        ),
        out_specs=P("tok", "head", None),
        check_vma=False,
    )
```

```python
import math

import jax
import jax.numpy as jnp
from jax import lax
from jax.experimental import pallas as pl
from jax.experimental.pallas import tpu as pltpu
from jax.sharding import PartitionSpec as P

HD = 128
E = 64
TOP = 6


EPS = 1e-06
NEG_BIG = -1e30


def normalize(values, gain_vector):
    wide = values.astype(jnp.float32)
    factor = lax.rsqrt(jnp.mean(wide * wide, axis=-1, keepdims=True) + EPS)
    return (wide * factor * gain_vector).astype(jnp.bfloat16)


def rotary(vectors, positions):
    half_dim = vectors.shape[-1] // 2
    freqs = 10000.0 ** (-jnp.arange(half_dim, dtype=jnp.float32) / half_dim)
    angles = positions.astype(jnp.float32)[:, None] * freqs[None, :]
    cosine = jnp.cos(angles)[:, None, :]
    sine_part = jnp.sin(angles)[:, None, :]
    lower = vectors[..., :half_dim]
    upper = vectors[..., half_dim:]
    return jnp.concatenate(
        [lower * cosine - upper * sine_part, upper * cosine + lower * sine_part], axis=-1
    )


def attend(queries, keys_new, values_new, keys_old, values_old, length):
    factor = 1.0 / math.sqrt(queries.shape[-1])
    score_old = jnp.dot(queries, keys_old.T, preferred_element_type=jnp.float32) * factor
    score_new = jnp.dot(queries, keys_new.T, preferred_element_type=jnp.float32) * factor
    old_slots = jnp.arange(keys_old.shape[0], dtype=jnp.int32)
    live_old = (old_slots < length)[None, :]
    new_slots = jnp.arange(queries.shape[0], dtype=jnp.int32)
    live_new = new_slots[None, :] <= new_slots[:, None]
    row_max = jnp.maximum(
        jnp.max(jnp.where(live_old, score_old, NEG_BIG), axis=1),
        jnp.max(jnp.where(live_new, score_new, NEG_BIG), axis=1),
    )
    prob_old = jnp.where(live_old, jnp.exp(score_old - row_max[:, None]), 0.0)
    prob_new = jnp.where(live_new, jnp.exp(score_new - row_max[:, None]), 0.0)
    denom = jnp.sum(prob_old, axis=1) + jnp.sum(prob_new, axis=1)
    weighted = jnp.dot(
        prob_old.astype(jnp.bfloat16), values_old, preferred_element_type=jnp.float32
    )
    weighted = weighted + jnp.dot(
        prob_new.astype(jnp.bfloat16), values_new, preferred_element_type=jnp.float32
    )
    return (weighted / denom[:, None]).astype(jnp.bfloat16)


def rotate(block, cosine, sine_signed):
    half = block.shape[-1] // 2
    return block * cosine + pltpu.roll(block, half, 1) * sine_signed


def attention_kernel(
    len_ref, q_ref, kn_ref, vn_ref, cq_ref, sq_ref, ck_ref, sk_ref, ko_ref, vo_ref, o_ref
):
    rows = q_ref.shape[0]
    new_len = kn_ref.shape[0]
    cache_rows = ko_ref.shape[1]
    length = len_ref[0]
    start = pl.program_id(1) * rows
    factor = 1.0 / math.sqrt(q_ref.shape[-1])
    contract = (((1,), (1,)), ((), ()))
    queries = rotate(q_ref[...], cq_ref[...], sq_ref[...]).astype(jnp.bfloat16)
    keys_new = rotate(kn_ref[...], ck_ref[...], sk_ref[...]).astype(jnp.bfloat16)
    values_new = vn_ref[...].astype(jnp.bfloat16)
    score_old = (
        lax.dot_general(queries, ko_ref[0], contract, preferred_element_type=jnp.float32) * factor
    )
    score_new = (
        lax.dot_general(queries, keys_new, contract, preferred_element_type=jnp.float32) * factor
    )
    live_old = lax.broadcasted_iota(jnp.int32, (rows, cache_rows), 1) < length
    new_cols = lax.broadcasted_iota(jnp.int32, (rows, new_len), 1)
    new_rows = lax.broadcasted_iota(jnp.int32, (rows, new_len), 0) + start
    live_new = new_cols <= new_rows
    row_max = jnp.maximum(
        jnp.max(jnp.where(live_old, score_old, NEG_BIG), axis=1, keepdims=True),
        jnp.max(jnp.where(live_new, score_new, NEG_BIG), axis=1, keepdims=True),
    )
    prob_old = jnp.where(live_old, jnp.exp(score_old - row_max), 0.0)
    prob_new = jnp.where(live_new, jnp.exp(score_new - row_max), 0.0)
    denom = jnp.sum(prob_old, axis=1, keepdims=True) + jnp.sum(prob_new, axis=1, keepdims=True)
    weighted = jnp.dot(
        prob_old.astype(jnp.bfloat16), vo_ref[0], preferred_element_type=jnp.float32
    )
    weighted = weighted + jnp.dot(
        prob_new.astype(jnp.bfloat16), values_new, preferred_element_type=jnp.float32
    )
    o_ref[...] = (weighted / denom).astype(o_ref.dtype)


def attention(length, qkv, cosine, sine_signed, k_cache, v_cache):
    new_len = qkv.shape[0]
    cache_rows = k_cache.shape[1]
    heads = qkv.shape[1] // (3 * HD)
    rows = min(128, new_len)
    grid_spec = pltpu.PrefetchScalarGridSpec(
        num_scalar_prefetch=1,
        grid=(heads, new_len // rows),
        in_specs=[
            pl.BlockSpec((rows, HD), lambda h, i, n: (i, 3 * h)),
            pl.BlockSpec((new_len, HD), lambda h, i, n: (0, 3 * h + 1)),
            pl.BlockSpec((new_len, HD), lambda h, i, n: (0, 3 * h + 2)),
            pl.BlockSpec((rows, HD), lambda h, i, n: (i, 0)),
            pl.BlockSpec((rows, HD), lambda h, i, n: (i, 0)),
            pl.BlockSpec((new_len, HD), lambda h, i, n: (0, 0)),
            pl.BlockSpec((new_len, HD), lambda h, i, n: (0, 0)),
            pl.BlockSpec((1, cache_rows, HD), lambda h, i, n: (0, 0, h)),
            pl.BlockSpec((1, cache_rows, HD), lambda h, i, n: (0, 0, h)),
        ],
        out_specs=pl.BlockSpec((rows, HD), lambda h, i, n: (i, h)),
    )
    return pl.pallas_call(
        attention_kernel,
        grid_spec=grid_spec,
        out_shape=jax.ShapeDtypeStruct((new_len, heads * HD), jnp.bfloat16),
        name="cached_attention",
    )(length, qkv, qkv, qkv, cosine, sine_signed, cosine, sine_signed, k_cache, v_cache)


def body(
    tokens,
    cache_len,
    attn_gain,
    w_qkv,
    k_cache,
    v_cache,
    w_out,
    moe_gain,
    w_shared,
    w_shared_down,
    expert_ids,
    expert_weights,
    expert_slot,
    w_expert,
    w_expert_down,
):
    req_local, qrows, width = tokens.shape
    head_count = lax.axis_size("head")
    tok_count = lax.axis_size("tok")
    new_len = qrows * head_count
    head_local = w_out.shape[0] // HD
    cache_rows = k_cache.shape[1]
    capacity = 2 * qrows * TOP // E
    slots = req_local * capacity
    local_rows = req_local * qrows
    flat_ids = expert_ids.reshape(req_local, qrows * TOP)
    hits = (flat_ids[:, :, None] == jnp.arange(E, dtype=jnp.int32)[None, None, :]).astype(jnp.int32)
    ranks = jnp.sum((jnp.cumsum(hits, axis=1) - 1) * hits, axis=2)
    slot_of = ranks + jnp.arange(req_local, dtype=jnp.int32)[:, None] * capacity
    place_of = jnp.sum(hits * expert_slot[None, None, :], axis=2)
    target = (place_of * slots + slot_of).reshape(local_rows, TOP)
    columns = jnp.arange(E * slots, dtype=jnp.int32)
    matches = (target[:, :, None] == columns[None, None, :]).astype(jnp.float32)
    placement = jnp.sum(matches, axis=1).astype(jnp.bfloat16)
    routing_matrix = jnp.sum(matches * expert_weights.reshape(local_rows, TOP)[:, :, None], axis=1)
    gathered = lax.all_gather(tokens, "head", axis=1, tiled=True)
    gathered, placement, routing_matrix = lax.optimization_barrier(
        (gathered, placement, routing_matrix)
    )
    normed = normalize(gathered, attn_gain)
    qkv = jnp.dot(normed[0], w_qkv, preferred_element_type=jnp.float32)
    length = cache_len[0]
    positions = length + jnp.arange(new_len, dtype=jnp.int32)
    half_dim = HD // 2
    freqs = 10000.0 ** (-jnp.arange(half_dim, dtype=jnp.float32) / half_dim)
    angles = positions.astype(jnp.float32)[:, None] * freqs[None, :]
    cosine = jnp.cos(angles)
    sine_part = jnp.sin(angles)
    cosine = jnp.concatenate([cosine, cosine], axis=1)
    sine_signed = jnp.concatenate([-sine_part, sine_part], axis=1)
    outputs = [attention(cache_len, qkv, cosine, sine_signed, k_cache, v_cache)]
    heads_out = jnp.stack(outputs, axis=1)
    row_block = heads_out
    attn_rows = lax.psum_scatter(
        jnp.einsum("crk,kd->crd", row_block, w_out, preferred_element_type=jnp.float32).astype(
            jnp.bfloat16
        ),
        "head",
        scatter_dimension=0,
        tiled=True,
    ).astype(jnp.float32)
    middle = (tokens.astype(jnp.float32) + jnp.transpose(attn_rows, (1, 0, 2))).astype(jnp.bfloat16)
    normed_mid = normalize(middle, moe_gain)
    gate_up = jnp.einsum(
        "rcd,djz->jcrz",
        lax.all_gather(normed_mid, "head", axis=1, tiled=True),
        w_shared,
        preferred_element_type=jnp.float32,
    )
    hidden_rows = (jax.nn.silu(gate_up[0]) * gate_up[1]).astype(jnp.bfloat16)
    row_block = hidden_rows
    shared_rows = lax.psum_scatter(
        jnp.einsum(
            "crz,zd->crd", row_block, w_shared_down, preferred_element_type=jnp.float32
        ).astype(jnp.bfloat16),
        "head",
        scatter_dimension=0,
        tiled=True,
    ).astype(jnp.float32)
    flat_mid = normed_mid.reshape(local_rows, width)
    outgoing = lax.dot_general(
        placement, flat_mid, (((0,), (0,)), ((), ())), preferred_element_type=jnp.float32
    ).astype(jnp.bfloat16)
    devices = head_count * tok_count
    per_device = max(1, E // devices)
    copies = max(1, devices // E)
    outgoing = outgoing.reshape(E, 1, slots, width)
    if copies > 1:
        outgoing = jnp.broadcast_to(outgoing, (E, copies, slots, width))
    outgoing = outgoing.reshape(devices, per_device, slots, width)
    unit_count = w_expert.shape[2] // per_device
    w_down = w_expert_down.reshape(per_device, unit_count, width)
    groups = E // per_device
    received = [
        lax.all_to_all(outgoing[:, c], ("head", "tok"), split_axis=0, concat_axis=0, tiled=True)
        for c in range(per_device)
    ]
    received[0], shared_rows = lax.optimization_barrier((received[0], shared_rows))
    routing_parts = routing_matrix.reshape(local_rows, groups, per_device, slots)
    routed = None
    for c in range(per_device):
        w_pair = w_expert[:, :, c * unit_count : (c + 1) * unit_count]
        gate_up = jnp.einsum(
            "gsd,dju->jgsu", received[c], w_pair, preferred_element_type=jnp.float32
        )
        hidden_part = (jax.nn.silu(gate_up[0]) * gate_up[1]).astype(jnp.bfloat16)
        expert_part = jnp.einsum(
            "gsu,ud->gsd", hidden_part, w_down[c], preferred_element_type=jnp.float32
        ).astype(jnp.bfloat16)
        back = lax.all_to_all(expert_part, ("head", "tok"), split_axis=0, concat_axis=0, tiled=True)
        summed = jnp.sum(back.reshape(groups, copies, slots, width).astype(jnp.float32), axis=1)
        part = jnp.dot(
            routing_parts[:, :, c].reshape(local_rows, groups * slots),
            summed.reshape(groups * slots, width),
            precision=lax.Precision.HIGHEST,
            preferred_element_type=jnp.float32,
        )
        routed = part if routed is None else routed + part
    routed = routed.reshape(req_local, qrows, width)
    layer_out = middle.astype(jnp.float32) + jnp.transpose(shared_rows, (1, 0, 2)) + routed
    return layer_out.astype(jnp.bfloat16)


def solution(mesh):
    return jax.shard_map(
        body,
        mesh=mesh,
        in_specs=(
            P("tok", "head", None),
            P("tok"),
            P(),
            P(None, "head"),
            P("tok", None, "head"),
            P("tok", None, "head"),
            P("head", None),
            P(),
            P(None, None, "head"),
            P("head", None),
            P("tok", "head", None),
            P("tok", "head", None),
            P(),
            P(None, None, ("head", "tok")),
            P(("head", "tok"), None),
        ),
        out_specs=P("tok", "head", None),
        check_vma=False,
    )
```

```python
import math

import jax
import jax.numpy as jnp
from jax import lax
from jax.experimental import pallas as pl
from jax.experimental.pallas import tpu as pltpu
from jax.sharding import PartitionSpec as P

HD = 128
E = 64
TOP = 6


EPS = 1e-06
NEG_BIG = -1e30


def normalize(values, gain_vector):
    wide = values.astype(jnp.float32)
    factor = lax.rsqrt(jnp.mean(wide * wide, axis=-1, keepdims=True) + EPS)
    return (wide * factor * gain_vector).astype(jnp.bfloat16)


def rotary(vectors, positions):
    half_dim = vectors.shape[-1] // 2
    freqs = 10000.0 ** (-jnp.arange(half_dim, dtype=jnp.float32) / half_dim)
    angles = positions.astype(jnp.float32)[:, None] * freqs[None, :]
    cosine = jnp.cos(angles)[:, None, :]
    sine_part = jnp.sin(angles)[:, None, :]
    lower = vectors[..., :half_dim]
    upper = vectors[..., half_dim:]
    return jnp.concatenate(
        [lower * cosine - upper * sine_part, upper * cosine + lower * sine_part], axis=-1
    )


def attend(queries, keys_new, values_new, keys_old, values_old, length):
    factor = 1.0 / math.sqrt(queries.shape[-1])
    score_old = jnp.dot(queries, keys_old.T, preferred_element_type=jnp.float32) * factor
    score_new = jnp.dot(queries, keys_new.T, preferred_element_type=jnp.float32) * factor
    old_slots = jnp.arange(keys_old.shape[0], dtype=jnp.int32)
    live_old = (old_slots < length)[None, :]
    new_slots = jnp.arange(queries.shape[0], dtype=jnp.int32)
    live_new = new_slots[None, :] <= new_slots[:, None]
    row_max = jnp.maximum(
        jnp.max(jnp.where(live_old, score_old, NEG_BIG), axis=1),
        jnp.max(jnp.where(live_new, score_new, NEG_BIG), axis=1),
    )
    prob_old = jnp.where(live_old, jnp.exp(score_old - row_max[:, None]), 0.0)
    prob_new = jnp.where(live_new, jnp.exp(score_new - row_max[:, None]), 0.0)
    denom = jnp.sum(prob_old, axis=1) + jnp.sum(prob_new, axis=1)
    weighted = jnp.dot(
        prob_old.astype(jnp.bfloat16), values_old, preferred_element_type=jnp.float32
    )
    weighted = weighted + jnp.dot(
        prob_new.astype(jnp.bfloat16), values_new, preferred_element_type=jnp.float32
    )
    return (weighted / denom[:, None]).astype(jnp.bfloat16)


def rotate(block, cosine, sine_signed):
    half = block.shape[-1] // 2
    return block * cosine + pltpu.roll(block, half, 1) * sine_signed


def attention_kernel(
    len_ref, q_ref, kn_ref, vn_ref, cq_ref, sq_ref, ck_ref, sk_ref, ko_ref, vo_ref, o_ref
):
    rows = q_ref.shape[0]
    new_len = kn_ref.shape[0]
    cache_rows = ko_ref.shape[1]
    length = len_ref[0]
    start = pl.program_id(1) * rows
    factor = 1.0 / math.sqrt(q_ref.shape[-1])
    contract = (((1,), (1,)), ((), ()))
    queries = rotate(q_ref[...], cq_ref[...], sq_ref[...]).astype(jnp.bfloat16)
    keys_new = rotate(kn_ref[...], ck_ref[...], sk_ref[...]).astype(jnp.bfloat16)
    values_new = vn_ref[...].astype(jnp.bfloat16)
    score_old = (
        lax.dot_general(queries, ko_ref[0], contract, preferred_element_type=jnp.float32) * factor
    )
    score_new = (
        lax.dot_general(queries, keys_new, contract, preferred_element_type=jnp.float32) * factor
    )
    live_old = lax.broadcasted_iota(jnp.int32, (rows, cache_rows), 1) < length
    new_cols = lax.broadcasted_iota(jnp.int32, (rows, new_len), 1)
    new_rows = lax.broadcasted_iota(jnp.int32, (rows, new_len), 0) + start
    live_new = new_cols <= new_rows
    row_max = jnp.maximum(
        jnp.max(jnp.where(live_old, score_old, NEG_BIG), axis=1, keepdims=True),
        jnp.max(jnp.where(live_new, score_new, NEG_BIG), axis=1, keepdims=True),
    )
    prob_old = jnp.where(live_old, jnp.exp(score_old - row_max), 0.0)
    prob_new = jnp.where(live_new, jnp.exp(score_new - row_max), 0.0)
    denom = jnp.sum(prob_old, axis=1, keepdims=True) + jnp.sum(prob_new, axis=1, keepdims=True)
    weighted = jnp.dot(
        prob_old.astype(jnp.bfloat16), vo_ref[0], preferred_element_type=jnp.float32
    )
    weighted = weighted + jnp.dot(
        prob_new.astype(jnp.bfloat16), values_new, preferred_element_type=jnp.float32
    )
    o_ref[...] = (weighted / denom).astype(o_ref.dtype)


def attention(length, qkv, cosine, sine_signed, k_cache, v_cache):
    new_len = qkv.shape[0]
    cache_rows = k_cache.shape[1]
    heads = qkv.shape[1] // (3 * HD)
    rows = min(128, new_len)
    grid_spec = pltpu.PrefetchScalarGridSpec(
        num_scalar_prefetch=1,
        grid=(heads, new_len // rows),
        in_specs=[
            pl.BlockSpec((rows, HD), lambda h, i, n: (i, 3 * h)),
            pl.BlockSpec((new_len, HD), lambda h, i, n: (0, 3 * h + 1)),
            pl.BlockSpec((new_len, HD), lambda h, i, n: (0, 3 * h + 2)),
            pl.BlockSpec((rows, HD), lambda h, i, n: (i, 0)),
            pl.BlockSpec((rows, HD), lambda h, i, n: (i, 0)),
            pl.BlockSpec((new_len, HD), lambda h, i, n: (0, 0)),
            pl.BlockSpec((new_len, HD), lambda h, i, n: (0, 0)),
            pl.BlockSpec((1, cache_rows, HD), lambda h, i, n: (0, 0, h)),
            pl.BlockSpec((1, cache_rows, HD), lambda h, i, n: (0, 0, h)),
        ],
        out_specs=pl.BlockSpec((rows, HD), lambda h, i, n: (i, h)),
    )
    return pl.pallas_call(
        attention_kernel,
        grid_spec=grid_spec,
        out_shape=jax.ShapeDtypeStruct((new_len, heads * HD), jnp.bfloat16),
        name="cached_attention",
    )(length, qkv, qkv, qkv, cosine, sine_signed, cosine, sine_signed, k_cache, v_cache)


def cross_perm(count, step):
    pairs = count // 2
    return [(j, ((j // 2 + step) % pairs) * 2 + j % 2) for j in range(count)]


def head_gather(block):
    count = lax.axis_size("head")
    pairs = count // 2
    index = lax.axis_index("head")
    pair, core = index // 2, index % 2
    pieces = [block] + [
        lax.ppermute(block, "head", cross_perm(count, step)) for step in range(1, pairs)
    ]
    stacked = jnp.stack(pieces)
    order = (pair - jnp.arange(pairs, dtype=jnp.int32)) % pairs
    mine = jnp.take(stacked, order, axis=0)
    partner = lax.ppermute(mine, "head", [(j, j ^ 1) for j in range(count)])
    first = jnp.where(core == 0, mine, partner)
    second = jnp.where(core == 0, partner, mine)
    return jnp.stack([first, second], axis=1).reshape((count * block.shape[0],) + block.shape[1:])


def head_scatter_sum(partial):
    count = lax.axis_size("head")
    pairs = count // 2
    index = lax.axis_index("head")
    pair, core = index // 2, index % 2
    blocks = partial.reshape((pairs, 2, partial.shape[0] // count) + partial.shape[1:])
    mine = jnp.where(core == 0, blocks[:, 0], blocks[:, 1])
    other = jnp.where(core == 0, blocks[:, 1], blocks[:, 0])
    received = lax.ppermute(other, "head", [(j, j ^ 1) for j in range(count)])
    chip_sum = mine.astype(jnp.float32) + received.astype(jnp.float32)
    result = jnp.take(chip_sum, pair, axis=0)
    for step in range(1, pairs):
        outgoing = jnp.take(chip_sum, (pair + step) % pairs, axis=0).astype(jnp.bfloat16)
        arrived = lax.ppermute(outgoing, "head", cross_perm(count, step))
        result = result + arrived.astype(jnp.float32)
    return result


def body(
    tokens,
    cache_len,
    attn_gain,
    w_qkv,
    k_cache,
    v_cache,
    w_out,
    moe_gain,
    w_shared,
    w_shared_down,
    expert_ids,
    expert_weights,
    expert_slot,
    w_expert,
    w_expert_down,
):
    req_local, qrows, width = tokens.shape
    head_count = lax.axis_size("head")
    tok_count = lax.axis_size("tok")
    new_len = qrows * head_count
    head_local = w_out.shape[0] // HD
    cache_rows = k_cache.shape[1]
    capacity = 2 * qrows * TOP // E
    slots = req_local * capacity
    local_rows = req_local * qrows
    flat_ids = expert_ids.reshape(req_local, qrows * TOP)
    hits = (flat_ids[:, :, None] == jnp.arange(E, dtype=jnp.int32)[None, None, :]).astype(jnp.int32)
    ranks = jnp.sum((jnp.cumsum(hits, axis=1) - 1) * hits, axis=2)
    slot_of = ranks + jnp.arange(req_local, dtype=jnp.int32)[:, None] * capacity
    place_of = jnp.sum(hits * expert_slot[None, None, :], axis=2)
    target = (place_of * slots + slot_of).reshape(local_rows, TOP)
    columns = jnp.arange(E * slots, dtype=jnp.int32)
    matches = (target[:, :, None] == columns[None, None, :]).astype(jnp.float32)
    placement = jnp.sum(matches, axis=1).astype(jnp.bfloat16)
    routing_matrix = jnp.sum(matches * expert_weights.reshape(local_rows, TOP)[:, :, None], axis=1)
    gathered = head_gather(tokens[0])[None]
    gathered, placement, routing_matrix = lax.optimization_barrier(
        (gathered, placement, routing_matrix)
    )
    normed = normalize(gathered, attn_gain)
    qkv = jnp.dot(normed[0], w_qkv, preferred_element_type=jnp.float32)
    length = cache_len[0]
    positions = length + jnp.arange(new_len, dtype=jnp.int32)
    half_dim = HD // 2
    freqs = 10000.0 ** (-jnp.arange(half_dim, dtype=jnp.float32) / half_dim)
    angles = positions.astype(jnp.float32)[:, None] * freqs[None, :]
    cosine = jnp.cos(angles)
    sine_part = jnp.sin(angles)
    cosine = jnp.concatenate([cosine, cosine], axis=1)
    sine_signed = jnp.concatenate([-sine_part, sine_part], axis=1)
    outputs = [attention(cache_len, qkv, cosine, sine_signed, k_cache, v_cache)]
    attn_rows = head_scatter_sum(
        jnp.dot(outputs[0], w_out, preferred_element_type=jnp.float32).astype(jnp.bfloat16)
    )[None]
    middle = (tokens.astype(jnp.float32) + attn_rows).astype(jnp.bfloat16)
    normed_mid = normalize(middle, moe_gain)
    gate_up = jnp.einsum(
        "cd,djz->jcz",
        head_gather(normed_mid[0]),
        w_shared,
        preferred_element_type=jnp.float32,
    )
    hidden_rows = (jax.nn.silu(gate_up[0]) * gate_up[1]).astype(jnp.bfloat16)
    shared_rows = head_scatter_sum(
        jnp.dot(hidden_rows, w_shared_down, preferred_element_type=jnp.float32).astype(
            jnp.bfloat16
        )
    )[None]
    flat_mid = normed_mid.reshape(local_rows, width)
    outgoing = lax.dot_general(
        placement, flat_mid, (((0,), (0,)), ((), ())), preferred_element_type=jnp.float32
    ).astype(jnp.bfloat16)
    devices = head_count * tok_count
    per_device = max(1, E // devices)
    copies = max(1, devices // E)
    outgoing = outgoing.reshape(E, 1, slots, width)
    if copies > 1:
        outgoing = jnp.broadcast_to(outgoing, (E, copies, slots, width))
    outgoing = outgoing.reshape(devices, per_device, slots, width)
    unit_count = w_expert.shape[2] // per_device
    w_down = w_expert_down.reshape(per_device, unit_count, width)
    groups = E // per_device
    received = [
        lax.all_to_all(outgoing[:, c], ("head", "tok"), split_axis=0, concat_axis=0, tiled=True)
        for c in range(per_device)
    ]
    received[0], shared_rows = lax.optimization_barrier((received[0], shared_rows))
    routing_parts = routing_matrix.reshape(local_rows, groups, per_device, slots)
    routed = None
    for c in range(per_device):
        w_pair = w_expert[:, :, c * unit_count : (c + 1) * unit_count]
        gate_up = jnp.einsum(
            "gsd,dju->jgsu", received[c], w_pair, preferred_element_type=jnp.float32
        )
        hidden_part = (jax.nn.silu(gate_up[0]) * gate_up[1]).astype(jnp.bfloat16)
        expert_part = jnp.einsum(
            "gsu,ud->gsd", hidden_part, w_down[c], preferred_element_type=jnp.float32
        ).astype(jnp.bfloat16)
        back = lax.all_to_all(expert_part, ("head", "tok"), split_axis=0, concat_axis=0, tiled=True)
        summed = jnp.sum(back.reshape(groups, copies, slots, width).astype(jnp.float32), axis=1)
        part = jnp.dot(
            routing_parts[:, :, c].reshape(local_rows, groups * slots),
            summed.reshape(groups * slots, width),
            precision=lax.Precision.HIGHEST,
            preferred_element_type=jnp.float32,
        )
        routed = part if routed is None else routed + part
    routed = routed.reshape(req_local, qrows, width)
    layer_out = middle.astype(jnp.float32) + shared_rows + routed
    return layer_out.astype(jnp.bfloat16)


def solution(mesh):
    return jax.shard_map(
        body,
        mesh=mesh,
        in_specs=(
            P("tok", "head", None),
            P("tok"),
            P(),
            P(None, "head"),
            P("tok", None, "head"),
            P("tok", None, "head"),
            P("head", None),
            P(),
            P(None, None, "head"),
            P("head", None),
            P("tok", "head", None),
            P("tok", "head", None),
            P(),
            P(None, None, ("head", "tok")),
            P(("head", "tok"), None),
        ),
        out_specs=P("tok", "head", None),
        check_vma=False,
    )
```

```python
import math

import jax
import jax.numpy as jnp
from jax import lax
from jax.experimental import pallas as pl
from jax.experimental.pallas import tpu as pltpu
from jax.sharding import PartitionSpec as P

HD = 128
E = 64
TOP = 6


EPS = 1e-06
NEG_BIG = -1e30


def normalize(values, gain_vector):
    wide = values.astype(jnp.float32)
    factor = lax.rsqrt(jnp.mean(wide * wide, axis=-1, keepdims=True) + EPS)
    return (wide * factor * gain_vector).astype(jnp.bfloat16)


def rotary(vectors, positions):
    half_dim = vectors.shape[-1] // 2
    freqs = 10000.0 ** (-jnp.arange(half_dim, dtype=jnp.float32) / half_dim)
    angles = positions.astype(jnp.float32)[:, None] * freqs[None, :]
    cosine = jnp.cos(angles)[:, None, :]
    sine_part = jnp.sin(angles)[:, None, :]
    lower = vectors[..., :half_dim]
    upper = vectors[..., half_dim:]
    return jnp.concatenate(
        [lower * cosine - upper * sine_part, upper * cosine + lower * sine_part], axis=-1
    )


def attend(queries, keys_new, values_new, keys_old, values_old, length):
    factor = 1.0 / math.sqrt(queries.shape[-1])
    score_old = jnp.dot(queries, keys_old.T, preferred_element_type=jnp.float32) * factor
    score_new = jnp.dot(queries, keys_new.T, preferred_element_type=jnp.float32) * factor
    old_slots = jnp.arange(keys_old.shape[0], dtype=jnp.int32)
    live_old = (old_slots < length)[None, :]
    new_slots = jnp.arange(queries.shape[0], dtype=jnp.int32)
    live_new = new_slots[None, :] <= new_slots[:, None]
    row_max = jnp.maximum(
        jnp.max(jnp.where(live_old, score_old, NEG_BIG), axis=1),
        jnp.max(jnp.where(live_new, score_new, NEG_BIG), axis=1),
    )
    prob_old = jnp.where(live_old, jnp.exp(score_old - row_max[:, None]), 0.0)
    prob_new = jnp.where(live_new, jnp.exp(score_new - row_max[:, None]), 0.0)
    denom = jnp.sum(prob_old, axis=1) + jnp.sum(prob_new, axis=1)
    weighted = jnp.dot(
        prob_old.astype(jnp.bfloat16), values_old, preferred_element_type=jnp.float32
    )
    weighted = weighted + jnp.dot(
        prob_new.astype(jnp.bfloat16), values_new, preferred_element_type=jnp.float32
    )
    return (weighted / denom[:, None]).astype(jnp.bfloat16)


def rotate(block, cosine, sine_signed):
    half = block.shape[-1] // 2
    return block * cosine + pltpu.roll(block, half, 1) * sine_signed


def attention_kernel(
    len_ref, q_ref, kn_ref, vn_ref, cq_ref, sq_ref, ck_ref, sk_ref, ko_ref, vo_ref, o_ref
):
    rows = q_ref.shape[0]
    new_len = kn_ref.shape[0]
    cache_rows = ko_ref.shape[1]
    length = len_ref[0]
    start = pl.program_id(1) * rows
    factor = 1.0 / math.sqrt(q_ref.shape[-1])
    contract = (((1,), (1,)), ((), ()))
    queries = rotate(q_ref[...], cq_ref[...], sq_ref[...]).astype(jnp.bfloat16)
    keys_new = rotate(kn_ref[...], ck_ref[...], sk_ref[...]).astype(jnp.bfloat16)
    values_new = vn_ref[...].astype(jnp.bfloat16)
    score_old = (
        lax.dot_general(queries, ko_ref[0], contract, preferred_element_type=jnp.float32) * factor
    )
    score_new = (
        lax.dot_general(queries, keys_new, contract, preferred_element_type=jnp.float32) * factor
    )
    live_old = lax.broadcasted_iota(jnp.int32, (rows, cache_rows), 1) < length
    new_cols = lax.broadcasted_iota(jnp.int32, (rows, new_len), 1)
    new_rows = lax.broadcasted_iota(jnp.int32, (rows, new_len), 0) + start
    live_new = new_cols <= new_rows
    row_max = jnp.maximum(
        jnp.max(jnp.where(live_old, score_old, NEG_BIG), axis=1, keepdims=True),
        jnp.max(jnp.where(live_new, score_new, NEG_BIG), axis=1, keepdims=True),
    )
    prob_old = jnp.where(live_old, jnp.exp(score_old - row_max), 0.0)
    prob_new = jnp.where(live_new, jnp.exp(score_new - row_max), 0.0)
    denom = jnp.sum(prob_old, axis=1, keepdims=True) + jnp.sum(prob_new, axis=1, keepdims=True)
    weighted = jnp.dot(
        prob_old.astype(jnp.bfloat16), vo_ref[0], preferred_element_type=jnp.float32
    )
    weighted = weighted + jnp.dot(
        prob_new.astype(jnp.bfloat16), values_new, preferred_element_type=jnp.float32
    )
    o_ref[...] = (weighted / denom).astype(o_ref.dtype)


def attention(length, qkv, cosine, sine_signed, k_cache, v_cache):
    new_len = qkv.shape[0]
    cache_rows = k_cache.shape[1]
    heads = qkv.shape[1] // (3 * HD)
    rows = min(128, new_len)
    grid_spec = pltpu.PrefetchScalarGridSpec(
        num_scalar_prefetch=1,
        grid=(heads, new_len // rows),
        in_specs=[
            pl.BlockSpec((rows, HD), lambda h, i, n: (i, 3 * h)),
            pl.BlockSpec((new_len, HD), lambda h, i, n: (0, 3 * h + 1)),
            pl.BlockSpec((new_len, HD), lambda h, i, n: (0, 3 * h + 2)),
            pl.BlockSpec((rows, HD), lambda h, i, n: (i, 0)),
            pl.BlockSpec((rows, HD), lambda h, i, n: (i, 0)),
            pl.BlockSpec((new_len, HD), lambda h, i, n: (0, 0)),
            pl.BlockSpec((new_len, HD), lambda h, i, n: (0, 0)),
            pl.BlockSpec((1, cache_rows, HD), lambda h, i, n: (0, 0, h)),
            pl.BlockSpec((1, cache_rows, HD), lambda h, i, n: (0, 0, h)),
        ],
        out_specs=pl.BlockSpec((rows, HD), lambda h, i, n: (i, h)),
    )
    return pl.pallas_call(
        attention_kernel,
        grid_spec=grid_spec,
        out_shape=jax.ShapeDtypeStruct((new_len, heads * HD), jnp.bfloat16),
        name="cached_attention",
    )(length, qkv, qkv, qkv, cosine, sine_signed, cosine, sine_signed, k_cache, v_cache)


def cross_perm(count, step):
    pairs = count // 2
    return [(j, ((j // 2 + step) % pairs) * 2 + j % 2) for j in range(count)]


def head_gather(block):
    count = lax.axis_size("head")
    pairs = count // 2
    index = lax.axis_index("head")
    pair, core = index // 2, index % 2
    pieces = [block] + [
        lax.ppermute(block, "head", cross_perm(count, step)) for step in range(1, pairs)
    ]
    stacked = jnp.stack(pieces)
    order = (pair - jnp.arange(pairs, dtype=jnp.int32)) % pairs
    mine = jnp.take(stacked, order, axis=0)
    partner = lax.ppermute(mine, "head", [(j, j ^ 1) for j in range(count)])
    first = jnp.where(core == 0, mine, partner)
    second = jnp.where(core == 0, partner, mine)
    return jnp.stack([first, second], axis=1).reshape((count * block.shape[0],) + block.shape[1:])


def head_scatter_sum(partial):
    count = lax.axis_size("head")
    pairs = count // 2
    index = lax.axis_index("head")
    pair, core = index // 2, index % 2
    blocks = partial.reshape((pairs, 2, partial.shape[0] // count) + partial.shape[1:])
    mine = jnp.where(core == 0, blocks[:, 0], blocks[:, 1])
    other = jnp.where(core == 0, blocks[:, 1], blocks[:, 0])
    received = lax.ppermute(other, "head", [(j, j ^ 1) for j in range(count)])
    chip_sum = mine.astype(jnp.float32) + received.astype(jnp.float32)
    result = jnp.take(chip_sum, pair, axis=0)
    for step in range(1, pairs):
        outgoing = jnp.take(chip_sum, (pair + step) % pairs, axis=0).astype(jnp.bfloat16)
        arrived = lax.ppermute(outgoing, "head", cross_perm(count, step))
        result = result + arrived.astype(jnp.float32)
    return result


def body(
    tokens,
    cache_len,
    attn_gain,
    w_qkv,
    k_cache,
    v_cache,
    w_out,
    moe_gain,
    w_shared,
    w_shared_down,
    expert_ids,
    expert_weights,
    expert_slot,
    w_expert,
    w_expert_down,
):
    req_local, qrows, width = tokens.shape
    head_count = lax.axis_size("head")
    tok_count = lax.axis_size("tok")
    new_len = qrows * head_count
    head_local = w_out.shape[0] // HD
    cache_rows = k_cache.shape[1]
    capacity = 2 * qrows * TOP // E
    slots = req_local * capacity
    local_rows = req_local * qrows
    flat_ids = expert_ids.reshape(req_local, qrows * TOP)
    hits = (flat_ids[:, :, None] == jnp.arange(E, dtype=jnp.int32)[None, None, :]).astype(jnp.int32)
    ranks = jnp.sum((jnp.cumsum(hits, axis=1) - 1) * hits, axis=2)
    slot_of = ranks + jnp.arange(req_local, dtype=jnp.int32)[:, None] * capacity
    place_of = jnp.sum(hits * expert_slot[None, None, :], axis=2)
    target = (place_of * slots + slot_of).reshape(local_rows, TOP)
    columns = jnp.arange(E * slots, dtype=jnp.int32)
    matches = (target[:, :, None] == columns[None, None, :]).astype(jnp.float32)
    placement = jnp.sum(matches, axis=1).astype(jnp.bfloat16)
    routing_matrix = jnp.sum(matches * expert_weights.reshape(local_rows, TOP)[:, :, None], axis=1)
    gathered = head_gather(tokens[0])[None]
    gathered, placement, routing_matrix = lax.optimization_barrier(
        (gathered, placement, routing_matrix)
    )
    normed = normalize(gathered, attn_gain)
    qkv = jnp.dot(normed[0], w_qkv, preferred_element_type=jnp.float32)
    length = cache_len[0]
    positions = length + jnp.arange(new_len, dtype=jnp.int32)
    half_dim = HD // 2
    freqs = 10000.0 ** (-jnp.arange(half_dim, dtype=jnp.float32) / half_dim)
    angles = positions.astype(jnp.float32)[:, None] * freqs[None, :]
    cosine = jnp.cos(angles)
    sine_part = jnp.sin(angles)
    cosine = jnp.concatenate([cosine, cosine], axis=1)
    sine_signed = jnp.concatenate([-sine_part, sine_part], axis=1)
    outputs = [attention(cache_len, qkv, cosine, sine_signed, k_cache, v_cache)]
    attn_rows = head_scatter_sum(
        jnp.dot(outputs[0], w_out, preferred_element_type=jnp.float32).astype(jnp.bfloat16)
    )[None]
    middle = (tokens.astype(jnp.float32) + attn_rows).astype(jnp.bfloat16)
    normed_mid = normalize(middle, moe_gain)
    flat_mid = normed_mid.reshape(local_rows, width)
    outgoing = lax.dot_general(
        placement, flat_mid, (((0,), (0,)), ((), ())), preferred_element_type=jnp.float32
    ).astype(jnp.bfloat16)
    devices = head_count * tok_count
    per_device = max(1, E // devices)
    copies = max(1, devices // E)
    outgoing = outgoing.reshape(E, 1, slots, width)
    if copies > 1:
        outgoing = jnp.broadcast_to(outgoing, (E, copies, slots, width))
    outgoing = outgoing.reshape(devices, per_device, slots, width)
    unit_count = w_expert.shape[2] // per_device
    w_down = w_expert_down.reshape(per_device, unit_count, width)
    groups = E // per_device
    received = [
        lax.all_to_all(outgoing[:, c], ("head", "tok"), split_axis=0, concat_axis=0, tiled=True)
        for c in range(per_device)
    ]
    routing_parts = routing_matrix.reshape(local_rows, groups, per_device, slots)
    routed = None
    for c in range(per_device):
        w_pair = w_expert[:, :, c * unit_count : (c + 1) * unit_count]
        gate_up = jnp.einsum(
            "gsd,dju->jgsu", received[c], w_pair, preferred_element_type=jnp.float32
        )
        hidden_part = (jax.nn.silu(gate_up[0]) * gate_up[1]).astype(jnp.bfloat16)
        expert_part = jnp.einsum(
            "gsu,ud->gsd", hidden_part, w_down[c], preferred_element_type=jnp.float32
        ).astype(jnp.bfloat16)
        if c == per_device - 1:
            expert_part, shared_in = lax.optimization_barrier((expert_part, normed_mid))
        back = lax.all_to_all(expert_part, ("head", "tok"), split_axis=0, concat_axis=0, tiled=True)
        summed = jnp.sum(back.reshape(groups, copies, slots, width).astype(jnp.float32), axis=1)
        part = jnp.dot(
            routing_parts[:, :, c].reshape(local_rows, groups * slots),
            summed.reshape(groups * slots, width),
            precision=lax.Precision.HIGHEST,
            preferred_element_type=jnp.float32,
        )
        routed = part if routed is None else routed + part
    routed = routed.reshape(req_local, qrows, width)
    gate_up = jnp.einsum(
        "cd,djz->jcz",
        head_gather(shared_in[0]),
        w_shared,
        preferred_element_type=jnp.float32,
    )
    hidden_rows = (jax.nn.silu(gate_up[0]) * gate_up[1]).astype(jnp.bfloat16)
    shared_rows = head_scatter_sum(
        jnp.dot(hidden_rows, w_shared_down, preferred_element_type=jnp.float32).astype(
            jnp.bfloat16
        )
    )[None]
    layer_out = middle.astype(jnp.float32) + shared_rows + routed
    return layer_out.astype(jnp.bfloat16)


def solution(mesh):
    return jax.shard_map(
        body,
        mesh=mesh,
        in_specs=(
            P("tok", "head", None),
            P("tok"),
            P(),
            P(None, "head"),
            P("tok", None, "head"),
            P("tok", None, "head"),
            P("head", None),
            P(),
            P(None, None, "head"),
            P("head", None),
            P("tok", "head", None),
            P("tok", "head", None),
            P(),
            P(None, None, ("head", "tok")),
            P(("head", "tok"), None),
        ),
        out_specs=P("tok", "head", None),
        check_vma=False,
    )
```

```python
import math

import jax
import jax.numpy as jnp
from jax import lax
from jax.experimental import pallas as pl
from jax.experimental.pallas import tpu as pltpu
from jax.sharding import PartitionSpec as P

HD = 128
E = 64
TOP = 6


EPS = 1e-06
NEG_BIG = -1e30


def normalize(values, gain_vector):
    wide = values.astype(jnp.float32)
    factor = lax.rsqrt(jnp.mean(wide * wide, axis=-1, keepdims=True) + EPS)
    return (wide * factor * gain_vector).astype(jnp.bfloat16)


def rotary(vectors, positions):
    half_dim = vectors.shape[-1] // 2
    freqs = 10000.0 ** (-jnp.arange(half_dim, dtype=jnp.float32) / half_dim)
    angles = positions.astype(jnp.float32)[:, None] * freqs[None, :]
    cosine = jnp.cos(angles)[:, None, :]
    sine_part = jnp.sin(angles)[:, None, :]
    lower = vectors[..., :half_dim]
    upper = vectors[..., half_dim:]
    return jnp.concatenate(
        [lower * cosine - upper * sine_part, upper * cosine + lower * sine_part], axis=-1
    )


def attend(queries, keys_new, values_new, keys_old, values_old, length):
    factor = 1.0 / math.sqrt(queries.shape[-1])
    score_old = jnp.dot(queries, keys_old.T, preferred_element_type=jnp.float32) * factor
    score_new = jnp.dot(queries, keys_new.T, preferred_element_type=jnp.float32) * factor
    old_slots = jnp.arange(keys_old.shape[0], dtype=jnp.int32)
    live_old = (old_slots < length)[None, :]
    new_slots = jnp.arange(queries.shape[0], dtype=jnp.int32)
    live_new = new_slots[None, :] <= new_slots[:, None]
    row_max = jnp.maximum(
        jnp.max(jnp.where(live_old, score_old, NEG_BIG), axis=1),
        jnp.max(jnp.where(live_new, score_new, NEG_BIG), axis=1),
    )
    prob_old = jnp.where(live_old, jnp.exp(score_old - row_max[:, None]), 0.0)
    prob_new = jnp.where(live_new, jnp.exp(score_new - row_max[:, None]), 0.0)
    denom = jnp.sum(prob_old, axis=1) + jnp.sum(prob_new, axis=1)
    weighted = jnp.dot(
        prob_old.astype(jnp.bfloat16), values_old, preferred_element_type=jnp.float32
    )
    weighted = weighted + jnp.dot(
        prob_new.astype(jnp.bfloat16), values_new, preferred_element_type=jnp.float32
    )
    return (weighted / denom[:, None]).astype(jnp.bfloat16)


def rotate(block, cosine, sine_signed):
    half = block.shape[-1] // 2
    return block * cosine + pltpu.roll(block, half, 1) * sine_signed


def attention_kernel(
    len_ref, q_ref, kn_ref, vn_ref, cq_ref, sq_ref, ck_ref, sk_ref, ko_ref, vo_ref, o_ref
):
    rows = q_ref.shape[0]
    new_len = kn_ref.shape[0]
    cache_rows = ko_ref.shape[1]
    length = len_ref[0]
    start = pl.program_id(1) * rows

    def compute(mask_cache):
        factor = 1.0 / math.sqrt(q_ref.shape[-1])
        contract = (((1,), (1,)), ((), ()))
        queries = rotate(q_ref[...], cq_ref[...], sq_ref[...]).astype(jnp.bfloat16)
        keys_new = rotate(kn_ref[...], ck_ref[...], sk_ref[...]).astype(jnp.bfloat16)
        values_new = vn_ref[...].astype(jnp.bfloat16)
        score_old = (
            lax.dot_general(queries, ko_ref[0], contract, preferred_element_type=jnp.float32)
            * factor
        )
        score_new = (
            lax.dot_general(queries, keys_new, contract, preferred_element_type=jnp.float32)
            * factor
        )
        if mask_cache:
            live_old = lax.broadcasted_iota(jnp.int32, (rows, cache_rows), 1) < length
            score_old = jnp.where(live_old, score_old, NEG_BIG)
        new_cols = lax.broadcasted_iota(jnp.int32, (rows, new_len), 1)
        new_rows = lax.broadcasted_iota(jnp.int32, (rows, new_len), 0) + start
        score_new = jnp.where(new_cols <= new_rows, score_new, NEG_BIG)
        row_max = jnp.maximum(
            jnp.max(score_old, axis=1, keepdims=True), jnp.max(score_new, axis=1, keepdims=True)
        )
        prob_old = jnp.exp(score_old - row_max)
        prob_new = jnp.exp(score_new - row_max)
        denom = jnp.sum(prob_old, axis=1, keepdims=True) + jnp.sum(
            prob_new, axis=1, keepdims=True
        )
        weighted = jnp.dot(
            prob_old.astype(jnp.bfloat16), vo_ref[0], preferred_element_type=jnp.float32
        )
        weighted = weighted + jnp.dot(
            prob_new.astype(jnp.bfloat16), values_new, preferred_element_type=jnp.float32
        )
        o_ref[...] = (weighted / denom).astype(o_ref.dtype)

    @pl.when(length >= cache_rows)
    def _():
        compute(False)

    @pl.when(length < cache_rows)
    def _():
        compute(True)


def attention(length, qkv, cosine, sine_signed, k_cache, v_cache):
    new_len = qkv.shape[0]
    cache_rows = k_cache.shape[1]
    heads = qkv.shape[1] // (3 * HD)
    rows = min(256, new_len)
    grid_spec = pltpu.PrefetchScalarGridSpec(
        num_scalar_prefetch=1,
        grid=(heads, new_len // rows),
        in_specs=[
            pl.BlockSpec((rows, HD), lambda h, i, n: (i, 3 * h)),
            pl.BlockSpec((new_len, HD), lambda h, i, n: (0, 3 * h + 1)),
            pl.BlockSpec((new_len, HD), lambda h, i, n: (0, 3 * h + 2)),
            pl.BlockSpec((rows, HD), lambda h, i, n: (i, 0)),
            pl.BlockSpec((rows, HD), lambda h, i, n: (i, 0)),
            pl.BlockSpec((new_len, HD), lambda h, i, n: (0, 0)),
            pl.BlockSpec((new_len, HD), lambda h, i, n: (0, 0)),
            pl.BlockSpec((1, cache_rows, HD), lambda h, i, n: (0, 0, h)),
            pl.BlockSpec((1, cache_rows, HD), lambda h, i, n: (0, 0, h)),
        ],
        out_specs=pl.BlockSpec((rows, HD), lambda h, i, n: (i, h)),
    )
    return pl.pallas_call(
        attention_kernel,
        grid_spec=grid_spec,
        out_shape=jax.ShapeDtypeStruct((new_len, heads * HD), jnp.bfloat16),
        name="cached_attention",
    )(length, qkv, qkv, qkv, cosine, sine_signed, cosine, sine_signed, k_cache, v_cache)


def cross_perm(count, step):
    pairs = count // 2
    return [(j, ((j // 2 + step) % pairs) * 2 + j % 2) for j in range(count)]


def head_gather(block):
    count = lax.axis_size("head")
    pairs = count // 2
    index = lax.axis_index("head")
    pair, core = index // 2, index % 2
    pieces = [block] + [
        lax.ppermute(block, "head", cross_perm(count, step)) for step in range(1, pairs)
    ]
    stacked = jnp.stack(pieces)
    order = (pair - jnp.arange(pairs, dtype=jnp.int32)) % pairs
    mine = jnp.take(stacked, order, axis=0)
    partner = lax.ppermute(mine, "head", [(j, j ^ 1) for j in range(count)])
    first = jnp.where(core == 0, mine, partner)
    second = jnp.where(core == 0, partner, mine)
    return jnp.stack([first, second], axis=1).reshape((count * block.shape[0],) + block.shape[1:])


def head_scatter_sum(partial):
    count = lax.axis_size("head")
    pairs = count // 2
    index = lax.axis_index("head")
    pair, core = index // 2, index % 2
    blocks = partial.reshape((pairs, 2, partial.shape[0] // count) + partial.shape[1:])
    mine = jnp.where(core == 0, blocks[:, 0], blocks[:, 1])
    other = jnp.where(core == 0, blocks[:, 1], blocks[:, 0])
    received = lax.ppermute(other, "head", [(j, j ^ 1) for j in range(count)])
    chip_sum = mine.astype(jnp.float32) + received.astype(jnp.float32)
    result = jnp.take(chip_sum, pair, axis=0)
    for step in range(1, pairs):
        outgoing = jnp.take(chip_sum, (pair + step) % pairs, axis=0).astype(jnp.bfloat16)
        arrived = lax.ppermute(outgoing, "head", cross_perm(count, step))
        result = result + arrived.astype(jnp.float32)
    return result


def body(
    tokens,
    cache_len,
    attn_gain,
    w_qkv,
    k_cache,
    v_cache,
    w_out,
    moe_gain,
    w_shared,
    w_shared_down,
    expert_ids,
    expert_weights,
    expert_slot,
    w_expert,
    w_expert_down,
):
    req_local, qrows, width = tokens.shape
    head_count = lax.axis_size("head")
    tok_count = lax.axis_size("tok")
    new_len = qrows * head_count
    head_local = w_out.shape[0] // HD
    cache_rows = k_cache.shape[1]
    capacity = 2 * qrows * TOP // E
    slots = req_local * capacity
    local_rows = req_local * qrows
    flat_ids = expert_ids.reshape(req_local, qrows * TOP)
    hits = (flat_ids[:, :, None] == jnp.arange(E, dtype=jnp.int32)[None, None, :]).astype(jnp.int32)
    ranks = jnp.sum((jnp.cumsum(hits, axis=1) - 1) * hits, axis=2)
    slot_of = ranks + jnp.arange(req_local, dtype=jnp.int32)[:, None] * capacity
    place_of = jnp.sum(hits * expert_slot[None, None, :], axis=2)
    target = (place_of * slots + slot_of).reshape(local_rows, TOP)
    columns = jnp.arange(E * slots, dtype=jnp.int32)
    matches = (target[:, :, None] == columns[None, None, :]).astype(jnp.float32)
    placement = jnp.sum(matches, axis=1).astype(jnp.bfloat16)
    routing_matrix = jnp.sum(matches * expert_weights.reshape(local_rows, TOP)[:, :, None], axis=1)
    gathered = head_gather(tokens[0])[None]
    gathered, placement, routing_matrix = lax.optimization_barrier(
        (gathered, placement, routing_matrix)
    )
    normed = normalize(gathered, attn_gain)
    qkv = jnp.dot(normed[0], w_qkv, preferred_element_type=jnp.float32)
    length = cache_len[0]
    positions = length + jnp.arange(new_len, dtype=jnp.int32)
    half_dim = HD // 2
    freqs = 10000.0 ** (-jnp.arange(half_dim, dtype=jnp.float32) / half_dim)
    angles = positions.astype(jnp.float32)[:, None] * freqs[None, :]
    cosine = jnp.cos(angles)
    sine_part = jnp.sin(angles)
    cosine = jnp.concatenate([cosine, cosine], axis=1)
    sine_signed = jnp.concatenate([-sine_part, sine_part], axis=1)
    outputs = [attention(cache_len, qkv, cosine, sine_signed, k_cache, v_cache)]
    attn_rows = head_scatter_sum(
        jnp.dot(outputs[0], w_out, preferred_element_type=jnp.float32).astype(jnp.bfloat16)
    )[None]
    middle = (tokens.astype(jnp.float32) + attn_rows).astype(jnp.bfloat16)
    normed_mid = normalize(middle, moe_gain)
    flat_mid = normed_mid.reshape(local_rows, width)
    outgoing = lax.dot_general(
        placement, flat_mid, (((0,), (0,)), ((), ())), preferred_element_type=jnp.float32
    ).astype(jnp.bfloat16)
    devices = head_count * tok_count
    per_device = max(1, E // devices)
    copies = max(1, devices // E)
    outgoing = outgoing.reshape(E, 1, slots, width)
    if copies > 1:
        outgoing = jnp.broadcast_to(outgoing, (E, copies, slots, width))
    outgoing = outgoing.reshape(devices, per_device, slots, width)
    unit_count = w_expert.shape[2] // per_device
    w_down = w_expert_down.reshape(per_device, unit_count, width)
    groups = E // per_device
    received = [
        lax.all_to_all(outgoing[:, c], ("head", "tok"), split_axis=0, concat_axis=0, tiled=True)
        for c in range(per_device)
    ]
    routing_parts = routing_matrix.reshape(local_rows, groups, per_device, slots)
    routed = None
    for c in range(per_device):
        w_pair = w_expert[:, :, c * unit_count : (c + 1) * unit_count]
        gate_up = jnp.einsum(
            "gsd,dju->jgsu", received[c], w_pair, preferred_element_type=jnp.float32
        )
        hidden_part = (jax.nn.silu(gate_up[0]) * gate_up[1]).astype(jnp.bfloat16)
        expert_part = jnp.einsum(
            "gsu,ud->gsd", hidden_part, w_down[c], preferred_element_type=jnp.float32
        ).astype(jnp.bfloat16)
        if c == per_device - 1:
            expert_part, shared_in = lax.optimization_barrier((expert_part, normed_mid))
        back = lax.all_to_all(expert_part, ("head", "tok"), split_axis=0, concat_axis=0, tiled=True)
        summed = jnp.sum(back.reshape(groups, copies, slots, width).astype(jnp.float32), axis=1)
        part = jnp.dot(
            routing_parts[:, :, c].reshape(local_rows, groups * slots),
            summed.reshape(groups * slots, width),
            precision=lax.Precision.HIGHEST,
            preferred_element_type=jnp.float32,
        )
        routed = part if routed is None else routed + part
    routed = routed.reshape(req_local, qrows, width)
    gate_up = jnp.einsum(
        "cd,djz->jcz",
        head_gather(shared_in[0]),
        w_shared,
        preferred_element_type=jnp.float32,
    )
    hidden_rows = (jax.nn.silu(gate_up[0]) * gate_up[1]).astype(jnp.bfloat16)
    shared_rows = head_scatter_sum(
        jnp.dot(hidden_rows, w_shared_down, preferred_element_type=jnp.float32).astype(
            jnp.bfloat16
        )
    )[None]
    layer_out = middle.astype(jnp.float32) + shared_rows + routed
    return layer_out.astype(jnp.bfloat16)


def solution(mesh):
    return jax.shard_map(
        body,
        mesh=mesh,
        in_specs=(
            P("tok", "head", None),
            P("tok"),
            P(),
            P(None, "head"),
            P("tok", None, "head"),
            P("tok", None, "head"),
            P("head", None),
            P(),
            P(None, None, "head"),
            P("head", None),
            P("tok", "head", None),
            P("tok", "head", None),
            P(),
            P(None, None, ("head", "tok")),
            P(("head", "tok"), None),
        ),
        out_specs=P("tok", "head", None),
        check_vma=False,
    )
```

```python
import math

import jax
import jax.numpy as jnp
from jax import lax
from jax.experimental import pallas as pl
from jax.experimental.pallas import tpu as pltpu
from jax.sharding import PartitionSpec as P

HD = 128
E = 64
TOP = 6


EPS = 1e-06
NEG_BIG = -1e30
CHUNK = 512


def normalize(values, gain_vector):
    wide = values.astype(jnp.float32)
    factor = lax.rsqrt(jnp.mean(wide * wide, axis=-1, keepdims=True) + EPS)
    return (wide * factor * gain_vector).astype(jnp.bfloat16)


def rotary(vectors, positions):
    half_dim = vectors.shape[-1] // 2
    freqs = 10000.0 ** (-jnp.arange(half_dim, dtype=jnp.float32) / half_dim)
    angles = positions.astype(jnp.float32)[:, None] * freqs[None, :]
    cosine = jnp.cos(angles)[:, None, :]
    sine_part = jnp.sin(angles)[:, None, :]
    lower = vectors[..., :half_dim]
    upper = vectors[..., half_dim:]
    return jnp.concatenate(
        [lower * cosine - upper * sine_part, upper * cosine + lower * sine_part], axis=-1
    )


def attend(queries, keys_new, values_new, keys_old, values_old, length):
    factor = 1.0 / math.sqrt(queries.shape[-1])
    score_old = jnp.dot(queries, keys_old.T, preferred_element_type=jnp.float32) * factor
    score_new = jnp.dot(queries, keys_new.T, preferred_element_type=jnp.float32) * factor
    old_slots = jnp.arange(keys_old.shape[0], dtype=jnp.int32)
    live_old = (old_slots < length)[None, :]
    new_slots = jnp.arange(queries.shape[0], dtype=jnp.int32)
    live_new = new_slots[None, :] <= new_slots[:, None]
    row_max = jnp.maximum(
        jnp.max(jnp.where(live_old, score_old, NEG_BIG), axis=1),
        jnp.max(jnp.where(live_new, score_new, NEG_BIG), axis=1),
    )
    prob_old = jnp.where(live_old, jnp.exp(score_old - row_max[:, None]), 0.0)
    prob_new = jnp.where(live_new, jnp.exp(score_new - row_max[:, None]), 0.0)
    denom = jnp.sum(prob_old, axis=1) + jnp.sum(prob_new, axis=1)
    weighted = jnp.dot(
        prob_old.astype(jnp.bfloat16), values_old, preferred_element_type=jnp.float32
    )
    weighted = weighted + jnp.dot(
        prob_new.astype(jnp.bfloat16), values_new, preferred_element_type=jnp.float32
    )
    return (weighted / denom[:, None]).astype(jnp.bfloat16)


def rotate(block, cosine, sine_signed):
    half = block.shape[-1] // 2
    return block * cosine + pltpu.roll(block, half, 1) * sine_signed


def attention_kernel(
    len_ref, q_ref, kn_ref, vn_ref, cq_ref, sq_ref, ck_ref, sk_ref, ko_ref, vo_ref, o_ref, s_ref
):
    rows = q_ref.shape[0]
    new_len = kn_ref.shape[0]
    cache_rows = ko_ref.shape[1]
    chunk = CHUNK if cache_rows % CHUNK == 0 else cache_rows
    chunk_count = cache_rows // chunk
    length = len_ref[0]
    start = pl.program_id(1) * rows
    factor = 1.0 / math.sqrt(q_ref.shape[-1])
    contract = (((1,), (1,)), ((), ()))
    queries = rotate(q_ref[...], cq_ref[...], sq_ref[...]).astype(jnp.bfloat16)
    keys_new = rotate(kn_ref[...], ck_ref[...], sk_ref[...]).astype(jnp.bfloat16)
    values_new = vn_ref[...].astype(jnp.bfloat16)
    score_new = (
        lax.dot_general(queries, keys_new, contract, preferred_element_type=jnp.float32) * factor
    )
    new_cols = lax.broadcasted_iota(jnp.int32, (rows, new_len), 1)
    new_rows = lax.broadcasted_iota(jnp.int32, (rows, new_len), 0) + start
    score_new = jnp.where(new_cols <= new_rows, score_new, NEG_BIG)
    full = jnp.minimum(length // chunk, chunk_count)
    partial = jnp.logical_and(full < chunk_count, length % chunk > 0)
    live = full + partial.astype(jnp.int32)

    def old_scores(index):
        offset = pl.multiple_of(index * chunk, chunk)
        keys = ko_ref[0, pl.ds(offset, chunk), :]
        return lax.dot_general(queries, keys, contract, preferred_element_type=jnp.float32) * factor

    def first_pass(index, row_max):
        scores = old_scores(index)
        s_ref[index] = scores
        return jnp.maximum(row_max, jnp.max(scores, axis=1, keepdims=True))

    row_max = lax.fori_loop(0, full, first_pass, jnp.max(score_new, axis=1, keepdims=True))
    s_ref[full] = jnp.full((rows, chunk), NEG_BIG, jnp.float32)

    @pl.when(partial)
    def _():
        scores = old_scores(full)
        cols = lax.broadcasted_iota(jnp.int32, (rows, chunk), 1) + full * chunk
        s_ref[full] = jnp.where(cols < length, scores, NEG_BIG)

    row_max = jnp.maximum(row_max, jnp.max(s_ref[full], axis=1, keepdims=True))
    prob_new = jnp.exp(score_new - row_max)
    denom = jnp.sum(prob_new, axis=1, keepdims=True)
    weighted = jnp.dot(
        prob_new.astype(jnp.bfloat16), values_new, preferred_element_type=jnp.float32
    )

    def second_pass(index, carry):
        denom, weighted = carry
        probs = jnp.exp(s_ref[index] - row_max)
        offset = pl.multiple_of(index * chunk, chunk)
        values = vo_ref[0, pl.ds(offset, chunk), :]
        denom = denom + jnp.sum(probs, axis=1, keepdims=True)
        weighted = weighted + jnp.dot(
            probs.astype(jnp.bfloat16), values, preferred_element_type=jnp.float32
        )
        return denom, weighted

    denom, weighted = lax.fori_loop(0, live, second_pass, (denom, weighted))
    o_ref[...] = (weighted / denom).astype(o_ref.dtype)


def attention(length, qkv, cosine, sine_signed, k_cache, v_cache):
    new_len = qkv.shape[0]
    cache_rows = k_cache.shape[1]
    heads = qkv.shape[1] // (3 * HD)
    rows = min(256, new_len)
    chunk = CHUNK if cache_rows % CHUNK == 0 else cache_rows
    grid_spec = pltpu.PrefetchScalarGridSpec(
        num_scalar_prefetch=1,
        grid=(heads, new_len // rows),
        in_specs=[
            pl.BlockSpec((rows, HD), lambda h, i, n: (i, 3 * h)),
            pl.BlockSpec((new_len, HD), lambda h, i, n: (0, 3 * h + 1)),
            pl.BlockSpec((new_len, HD), lambda h, i, n: (0, 3 * h + 2)),
            pl.BlockSpec((rows, HD), lambda h, i, n: (i, 0)),
            pl.BlockSpec((rows, HD), lambda h, i, n: (i, 0)),
            pl.BlockSpec((new_len, HD), lambda h, i, n: (0, 0)),
            pl.BlockSpec((new_len, HD), lambda h, i, n: (0, 0)),
            pl.BlockSpec((1, cache_rows, HD), lambda h, i, n: (0, 0, h)),
            pl.BlockSpec((1, cache_rows, HD), lambda h, i, n: (0, 0, h)),
        ],
        out_specs=pl.BlockSpec((rows, HD), lambda h, i, n: (i, h)),
        scratch_shapes=[pltpu.VMEM((cache_rows // chunk + 1, rows, chunk), jnp.float32)],
    )
    return pl.pallas_call(
        attention_kernel,
        grid_spec=grid_spec,
        out_shape=jax.ShapeDtypeStruct((new_len, heads * HD), jnp.bfloat16),
        name="cached_attention",
    )(length, qkv, qkv, qkv, cosine, sine_signed, cosine, sine_signed, k_cache, v_cache)


def cross_perm(count, step):
    pairs = count // 2
    return [(j, ((j // 2 + step) % pairs) * 2 + j % 2) for j in range(count)]


def head_gather(block):
    count = lax.axis_size("head")
    pairs = count // 2
    index = lax.axis_index("head")
    pair, core = index // 2, index % 2
    pieces = [block] + [
        lax.ppermute(block, "head", cross_perm(count, step)) for step in range(1, pairs)
    ]
    stacked = jnp.stack(pieces)
    order = (pair - jnp.arange(pairs, dtype=jnp.int32)) % pairs
    mine = jnp.take(stacked, order, axis=0)
    partner = lax.ppermute(mine, "head", [(j, j ^ 1) for j in range(count)])
    first = jnp.where(core == 0, mine, partner)
    second = jnp.where(core == 0, partner, mine)
    return jnp.stack([first, second], axis=1).reshape((count * block.shape[0],) + block.shape[1:])


def head_scatter_sum(partial):
    count = lax.axis_size("head")
    pairs = count // 2
    index = lax.axis_index("head")
    pair, core = index // 2, index % 2
    blocks = partial.reshape((pairs, 2, partial.shape[0] // count) + partial.shape[1:])
    mine = jnp.where(core == 0, blocks[:, 0], blocks[:, 1])
    other = jnp.where(core == 0, blocks[:, 1], blocks[:, 0])
    received = lax.ppermute(other, "head", [(j, j ^ 1) for j in range(count)])
    chip_sum = mine.astype(jnp.float32) + received.astype(jnp.float32)
    result = jnp.take(chip_sum, pair, axis=0)
    for step in range(1, pairs):
        outgoing = jnp.take(chip_sum, (pair + step) % pairs, axis=0).astype(jnp.bfloat16)
        arrived = lax.ppermute(outgoing, "head", cross_perm(count, step))
        result = result + arrived.astype(jnp.float32)
    return result


def body(
    tokens,
    cache_len,
    attn_gain,
    w_qkv,
    k_cache,
    v_cache,
    w_out,
    moe_gain,
    w_shared,
    w_shared_down,
    expert_ids,
    expert_weights,
    expert_slot,
    w_expert,
    w_expert_down,
):
    req_local, qrows, width = tokens.shape
    head_count = lax.axis_size("head")
    tok_count = lax.axis_size("tok")
    new_len = qrows * head_count
    head_local = w_out.shape[0] // HD
    cache_rows = k_cache.shape[1]
    capacity = 2 * qrows * TOP // E
    slots = req_local * capacity
    local_rows = req_local * qrows
    flat_ids = expert_ids.reshape(req_local, qrows * TOP)
    hits = (flat_ids[:, :, None] == jnp.arange(E, dtype=jnp.int32)[None, None, :]).astype(jnp.int32)
    ranks = jnp.sum((jnp.cumsum(hits, axis=1) - 1) * hits, axis=2)
    slot_of = ranks + jnp.arange(req_local, dtype=jnp.int32)[:, None] * capacity
    place_of = jnp.sum(hits * expert_slot[None, None, :], axis=2)
    target = (place_of * slots + slot_of).reshape(local_rows, TOP)
    columns = jnp.arange(E * slots, dtype=jnp.int32)
    matches = (target[:, :, None] == columns[None, None, :]).astype(jnp.float32)
    placement = jnp.sum(matches, axis=1).astype(jnp.bfloat16)
    routing_matrix = jnp.sum(matches * expert_weights.reshape(local_rows, TOP)[:, :, None], axis=1)
    gathered = head_gather(tokens[0])[None]
    gathered, placement, routing_matrix = lax.optimization_barrier(
        (gathered, placement, routing_matrix)
    )
    normed = normalize(gathered, attn_gain)
    qkv = jnp.dot(normed[0], w_qkv, preferred_element_type=jnp.float32)
    length = cache_len[0]
    positions = length + jnp.arange(new_len, dtype=jnp.int32)
    half_dim = HD // 2
    freqs = 10000.0 ** (-jnp.arange(half_dim, dtype=jnp.float32) / half_dim)
    angles = positions.astype(jnp.float32)[:, None] * freqs[None, :]
    cosine = jnp.cos(angles)
    sine_part = jnp.sin(angles)
    cosine = jnp.concatenate([cosine, cosine], axis=1)
    sine_signed = jnp.concatenate([-sine_part, sine_part], axis=1)
    outputs = [attention(cache_len, qkv, cosine, sine_signed, k_cache, v_cache)]
    attn_rows = head_scatter_sum(
        jnp.dot(outputs[0], w_out, preferred_element_type=jnp.float32).astype(jnp.bfloat16)
    )[None]
    middle = (tokens.astype(jnp.float32) + attn_rows).astype(jnp.bfloat16)
    normed_mid = normalize(middle, moe_gain)
    flat_mid = normed_mid.reshape(local_rows, width)
    outgoing = lax.dot_general(
        placement, flat_mid, (((0,), (0,)), ((), ())), preferred_element_type=jnp.float32
    ).astype(jnp.bfloat16)
    devices = head_count * tok_count
    per_device = max(1, E // devices)
    copies = max(1, devices // E)
    outgoing = outgoing.reshape(E, 1, slots, width)
    if copies > 1:
        outgoing = jnp.broadcast_to(outgoing, (E, copies, slots, width))
    outgoing = outgoing.reshape(devices, per_device, slots, width)
    unit_count = w_expert.shape[2] // per_device
    w_down = w_expert_down.reshape(per_device, unit_count, width)
    groups = E // per_device
    received = [
        lax.all_to_all(outgoing[:, c], ("head", "tok"), split_axis=0, concat_axis=0, tiled=True)
        for c in range(per_device)
    ]
    routing_parts = routing_matrix.reshape(local_rows, groups, per_device, slots)
    routed = None
    for c in range(per_device):
        w_pair = w_expert[:, :, c * unit_count : (c + 1) * unit_count]
        gate_up = jnp.einsum(
            "gsd,dju->jgsu", received[c], w_pair, preferred_element_type=jnp.float32
        )
        hidden_part = (jax.nn.silu(gate_up[0]) * gate_up[1]).astype(jnp.bfloat16)
        expert_part = jnp.einsum(
            "gsu,ud->gsd", hidden_part, w_down[c], preferred_element_type=jnp.float32
        ).astype(jnp.bfloat16)
        if c == per_device - 1:
            expert_part, shared_in = lax.optimization_barrier((expert_part, normed_mid))
        back = lax.all_to_all(expert_part, ("head", "tok"), split_axis=0, concat_axis=0, tiled=True)
        summed = jnp.sum(back.reshape(groups, copies, slots, width).astype(jnp.float32), axis=1)
        part = jnp.dot(
            routing_parts[:, :, c].reshape(local_rows, groups * slots),
            summed.reshape(groups * slots, width),
            precision=lax.Precision.HIGHEST,
            preferred_element_type=jnp.float32,
        )
        routed = part if routed is None else routed + part
    routed = routed.reshape(req_local, qrows, width)
    gate_up = jnp.einsum(
        "cd,djz->jcz",
        head_gather(shared_in[0]),
        w_shared,
        preferred_element_type=jnp.float32,
    )
    hidden_rows = (jax.nn.silu(gate_up[0]) * gate_up[1]).astype(jnp.bfloat16)
    shared_rows = head_scatter_sum(
        jnp.dot(hidden_rows, w_shared_down, preferred_element_type=jnp.float32).astype(
            jnp.bfloat16
        )
    )[None]
    layer_out = middle.astype(jnp.float32) + shared_rows + routed
    return layer_out.astype(jnp.bfloat16)


def solution(mesh):
    return jax.shard_map(
        body,
        mesh=mesh,
        in_specs=(
            P("tok", "head", None),
            P("tok"),
            P(),
            P(None, "head"),
            P("tok", None, "head"),
            P("tok", None, "head"),
            P("head", None),
            P(),
            P(None, None, "head"),
            P("head", None),
            P("tok", "head", None),
            P("tok", "head", None),
            P(),
            P(None, None, ("head", "tok")),
            P(("head", "tok"), None),
        ),
        out_specs=P("tok", "head", None),
        check_vma=False,
    )
```

```python
import math

import jax
import jax.numpy as jnp
from jax import lax
from jax.experimental import pallas as pl
from jax.experimental.pallas import tpu as pltpu
from jax.sharding import PartitionSpec as P

HD = 128
E = 64
TOP = 6


EPS = 1e-06
NEG_BIG = -1e30


def normalize(values, gain_vector):
    wide = values.astype(jnp.float32)
    factor = lax.rsqrt(jnp.mean(wide * wide, axis=-1, keepdims=True) + EPS)
    return (wide * factor * gain_vector).astype(jnp.bfloat16)


def rotary(vectors, positions):
    half_dim = vectors.shape[-1] // 2
    freqs = 10000.0 ** (-jnp.arange(half_dim, dtype=jnp.float32) / half_dim)
    angles = positions.astype(jnp.float32)[:, None] * freqs[None, :]
    cosine = jnp.cos(angles)[:, None, :]
    sine_part = jnp.sin(angles)[:, None, :]
    lower = vectors[..., :half_dim]
    upper = vectors[..., half_dim:]
    return jnp.concatenate(
        [lower * cosine - upper * sine_part, upper * cosine + lower * sine_part], axis=-1
    )


def attend(queries, keys_new, values_new, keys_old, values_old, length):
    factor = 1.0 / math.sqrt(queries.shape[-1])
    score_old = jnp.dot(queries, keys_old.T, preferred_element_type=jnp.float32) * factor
    score_new = jnp.dot(queries, keys_new.T, preferred_element_type=jnp.float32) * factor
    old_slots = jnp.arange(keys_old.shape[0], dtype=jnp.int32)
    live_old = (old_slots < length)[None, :]
    new_slots = jnp.arange(queries.shape[0], dtype=jnp.int32)
    live_new = new_slots[None, :] <= new_slots[:, None]
    row_max = jnp.maximum(
        jnp.max(jnp.where(live_old, score_old, NEG_BIG), axis=1),
        jnp.max(jnp.where(live_new, score_new, NEG_BIG), axis=1),
    )
    prob_old = jnp.where(live_old, jnp.exp(score_old - row_max[:, None]), 0.0)
    prob_new = jnp.where(live_new, jnp.exp(score_new - row_max[:, None]), 0.0)
    denom = jnp.sum(prob_old, axis=1) + jnp.sum(prob_new, axis=1)
    weighted = jnp.dot(
        prob_old.astype(jnp.bfloat16), values_old, preferred_element_type=jnp.float32
    )
    weighted = weighted + jnp.dot(
        prob_new.astype(jnp.bfloat16), values_new, preferred_element_type=jnp.float32
    )
    return (weighted / denom[:, None]).astype(jnp.bfloat16)


def rotate(block, cosine, sine_signed):
    half = block.shape[-1] // 2
    return block * cosine + pltpu.roll(block, half, 1) * sine_signed


def attention_kernel(
    len_ref, q_ref, kn_ref, vn_ref, cq_ref, sq_ref, ck_ref, sk_ref, ko_ref, vo_ref, o_ref
):
    rows = q_ref.shape[0]
    new_len = kn_ref.shape[0]
    cache_rows = ko_ref.shape[1]
    length = len_ref[0]
    start = pl.program_id(1) * rows

    def compute(mask_cache):
        factor = 1.0 / math.sqrt(q_ref.shape[-1])
        contract = (((1,), (1,)), ((), ()))
        queries = rotate(q_ref[...], cq_ref[...], sq_ref[...]).astype(jnp.bfloat16)
        keys_new = rotate(kn_ref[...], ck_ref[...], sk_ref[...]).astype(jnp.bfloat16)
        values_new = vn_ref[...].astype(jnp.bfloat16)
        score_old = (
            lax.dot_general(queries, ko_ref[0], contract, preferred_element_type=jnp.float32)
            * factor
        )
        score_new = (
            lax.dot_general(queries, keys_new, contract, preferred_element_type=jnp.float32)
            * factor
        )
        if mask_cache:
            live_old = lax.broadcasted_iota(jnp.int32, (rows, cache_rows), 1) < length
            score_old = jnp.where(live_old, score_old, NEG_BIG)
        new_cols = lax.broadcasted_iota(jnp.int32, (rows, new_len), 1)
        new_rows = lax.broadcasted_iota(jnp.int32, (rows, new_len), 0) + start
        score_new = jnp.where(new_cols <= new_rows, score_new, NEG_BIG)
        row_max = jnp.maximum(
            jnp.max(score_old, axis=1, keepdims=True), jnp.max(score_new, axis=1, keepdims=True)
        )
        prob_old = jnp.exp(score_old - row_max)
        prob_new = jnp.exp(score_new - row_max)
        denom = jnp.sum(prob_old, axis=1, keepdims=True) + jnp.sum(
            prob_new, axis=1, keepdims=True
        )
        weighted = jnp.dot(
            prob_old.astype(jnp.bfloat16), vo_ref[0], preferred_element_type=jnp.float32
        )
        weighted = weighted + jnp.dot(
            prob_new.astype(jnp.bfloat16), values_new, preferred_element_type=jnp.float32
        )
        o_ref[...] = (weighted / denom).astype(o_ref.dtype)

    @pl.when(length >= cache_rows)
    def _():
        compute(False)

    @pl.when(length < cache_rows)
    def _():
        compute(True)


def attention(length, qkv, cosine, sine_signed, k_cache, v_cache):
    new_len = qkv.shape[0]
    cache_rows = k_cache.shape[1]
    heads = qkv.shape[1] // (3 * HD)
    rows = min(256, new_len)
    grid_spec = pltpu.PrefetchScalarGridSpec(
        num_scalar_prefetch=1,
        grid=(heads, new_len // rows),
        in_specs=[
            pl.BlockSpec((rows, HD), lambda h, i, n: (i, 3 * h)),
            pl.BlockSpec((new_len, HD), lambda h, i, n: (0, 3 * h + 1)),
            pl.BlockSpec((new_len, HD), lambda h, i, n: (0, 3 * h + 2)),
            pl.BlockSpec((rows, HD), lambda h, i, n: (i, 0)),
            pl.BlockSpec((rows, HD), lambda h, i, n: (i, 0)),
            pl.BlockSpec((new_len, HD), lambda h, i, n: (0, 0)),
            pl.BlockSpec((new_len, HD), lambda h, i, n: (0, 0)),
            pl.BlockSpec((1, cache_rows, HD), lambda h, i, n: (0, 0, h)),
            pl.BlockSpec((1, cache_rows, HD), lambda h, i, n: (0, 0, h)),
        ],
        out_specs=pl.BlockSpec((rows, HD), lambda h, i, n: (i, h)),
    )
    return pl.pallas_call(
        attention_kernel,
        grid_spec=grid_spec,
        out_shape=jax.ShapeDtypeStruct((new_len, heads * HD), jnp.bfloat16),
        name="cached_attention",
    )(length, qkv, qkv, qkv, cosine, sine_signed, cosine, sine_signed, k_cache, v_cache)


def cross_perm(count, step):
    pairs = count // 2
    return [(j, ((j // 2 + step) % pairs) * 2 + j % 2) for j in range(count)]


def head_gather(block):
    count = lax.axis_size("head")
    pairs = count // 2
    index = lax.axis_index("head")
    pair, core = index // 2, index % 2
    pieces = [block] + [
        lax.ppermute(block, "head", cross_perm(count, step)) for step in range(1, pairs)
    ]
    stacked = jnp.stack(pieces)
    order = (pair - jnp.arange(pairs, dtype=jnp.int32)) % pairs
    mine = jnp.take(stacked, order, axis=0)
    partner = lax.ppermute(mine, "head", [(j, j ^ 1) for j in range(count)])
    first = jnp.where(core == 0, mine, partner)
    second = jnp.where(core == 0, partner, mine)
    return jnp.stack([first, second], axis=1).reshape((count * block.shape[0],) + block.shape[1:])


def head_scatter_sum(partial):
    count = lax.axis_size("head")
    pairs = count // 2
    index = lax.axis_index("head")
    pair, core = index // 2, index % 2
    blocks = partial.reshape((pairs, 2, partial.shape[0] // count) + partial.shape[1:])
    mine = jnp.where(core == 0, blocks[:, 0], blocks[:, 1])
    other = jnp.where(core == 0, blocks[:, 1], blocks[:, 0])
    received = lax.ppermute(other, "head", [(j, j ^ 1) for j in range(count)])
    chip_sum = mine.astype(jnp.float32) + received.astype(jnp.float32)
    result = jnp.take(chip_sum, pair, axis=0)
    for step in range(1, pairs):
        outgoing = jnp.take(chip_sum, (pair + step) % pairs, axis=0).astype(jnp.bfloat16)
        arrived = lax.ppermute(outgoing, "head", cross_perm(count, step))
        result = result + arrived.astype(jnp.float32)
    return result


def body(
    tokens,
    cache_len,
    attn_gain,
    w_qkv,
    k_cache,
    v_cache,
    w_out,
    moe_gain,
    w_shared,
    w_shared_down,
    expert_ids,
    expert_weights,
    expert_slot,
    w_expert,
    w_expert_down,
):
    req_local, qrows, width = tokens.shape
    head_count = lax.axis_size("head")
    tok_count = lax.axis_size("tok")
    new_len = qrows * head_count
    head_local = w_out.shape[0] // HD
    cache_rows = k_cache.shape[1]
    capacity = 2 * qrows * TOP // E
    slots = req_local * capacity
    local_rows = req_local * qrows
    flat_ids = expert_ids.reshape(req_local, qrows * TOP)
    hits = (flat_ids[:, :, None] == jnp.arange(E, dtype=jnp.int32)[None, None, :]).astype(jnp.int32)
    ranks = jnp.sum((jnp.cumsum(hits, axis=1) - 1) * hits, axis=2)
    slot_of = ranks + jnp.arange(req_local, dtype=jnp.int32)[:, None] * capacity
    place_of = jnp.sum(hits * expert_slot[None, None, :], axis=2)
    target = (place_of * slots + slot_of).reshape(local_rows, TOP)
    columns = jnp.arange(E * slots, dtype=jnp.int32)
    matches = (target[:, :, None] == columns[None, None, :]).astype(jnp.float32)
    placement = jnp.sum(matches, axis=1).astype(jnp.bfloat16)
    routing_matrix = jnp.sum(matches * expert_weights.reshape(local_rows, TOP)[:, :, None], axis=1)
    normed = head_gather(normalize(tokens[0], attn_gain))[None]
    normed, placement, routing_matrix = lax.optimization_barrier(
        (normed, placement, routing_matrix)
    )
    qkv = jnp.dot(normed[0], w_qkv, preferred_element_type=jnp.float32)
    length = cache_len[0]
    positions = length + jnp.arange(new_len, dtype=jnp.int32)
    half_dim = HD // 2
    freqs = 10000.0 ** (-jnp.arange(half_dim, dtype=jnp.float32) / half_dim)
    angles = positions.astype(jnp.float32)[:, None] * freqs[None, :]
    cosine = jnp.cos(angles)
    sine_part = jnp.sin(angles)
    cosine = jnp.concatenate([cosine, cosine], axis=1)
    sine_signed = jnp.concatenate([-sine_part, sine_part], axis=1)
    outputs = [attention(cache_len, qkv, cosine, sine_signed, k_cache, v_cache)]
    attn_rows = head_scatter_sum(
        jnp.dot(outputs[0], w_out, preferred_element_type=jnp.float32).astype(jnp.bfloat16)
    )[None]
    middle = (tokens.astype(jnp.float32) + attn_rows).astype(jnp.bfloat16)
    normed_mid = normalize(middle, moe_gain)
    flat_mid = normed_mid.reshape(local_rows, width)
    outgoing = lax.dot_general(
        placement, flat_mid, (((0,), (0,)), ((), ())), preferred_element_type=jnp.float32
    ).astype(jnp.bfloat16)
    devices = head_count * tok_count
    per_device = max(1, E // devices)
    copies = max(1, devices // E)
    outgoing = outgoing.reshape(E, 1, slots, width)
    if copies > 1:
        outgoing = jnp.broadcast_to(outgoing, (E, copies, slots, width))
    outgoing = outgoing.reshape(devices, per_device, slots, width)
    unit_count = w_expert.shape[2] // per_device
    w_down = w_expert_down.reshape(per_device, unit_count, width)
    groups = E // per_device
    received = [
        lax.all_to_all(outgoing[:, c], ("head", "tok"), split_axis=0, concat_axis=0, tiled=True)
        for c in range(per_device)
    ]
    routing_parts = routing_matrix.reshape(local_rows, groups, per_device, slots)
    routed = None
    for c in range(per_device):
        w_pair = w_expert[:, :, c * unit_count : (c + 1) * unit_count]
        gate_up = jnp.einsum(
            "gsd,dju->jgsu", received[c], w_pair, preferred_element_type=jnp.float32
        )
        hidden_part = (jax.nn.silu(gate_up[0]) * gate_up[1]).astype(jnp.bfloat16)
        expert_part = jnp.einsum(
            "gsu,ud->gsd", hidden_part, w_down[c], preferred_element_type=jnp.float32
        ).astype(jnp.bfloat16)
        if c == per_device - 1:
            expert_part, shared_in = lax.optimization_barrier((expert_part, normed_mid))
        back = lax.all_to_all(expert_part, ("head", "tok"), split_axis=0, concat_axis=0, tiled=True)
        summed = jnp.sum(back.reshape(groups, copies, slots, width).astype(jnp.float32), axis=1)
        part = jnp.dot(
            routing_parts[:, :, c].reshape(local_rows, groups * slots),
            summed.reshape(groups * slots, width),
            precision=lax.Precision.HIGHEST,
            preferred_element_type=jnp.float32,
        )
        routed = part if routed is None else routed + part
    routed = routed.reshape(req_local, qrows, width)
    gate_up = jnp.einsum(
        "cd,djz->jcz",
        head_gather(shared_in[0]),
        w_shared,
        preferred_element_type=jnp.float32,
    )
    hidden_rows = (jax.nn.silu(gate_up[0]) * gate_up[1]).astype(jnp.bfloat16)
    shared_rows = head_scatter_sum(
        jnp.dot(hidden_rows, w_shared_down, preferred_element_type=jnp.float32).astype(
            jnp.bfloat16
        )
    )[None]
    layer_out = middle.astype(jnp.float32) + shared_rows + routed
    return layer_out.astype(jnp.bfloat16)


def solution(mesh):
    return jax.shard_map(
        body,
        mesh=mesh,
        in_specs=(
            P("tok", "head", None),
            P("tok"),
            P(),
            P(None, "head"),
            P("tok", None, "head"),
            P("tok", None, "head"),
            P("head", None),
            P(),
            P(None, None, "head"),
            P("head", None),
            P("tok", "head", None),
            P("tok", "head", None),
            P(),
            P(None, None, ("head", "tok")),
            P(("head", "tok"), None),
        ),
        out_specs=P("tok", "head", None),
        check_vma=False,
    )
```

```python
import math

import jax
import jax.numpy as jnp
from jax import lax
from jax.experimental import pallas as pl
from jax.experimental.pallas import tpu as pltpu
from jax.sharding import PartitionSpec as P

HD = 128
E = 64
TOP = 6


EPS = 1e-06
NEG_BIG = -1e30


def normalize(values, gain_vector):
    wide = values.astype(jnp.float32)
    factor = lax.rsqrt(jnp.mean(wide * wide, axis=-1, keepdims=True) + EPS)
    return (wide * factor * gain_vector).astype(jnp.bfloat16)


def rotary(vectors, positions):
    half_dim = vectors.shape[-1] // 2
    freqs = 10000.0 ** (-jnp.arange(half_dim, dtype=jnp.float32) / half_dim)
    angles = positions.astype(jnp.float32)[:, None] * freqs[None, :]
    cosine = jnp.cos(angles)[:, None, :]
    sine_part = jnp.sin(angles)[:, None, :]
    lower = vectors[..., :half_dim]
    upper = vectors[..., half_dim:]
    return jnp.concatenate(
        [lower * cosine - upper * sine_part, upper * cosine + lower * sine_part], axis=-1
    )


def attend(queries, keys_new, values_new, keys_old, values_old, length):
    factor = 1.0 / math.sqrt(queries.shape[-1])
    score_old = jnp.dot(queries, keys_old.T, preferred_element_type=jnp.float32) * factor
    score_new = jnp.dot(queries, keys_new.T, preferred_element_type=jnp.float32) * factor
    old_slots = jnp.arange(keys_old.shape[0], dtype=jnp.int32)
    live_old = (old_slots < length)[None, :]
    new_slots = jnp.arange(queries.shape[0], dtype=jnp.int32)
    live_new = new_slots[None, :] <= new_slots[:, None]
    row_max = jnp.maximum(
        jnp.max(jnp.where(live_old, score_old, NEG_BIG), axis=1),
        jnp.max(jnp.where(live_new, score_new, NEG_BIG), axis=1),
    )
    prob_old = jnp.where(live_old, jnp.exp(score_old - row_max[:, None]), 0.0)
    prob_new = jnp.where(live_new, jnp.exp(score_new - row_max[:, None]), 0.0)
    denom = jnp.sum(prob_old, axis=1) + jnp.sum(prob_new, axis=1)
    weighted = jnp.dot(
        prob_old.astype(jnp.bfloat16), values_old, preferred_element_type=jnp.float32
    )
    weighted = weighted + jnp.dot(
        prob_new.astype(jnp.bfloat16), values_new, preferred_element_type=jnp.float32
    )
    return (weighted / denom[:, None]).astype(jnp.bfloat16)


def rotate(block, cosine, sine_signed):
    half = block.shape[-1] // 2
    return block * cosine + pltpu.roll(block, half, 1) * sine_signed


def attention_kernel(
    len_ref, q_ref, kn_ref, vn_ref, cq_ref, sq_ref, ck_ref, sk_ref, ko_ref, vo_ref, o_ref
):
    rows = q_ref.shape[0]
    new_len = kn_ref.shape[0]
    cache_rows = ko_ref.shape[1]
    length = len_ref[0]
    start = pl.program_id(1) * rows

    def compute(mask_cache):
        factor = 1.0 / math.sqrt(q_ref.shape[-1])
        contract = (((1,), (1,)), ((), ()))
        queries = rotate(q_ref[...], cq_ref[...], sq_ref[...]).astype(jnp.bfloat16)
        keys_new = rotate(kn_ref[...], ck_ref[...], sk_ref[...]).astype(jnp.bfloat16)
        values_new = vn_ref[...].astype(jnp.bfloat16)
        score_old = (
            lax.dot_general(queries, ko_ref[0], contract, preferred_element_type=jnp.float32)
            * factor
        )
        score_new = (
            lax.dot_general(queries, keys_new, contract, preferred_element_type=jnp.float32)
            * factor
        )
        if mask_cache:
            live_old = lax.broadcasted_iota(jnp.int32, (rows, cache_rows), 1) < length
            score_old = jnp.where(live_old, score_old, NEG_BIG)
        new_cols = lax.broadcasted_iota(jnp.int32, (rows, new_len), 1)
        new_rows = lax.broadcasted_iota(jnp.int32, (rows, new_len), 0) + start
        score_new = jnp.where(new_cols <= new_rows, score_new, NEG_BIG)
        row_max = jnp.maximum(
            jnp.max(score_old, axis=1, keepdims=True), jnp.max(score_new, axis=1, keepdims=True)
        )
        prob_old = jnp.exp(score_old - row_max)
        prob_new = jnp.exp(score_new - row_max)
        denom = jnp.sum(prob_old, axis=1, keepdims=True) + jnp.sum(
            prob_new, axis=1, keepdims=True
        )
        weighted = jnp.dot(
            prob_old.astype(jnp.bfloat16), vo_ref[0], preferred_element_type=jnp.float32
        )
        weighted = weighted + jnp.dot(
            prob_new.astype(jnp.bfloat16), values_new, preferred_element_type=jnp.float32
        )
        o_ref[...] = (weighted / denom).astype(o_ref.dtype)

    @pl.when(length >= cache_rows)
    def _():
        compute(False)

    @pl.when(length < cache_rows)
    def _():
        compute(True)


def attention(length, qkv, cosine, sine_signed, k_cache, v_cache):
    new_len = qkv.shape[0]
    cache_rows = k_cache.shape[1]
    heads = qkv.shape[1] // (3 * HD)
    rows = min(256, new_len)
    grid_spec = pltpu.PrefetchScalarGridSpec(
        num_scalar_prefetch=1,
        grid=(heads, new_len // rows),
        in_specs=[
            pl.BlockSpec((rows, HD), lambda h, i, n: (i, 3 * h)),
            pl.BlockSpec((new_len, HD), lambda h, i, n: (0, 3 * h + 1)),
            pl.BlockSpec((new_len, HD), lambda h, i, n: (0, 3 * h + 2)),
            pl.BlockSpec((rows, HD), lambda h, i, n: (i, 0)),
            pl.BlockSpec((rows, HD), lambda h, i, n: (i, 0)),
            pl.BlockSpec((new_len, HD), lambda h, i, n: (0, 0)),
            pl.BlockSpec((new_len, HD), lambda h, i, n: (0, 0)),
            pl.BlockSpec((1, cache_rows, HD), lambda h, i, n: (0, 0, h)),
            pl.BlockSpec((1, cache_rows, HD), lambda h, i, n: (0, 0, h)),
        ],
        out_specs=pl.BlockSpec((rows, HD), lambda h, i, n: (i, h)),
    )
    return pl.pallas_call(
        attention_kernel,
        grid_spec=grid_spec,
        out_shape=jax.ShapeDtypeStruct((new_len, heads * HD), jnp.bfloat16),
        name="cached_attention",
    )(length, qkv, qkv, qkv, cosine, sine_signed, cosine, sine_signed, k_cache, v_cache)


def cross_perm(count, step):
    pairs = count // 2
    return [(j, ((j // 2 + step) % pairs) * 2 + j % 2) for j in range(count)]


def head_gather(block):
    count = lax.axis_size("head")
    pairs = count // 2
    index = lax.axis_index("head")
    pair, core = index // 2, index % 2
    pieces = [block] + [
        lax.ppermute(block, "head", cross_perm(count, step)) for step in range(1, pairs)
    ]
    stacked = jnp.stack(pieces)
    order = (pair - jnp.arange(pairs, dtype=jnp.int32)) % pairs
    mine = jnp.take(stacked, order, axis=0)
    partner = lax.ppermute(mine, "head", [(j, j ^ 1) for j in range(count)])
    first = jnp.where(core == 0, mine, partner)
    second = jnp.where(core == 0, partner, mine)
    return jnp.stack([first, second], axis=1).reshape((count * block.shape[0],) + block.shape[1:])


def head_scatter_sum(partial):
    count = lax.axis_size("head")
    pairs = count // 2
    index = lax.axis_index("head")
    pair, core = index // 2, index % 2
    blocks = partial.reshape((pairs, 2, partial.shape[0] // count) + partial.shape[1:])
    mine = jnp.where(core == 0, blocks[:, 0], blocks[:, 1])
    other = jnp.where(core == 0, blocks[:, 1], blocks[:, 0])
    received = lax.ppermute(other, "head", [(j, j ^ 1) for j in range(count)])
    chip_sum = mine.astype(jnp.float32) + received.astype(jnp.float32)
    result = jnp.take(chip_sum, pair, axis=0)
    for step in range(1, pairs):
        outgoing = jnp.take(chip_sum, (pair + step) % pairs, axis=0).astype(jnp.bfloat16)
        arrived = lax.ppermute(outgoing, "head", cross_perm(count, step))
        result = result + arrived.astype(jnp.float32)
    return result


def body(
    tokens,
    cache_len,
    attn_gain,
    w_qkv,
    k_cache,
    v_cache,
    w_out,
    moe_gain,
    w_shared,
    w_shared_down,
    expert_ids,
    expert_weights,
    expert_slot,
    w_expert,
    w_expert_down,
):
    req_local, qrows, width = tokens.shape
    head_count = lax.axis_size("head")
    tok_count = lax.axis_size("tok")
    new_len = qrows * head_count
    head_local = w_out.shape[0] // HD
    cache_rows = k_cache.shape[1]
    capacity = 2 * qrows * TOP // E
    slots = req_local * capacity
    local_rows = req_local * qrows
    flat_ids = expert_ids.reshape(req_local, qrows * TOP)
    hits = (flat_ids[:, :, None] == jnp.arange(E, dtype=jnp.int32)[None, None, :]).astype(jnp.int32)
    ranks = jnp.sum((jnp.cumsum(hits, axis=1) - 1) * hits, axis=2)
    slot_of = ranks + jnp.arange(req_local, dtype=jnp.int32)[:, None] * capacity
    place_of = jnp.sum(hits * expert_slot[None, None, :], axis=2)
    target = (place_of * slots + slot_of).reshape(local_rows, TOP)
    columns = jnp.arange(E * slots, dtype=jnp.int32)
    matches = (target[:, :, None] == columns[None, None, :]).astype(jnp.float32)
    placement = jnp.sum(matches, axis=1).astype(jnp.bfloat16)
    routing_matrix = jnp.sum(matches * expert_weights.reshape(local_rows, TOP)[:, :, None], axis=1)
    gathered = head_gather(tokens[0])[None]
    gathered, placement, routing_matrix = lax.optimization_barrier(
        (gathered, placement, routing_matrix)
    )
    normed = normalize(gathered, attn_gain)
    qkv = jnp.dot(normed[0], w_qkv, preferred_element_type=jnp.float32)
    length = cache_len[0]
    positions = length + jnp.arange(new_len, dtype=jnp.int32)
    half_dim = HD // 2
    freqs = 10000.0 ** (-jnp.arange(half_dim, dtype=jnp.float32) / half_dim)
    angles = positions.astype(jnp.float32)[:, None] * freqs[None, :]
    cosine = jnp.cos(angles)
    sine_part = jnp.sin(angles)
    cosine = jnp.concatenate([cosine, cosine], axis=1)
    sine_signed = jnp.concatenate([-sine_part, sine_part], axis=1)
    outputs = [attention(cache_len, qkv, cosine, sine_signed, k_cache, v_cache)]
    attn_rows = head_scatter_sum(
        jnp.dot(outputs[0], w_out, preferred_element_type=jnp.float32).astype(jnp.bfloat16)
    )[None]
    middle = (tokens.astype(jnp.float32) + attn_rows).astype(jnp.bfloat16)
    normed_mid = normalize(middle, moe_gain)
    flat_mid = normed_mid.reshape(local_rows, width)
    outgoing = lax.dot_general(
        placement, flat_mid, (((0,), (0,)), ((), ())), preferred_element_type=jnp.float32
    ).astype(jnp.bfloat16)
    devices = head_count * tok_count
    per_device = max(1, E // devices)
    copies = max(1, devices // E)
    outgoing = outgoing.reshape(E, 1, slots, width)
    if copies > 1:
        outgoing = jnp.broadcast_to(outgoing, (E, copies, slots, width))
    outgoing = outgoing.reshape(devices, per_device, slots, width)
    unit_count = w_expert.shape[2] // per_device
    w_down = w_expert_down.reshape(per_device, unit_count, width)
    groups = E // per_device
    received = [
        lax.all_to_all(outgoing[:, c], ("head", "tok"), split_axis=0, concat_axis=0, tiled=True)
        for c in range(per_device)
    ]
    received[0], shared_in = lax.optimization_barrier((received[0], normed_mid))
    gathered_mid = head_gather(shared_in[0])
    routing_parts = routing_matrix.reshape(local_rows, groups, per_device, slots)
    routed = None
    for c in range(per_device):
        w_pair = w_expert[:, :, c * unit_count : (c + 1) * unit_count]
        gate_up = jnp.einsum(
            "gsd,dju->jgsu", received[c], w_pair, preferred_element_type=jnp.float32
        )
        hidden_part = (jax.nn.silu(gate_up[0]) * gate_up[1]).astype(jnp.bfloat16)
        expert_part = jnp.einsum(
            "gsu,ud->gsd", hidden_part, w_down[c], preferred_element_type=jnp.float32
        ).astype(jnp.bfloat16)
        if c == per_device - 1:
            expert_part, gathered_mid = lax.optimization_barrier((expert_part, gathered_mid))
        back = lax.all_to_all(expert_part, ("head", "tok"), split_axis=0, concat_axis=0, tiled=True)
        summed = jnp.sum(back.reshape(groups, copies, slots, width).astype(jnp.float32), axis=1)
        part = jnp.dot(
            routing_parts[:, :, c].reshape(local_rows, groups * slots),
            summed.reshape(groups * slots, width),
            precision=lax.Precision.HIGHEST,
            preferred_element_type=jnp.float32,
        )
        routed = part if routed is None else routed + part
    routed = routed.reshape(req_local, qrows, width)
    gate_up = jnp.einsum(
        "cd,djz->jcz",
        gathered_mid,
        w_shared,
        preferred_element_type=jnp.float32,
    )
    hidden_rows = (jax.nn.silu(gate_up[0]) * gate_up[1]).astype(jnp.bfloat16)
    shared_rows = head_scatter_sum(
        jnp.dot(hidden_rows, w_shared_down, preferred_element_type=jnp.float32).astype(
            jnp.bfloat16
        )
    )[None]
    layer_out = middle.astype(jnp.float32) + shared_rows + routed
    return layer_out.astype(jnp.bfloat16)


def solution(mesh):
    return jax.shard_map(
        body,
        mesh=mesh,
        in_specs=(
            P("tok", "head", None),
            P("tok"),
            P(),
            P(None, "head"),
            P("tok", None, "head"),
            P("tok", None, "head"),
            P("head", None),
            P(),
            P(None, None, "head"),
            P("head", None),
            P("tok", "head", None),
            P("tok", "head", None),
            P(),
            P(None, None, ("head", "tok")),
            P(("head", "tok"), None),
        ),
        out_specs=P("tok", "head", None),
        check_vma=False,
    )
```

```python
import math

import jax
import jax.numpy as jnp
from jax import lax
from jax.experimental import pallas as pl
from jax.experimental.pallas import tpu as pltpu
from jax.sharding import PartitionSpec as P

HD = 128
E = 64
TOP = 6


EPS = 1e-06
NEG_BIG = -1e30


def normalize(values, gain_vector):
    wide = values.astype(jnp.float32)
    factor = lax.rsqrt(jnp.mean(wide * wide, axis=-1, keepdims=True) + EPS)
    return (wide * factor * gain_vector).astype(jnp.bfloat16)


def rotary(vectors, positions):
    half_dim = vectors.shape[-1] // 2
    freqs = 10000.0 ** (-jnp.arange(half_dim, dtype=jnp.float32) / half_dim)
    angles = positions.astype(jnp.float32)[:, None] * freqs[None, :]
    cosine = jnp.cos(angles)[:, None, :]
    sine_part = jnp.sin(angles)[:, None, :]
    lower = vectors[..., :half_dim]
    upper = vectors[..., half_dim:]
    return jnp.concatenate(
        [lower * cosine - upper * sine_part, upper * cosine + lower * sine_part], axis=-1
    )


def attend(queries, keys_new, values_new, keys_old, values_old, length):
    factor = 1.0 / math.sqrt(queries.shape[-1])
    score_old = jnp.dot(queries, keys_old.T, preferred_element_type=jnp.float32) * factor
    score_new = jnp.dot(queries, keys_new.T, preferred_element_type=jnp.float32) * factor
    old_slots = jnp.arange(keys_old.shape[0], dtype=jnp.int32)
    live_old = (old_slots < length)[None, :]
    new_slots = jnp.arange(queries.shape[0], dtype=jnp.int32)
    live_new = new_slots[None, :] <= new_slots[:, None]
    row_max = jnp.maximum(
        jnp.max(jnp.where(live_old, score_old, NEG_BIG), axis=1),
        jnp.max(jnp.where(live_new, score_new, NEG_BIG), axis=1),
    )
    prob_old = jnp.where(live_old, jnp.exp(score_old - row_max[:, None]), 0.0)
    prob_new = jnp.where(live_new, jnp.exp(score_new - row_max[:, None]), 0.0)
    denom = jnp.sum(prob_old, axis=1) + jnp.sum(prob_new, axis=1)
    weighted = jnp.dot(
        prob_old.astype(jnp.bfloat16), values_old, preferred_element_type=jnp.float32
    )
    weighted = weighted + jnp.dot(
        prob_new.astype(jnp.bfloat16), values_new, preferred_element_type=jnp.float32
    )
    return (weighted / denom[:, None]).astype(jnp.bfloat16)


def rotate(block, cosine, sine_signed):
    half = block.shape[-1] // 2
    return block * cosine + pltpu.roll(block, half, 1) * sine_signed


def attention_kernel(
    len_ref, q_ref, kn_ref, vn_ref, cq_ref, sq_ref, ck_ref, sk_ref, ko_ref, vo_ref, o_ref
):
    rows = q_ref.shape[0]
    new_len = kn_ref.shape[0]
    cache_rows = ko_ref.shape[1]
    length = len_ref[0]
    start = pl.program_id(1) * rows

    def compute(mask_cache):
        factor = 1.0 / math.sqrt(q_ref.shape[-1])
        contract = (((1,), (1,)), ((), ()))
        queries = rotate(q_ref[...], cq_ref[...], sq_ref[...]).astype(jnp.bfloat16)
        keys_new = rotate(kn_ref[...], ck_ref[...], sk_ref[...]).astype(jnp.bfloat16)
        values_new = vn_ref[...].astype(jnp.bfloat16)
        score_old = (
            lax.dot_general(queries, ko_ref[0], contract, preferred_element_type=jnp.float32)
            * factor
        )
        score_new = (
            lax.dot_general(queries, keys_new, contract, preferred_element_type=jnp.float32)
            * factor
        )
        if mask_cache:
            live_old = lax.broadcasted_iota(jnp.int32, (rows, cache_rows), 1) < length
            score_old = jnp.where(live_old, score_old, NEG_BIG)
        new_cols = lax.broadcasted_iota(jnp.int32, (rows, new_len), 1)
        new_rows = lax.broadcasted_iota(jnp.int32, (rows, new_len), 0) + start
        score_new = jnp.where(new_cols <= new_rows, score_new, NEG_BIG)
        row_max = jnp.maximum(
            jnp.max(score_old, axis=1, keepdims=True), jnp.max(score_new, axis=1, keepdims=True)
        )
        prob_old = jnp.exp(score_old - row_max)
        prob_new = jnp.exp(score_new - row_max)
        denom = jnp.sum(prob_old, axis=1, keepdims=True) + jnp.sum(
            prob_new, axis=1, keepdims=True
        )
        weighted = jnp.dot(
            prob_old.astype(jnp.bfloat16), vo_ref[0], preferred_element_type=jnp.float32
        )
        weighted = weighted + jnp.dot(
            prob_new.astype(jnp.bfloat16), values_new, preferred_element_type=jnp.float32
        )
        o_ref[...] = (weighted / denom).astype(o_ref.dtype)

    @pl.when(length >= cache_rows)
    def _():
        compute(False)

    @pl.when(length < cache_rows)
    def _():
        compute(True)


def attention(length, qkv, cosine, sine_signed, k_cache, v_cache):
    new_len = qkv.shape[0]
    cache_rows = k_cache.shape[1]
    heads = qkv.shape[1] // (3 * HD)
    rows = min(256, new_len)
    grid_spec = pltpu.PrefetchScalarGridSpec(
        num_scalar_prefetch=1,
        grid=(heads, new_len // rows),
        in_specs=[
            pl.BlockSpec((rows, HD), lambda h, i, n: (i, 3 * h)),
            pl.BlockSpec((new_len, HD), lambda h, i, n: (0, 3 * h + 1)),
            pl.BlockSpec((new_len, HD), lambda h, i, n: (0, 3 * h + 2)),
            pl.BlockSpec((rows, HD), lambda h, i, n: (i, 0)),
            pl.BlockSpec((rows, HD), lambda h, i, n: (i, 0)),
            pl.BlockSpec((new_len, HD), lambda h, i, n: (0, 0)),
            pl.BlockSpec((new_len, HD), lambda h, i, n: (0, 0)),
            pl.BlockSpec((1, cache_rows, HD), lambda h, i, n: (0, 0, h)),
            pl.BlockSpec((1, cache_rows, HD), lambda h, i, n: (0, 0, h)),
        ],
        out_specs=pl.BlockSpec((rows, HD), lambda h, i, n: (i, h)),
    )
    return pl.pallas_call(
        attention_kernel,
        grid_spec=grid_spec,
        out_shape=jax.ShapeDtypeStruct((new_len, heads * HD), jnp.bfloat16),
        name="cached_attention",
    )(length, qkv, qkv, qkv, cosine, sine_signed, cosine, sine_signed, k_cache, v_cache)


def cross_perm(count, step):
    pairs = count // 2
    return [(j, ((j // 2 + step) % pairs) * 2 + j % 2) for j in range(count)]


def head_gather(block):
    count = lax.axis_size("head")
    pairs = count // 2
    index = lax.axis_index("head")
    pair, core = index // 2, index % 2
    pieces = [block] + [
        lax.ppermute(block, "head", cross_perm(count, step)) for step in range(1, pairs)
    ]
    stacked = jnp.stack(pieces)
    order = (pair - jnp.arange(pairs, dtype=jnp.int32)) % pairs
    mine = jnp.take(stacked, order, axis=0)
    partner = lax.ppermute(mine, "head", [(j, j ^ 1) for j in range(count)])
    first = jnp.where(core == 0, mine, partner)
    second = jnp.where(core == 0, partner, mine)
    return jnp.stack([first, second], axis=1).reshape((count * block.shape[0],) + block.shape[1:])


def head_scatter_sum(partial):
    count = lax.axis_size("head")
    pairs = count // 2
    index = lax.axis_index("head")
    pair, core = index // 2, index % 2
    blocks = partial.reshape((pairs, 2, partial.shape[0] // count) + partial.shape[1:])
    mine = jnp.where(core == 0, blocks[:, 0], blocks[:, 1])
    other = jnp.where(core == 0, blocks[:, 1], blocks[:, 0])
    received = lax.ppermute(other, "head", [(j, j ^ 1) for j in range(count)])
    chip_sum = mine.astype(jnp.float32) + received.astype(jnp.float32)
    result = jnp.take(chip_sum, pair, axis=0)
    for step in range(1, pairs):
        outgoing = jnp.take(chip_sum, (pair + step) % pairs, axis=0).astype(jnp.bfloat16)
        arrived = lax.ppermute(outgoing, "head", cross_perm(count, step))
        result = result + arrived.astype(jnp.float32)
    return result


def body(
    tokens,
    cache_len,
    attn_gain,
    w_qkv,
    k_cache,
    v_cache,
    w_out,
    moe_gain,
    w_shared,
    w_shared_down,
    expert_ids,
    expert_weights,
    expert_slot,
    w_expert,
    w_expert_down,
):
    req_local, qrows, width = tokens.shape
    head_count = lax.axis_size("head")
    tok_count = lax.axis_size("tok")
    new_len = qrows * head_count
    head_local = w_out.shape[0] // HD
    cache_rows = k_cache.shape[1]
    capacity = 2 * qrows * TOP // E
    slots = req_local * capacity
    local_rows = req_local * qrows
    flat_ids = expert_ids.reshape(req_local, qrows * TOP)
    hits = (flat_ids[:, :, None] == jnp.arange(E, dtype=jnp.int32)[None, None, :]).astype(jnp.int32)
    ranks = jnp.sum((jnp.cumsum(hits, axis=1) - 1) * hits, axis=2)
    slot_of = ranks + jnp.arange(req_local, dtype=jnp.int32)[:, None] * capacity
    place_of = jnp.sum(hits * expert_slot[None, None, :], axis=2)
    target = (place_of * slots + slot_of).reshape(local_rows, TOP)
    columns = jnp.arange(E * slots, dtype=jnp.int32)
    matches = (target[:, :, None] == columns[None, None, :]).astype(jnp.float32)
    placement = jnp.sum(matches, axis=1).astype(jnp.bfloat16)
    routing_matrix = jnp.sum(matches * expert_weights.reshape(local_rows, TOP)[:, :, None], axis=1)
    gathered = head_gather(tokens[0])[None]
    gathered, placement, routing_matrix = lax.optimization_barrier(
        (gathered, placement, routing_matrix)
    )
    normed = normalize(gathered, attn_gain)
    qkv = jnp.dot(normed[0], w_qkv, preferred_element_type=jnp.float32)
    length = cache_len[0]
    positions = length + jnp.arange(new_len, dtype=jnp.int32)
    half_dim = HD // 2
    freqs = 10000.0 ** (-jnp.arange(half_dim, dtype=jnp.float32) / half_dim)
    angles = positions.astype(jnp.float32)[:, None] * freqs[None, :]
    cosine = jnp.cos(angles)
    sine_part = jnp.sin(angles)
    cosine = jnp.concatenate([cosine, cosine], axis=1)
    sine_signed = jnp.concatenate([-sine_part, sine_part], axis=1)
    outputs = [attention(cache_len, qkv, cosine, sine_signed, k_cache, v_cache)]
    attn_rows = head_scatter_sum(
        jnp.dot(outputs[0], w_out, preferred_element_type=jnp.float32).astype(jnp.bfloat16)
    )[None]
    middle = (tokens.astype(jnp.float32) + attn_rows).astype(jnp.bfloat16)
    normed_mid = normalize(middle, moe_gain)
    flat_mid = normed_mid.reshape(local_rows, width)
    devices = head_count * tok_count
    per_device = max(1, E // devices)
    copies = max(1, devices // E)
    unit_count = w_expert.shape[2] // per_device
    w_down = w_expert_down.reshape(per_device, unit_count, width)
    groups = E // per_device
    placement_parts = placement.reshape(local_rows, groups, per_device, slots)
    received = []
    for c in range(per_device):
        outgoing = lax.dot_general(
            placement_parts[:, :, c].reshape(local_rows, groups * slots),
            flat_mid,
            (((0,), (0,)), ((), ())),
            preferred_element_type=jnp.float32,
        ).astype(jnp.bfloat16)
        outgoing = outgoing.reshape(groups, 1, slots, width)
        if copies > 1:
            outgoing = jnp.broadcast_to(outgoing, (groups, copies, slots, width))
        outgoing = outgoing.reshape(devices, slots, width)
        received.append(
            lax.all_to_all(outgoing, ("head", "tok"), split_axis=0, concat_axis=0, tiled=True)
        )
    received[0], shared_in = lax.optimization_barrier((received[0], normed_mid))
    gathered_mid = head_gather(shared_in[0])
    routing_parts = routing_matrix.reshape(local_rows, groups, per_device, slots)
    routed = None
    for c in range(per_device):
        w_pair = w_expert[:, :, c * unit_count : (c + 1) * unit_count]
        gate_up = jnp.einsum(
            "gsd,dju->jgsu", received[c], w_pair, preferred_element_type=jnp.float32
        )
        hidden_part = (jax.nn.silu(gate_up[0]) * gate_up[1]).astype(jnp.bfloat16)
        expert_part = jnp.einsum(
            "gsu,ud->gsd", hidden_part, w_down[c], preferred_element_type=jnp.float32
        ).astype(jnp.bfloat16)
        if c == per_device - 1:
            expert_part, gathered_mid = lax.optimization_barrier((expert_part, gathered_mid))
        back = lax.all_to_all(expert_part, ("head", "tok"), split_axis=0, concat_axis=0, tiled=True)
        summed = jnp.sum(back.reshape(groups, copies, slots, width).astype(jnp.float32), axis=1)
        part = jnp.dot(
            routing_parts[:, :, c].reshape(local_rows, groups * slots),
            summed.reshape(groups * slots, width),
            precision=lax.Precision.HIGHEST,
            preferred_element_type=jnp.float32,
        )
        routed = part if routed is None else routed + part
    routed = routed.reshape(req_local, qrows, width)
    gate_up = jnp.einsum(
        "cd,djz->jcz",
        gathered_mid,
        w_shared,
        preferred_element_type=jnp.float32,
    )
    hidden_rows = (jax.nn.silu(gate_up[0]) * gate_up[1]).astype(jnp.bfloat16)
    shared_rows = head_scatter_sum(
        jnp.dot(hidden_rows, w_shared_down, preferred_element_type=jnp.float32).astype(
            jnp.bfloat16
        )
    )[None]
    layer_out = middle.astype(jnp.float32) + shared_rows + routed
    return layer_out.astype(jnp.bfloat16)


def solution(mesh):
    return jax.shard_map(
        body,
        mesh=mesh,
        in_specs=(
            P("tok", "head", None),
            P("tok"),
            P(),
            P(None, "head"),
            P("tok", None, "head"),
            P("tok", None, "head"),
            P("head", None),
            P(),
            P(None, None, "head"),
            P("head", None),
            P("tok", "head", None),
            P("tok", "head", None),
            P(),
            P(None, None, ("head", "tok")),
            P(("head", "tok"), None),
        ),
        out_specs=P("tok", "head", None),
        check_vma=False,
    )
```

```python
import math

import jax
import jax.numpy as jnp
from jax import lax
from jax.experimental import pallas as pl
from jax.experimental.pallas import tpu as pltpu
from jax.sharding import PartitionSpec as P

HD = 128
E = 64
TOP = 6


EPS = 1e-06
NEG_BIG = -1e30


def normalize(values, gain_vector):
    wide = values.astype(jnp.float32)
    factor = lax.rsqrt(jnp.mean(wide * wide, axis=-1, keepdims=True) + EPS)
    return (wide * factor * gain_vector).astype(jnp.bfloat16)


def rotary(vectors, positions):
    half_dim = vectors.shape[-1] // 2
    freqs = 10000.0 ** (-jnp.arange(half_dim, dtype=jnp.float32) / half_dim)
    angles = positions.astype(jnp.float32)[:, None] * freqs[None, :]
    cosine = jnp.cos(angles)[:, None, :]
    sine_part = jnp.sin(angles)[:, None, :]
    lower = vectors[..., :half_dim]
    upper = vectors[..., half_dim:]
    return jnp.concatenate(
        [lower * cosine - upper * sine_part, upper * cosine + lower * sine_part], axis=-1
    )


def attend(queries, keys_new, values_new, keys_old, values_old, length):
    factor = 1.0 / math.sqrt(queries.shape[-1])
    score_old = jnp.dot(queries, keys_old.T, preferred_element_type=jnp.float32) * factor
    score_new = jnp.dot(queries, keys_new.T, preferred_element_type=jnp.float32) * factor
    old_slots = jnp.arange(keys_old.shape[0], dtype=jnp.int32)
    live_old = (old_slots < length)[None, :]
    new_slots = jnp.arange(queries.shape[0], dtype=jnp.int32)
    live_new = new_slots[None, :] <= new_slots[:, None]
    row_max = jnp.maximum(
        jnp.max(jnp.where(live_old, score_old, NEG_BIG), axis=1),
        jnp.max(jnp.where(live_new, score_new, NEG_BIG), axis=1),
    )
    prob_old = jnp.where(live_old, jnp.exp(score_old - row_max[:, None]), 0.0)
    prob_new = jnp.where(live_new, jnp.exp(score_new - row_max[:, None]), 0.0)
    denom = jnp.sum(prob_old, axis=1) + jnp.sum(prob_new, axis=1)
    weighted = jnp.dot(
        prob_old.astype(jnp.bfloat16), values_old, preferred_element_type=jnp.float32
    )
    weighted = weighted + jnp.dot(
        prob_new.astype(jnp.bfloat16), values_new, preferred_element_type=jnp.float32
    )
    return (weighted / denom[:, None]).astype(jnp.bfloat16)


def rotate(block, cosine, sine_signed):
    half = block.shape[-1] // 2
    return block * cosine + pltpu.roll(block, half, 1) * sine_signed


def attention_kernel(
    len_ref, q_ref, kn_ref, vn_ref, cq_ref, sq_ref, ck_ref, sk_ref, ko_ref, vo_ref, o_ref
):
    rows = q_ref.shape[0]
    new_len = kn_ref.shape[0]
    cache_rows = ko_ref.shape[1]
    length = len_ref[0]
    start = pl.program_id(1) * rows

    def compute(mask_cache):
        factor = 1.0 / math.sqrt(q_ref.shape[-1])
        contract = (((1,), (1,)), ((), ()))
        queries = rotate(q_ref[...], cq_ref[...], sq_ref[...]).astype(jnp.bfloat16)
        keys_new = rotate(kn_ref[...], ck_ref[...], sk_ref[...]).astype(jnp.bfloat16)
        values_new = vn_ref[...].astype(jnp.bfloat16)
        score_old = (
            lax.dot_general(queries, ko_ref[0], contract, preferred_element_type=jnp.float32)
            * factor
        )
        score_new = (
            lax.dot_general(queries, keys_new, contract, preferred_element_type=jnp.float32)
            * factor
        )
        if mask_cache:
            live_old = lax.broadcasted_iota(jnp.int32, (rows, cache_rows), 1) < length
            score_old = jnp.where(live_old, score_old, NEG_BIG)
        new_cols = lax.broadcasted_iota(jnp.int32, (rows, new_len), 1)
        new_rows = lax.broadcasted_iota(jnp.int32, (rows, new_len), 0) + start
        score_new = jnp.where(new_cols <= new_rows, score_new, NEG_BIG)
        row_max = jnp.maximum(
            jnp.max(score_old, axis=1, keepdims=True), jnp.max(score_new, axis=1, keepdims=True)
        )
        prob_old = jnp.exp(score_old - row_max)
        prob_new = jnp.exp(score_new - row_max)
        denom = jnp.sum(prob_old, axis=1, keepdims=True) + jnp.sum(
            prob_new, axis=1, keepdims=True
        )
        weighted = jnp.dot(
            prob_old.astype(jnp.bfloat16), vo_ref[0], preferred_element_type=jnp.float32
        )
        weighted = weighted + jnp.dot(
            prob_new.astype(jnp.bfloat16), values_new, preferred_element_type=jnp.float32
        )
        o_ref[...] = (weighted / denom).astype(o_ref.dtype)

    @pl.when(length >= cache_rows)
    def _():
        compute(False)

    @pl.when(length < cache_rows)
    def _():
        compute(True)


def attention(length, qkv, cosine, sine_signed, k_cache, v_cache):
    new_len = qkv.shape[0]
    cache_rows = k_cache.shape[1]
    heads = qkv.shape[1] // (3 * HD)
    rows = min(256, new_len)
    grid_spec = pltpu.PrefetchScalarGridSpec(
        num_scalar_prefetch=1,
        grid=(heads, new_len // rows),
        in_specs=[
            pl.BlockSpec((rows, HD), lambda h, i, n: (i, 3 * h)),
            pl.BlockSpec((new_len, HD), lambda h, i, n: (0, 3 * h + 1)),
            pl.BlockSpec((new_len, HD), lambda h, i, n: (0, 3 * h + 2)),
            pl.BlockSpec((rows, HD), lambda h, i, n: (i, 0)),
            pl.BlockSpec((rows, HD), lambda h, i, n: (i, 0)),
            pl.BlockSpec((new_len, HD), lambda h, i, n: (0, 0)),
            pl.BlockSpec((new_len, HD), lambda h, i, n: (0, 0)),
            pl.BlockSpec((1, cache_rows, HD), lambda h, i, n: (0, 0, h)),
            pl.BlockSpec((1, cache_rows, HD), lambda h, i, n: (0, 0, h)),
        ],
        out_specs=pl.BlockSpec((rows, HD), lambda h, i, n: (i, h)),
    )
    return pl.pallas_call(
        attention_kernel,
        grid_spec=grid_spec,
        out_shape=jax.ShapeDtypeStruct((new_len, heads * HD), jnp.bfloat16),
        name="cached_attention",
    )(length, qkv, qkv, qkv, cosine, sine_signed, cosine, sine_signed, k_cache, v_cache)


def cross_perm(count, step):
    pairs = count // 2
    return [(j, ((j // 2 + step) % pairs) * 2 + j % 2) for j in range(count)]


def head_gather(block):
    count = lax.axis_size("head")
    pairs = count // 2
    index = lax.axis_index("head")
    pair, core = index // 2, index % 2
    pieces = [block] + [
        lax.ppermute(block, "head", cross_perm(count, step)) for step in range(1, pairs)
    ]
    stacked = jnp.stack(pieces)
    order = (pair - jnp.arange(pairs, dtype=jnp.int32)) % pairs
    mine = jnp.take(stacked, order, axis=0)
    partner = lax.ppermute(mine, "head", [(j, j ^ 1) for j in range(count)])
    first = jnp.where(core == 0, mine, partner)
    second = jnp.where(core == 0, partner, mine)
    return jnp.stack([first, second], axis=1).reshape((count * block.shape[0],) + block.shape[1:])


def head_scatter_sum(partial):
    count = lax.axis_size("head")
    pairs = count // 2
    index = lax.axis_index("head")
    pair, core = index // 2, index % 2
    blocks = partial.reshape((pairs, 2, partial.shape[0] // count) + partial.shape[1:])
    mine = jnp.where(core == 0, blocks[:, 0], blocks[:, 1])
    other = jnp.where(core == 0, blocks[:, 1], blocks[:, 0])
    received = lax.ppermute(other, "head", [(j, j ^ 1) for j in range(count)])
    chip_sum = mine.astype(jnp.float32) + received.astype(jnp.float32)
    result = jnp.take(chip_sum, pair, axis=0)
    for step in range(1, pairs):
        outgoing = jnp.take(chip_sum, (pair + step) % pairs, axis=0).astype(jnp.bfloat16)
        arrived = lax.ppermute(outgoing, "head", cross_perm(count, step))
        result = result + arrived.astype(jnp.float32)
    return result


def body(
    tokens,
    cache_len,
    attn_gain,
    w_qkv,
    k_cache,
    v_cache,
    w_out,
    moe_gain,
    w_shared,
    w_shared_down,
    expert_ids,
    expert_weights,
    expert_slot,
    w_expert,
    w_expert_down,
):
    req_local, qrows, width = tokens.shape
    head_count = lax.axis_size("head")
    tok_count = lax.axis_size("tok")
    new_len = qrows * head_count
    head_local = w_out.shape[0] // HD
    cache_rows = k_cache.shape[1]
    capacity = 2 * qrows * TOP // E
    slots = req_local * capacity
    local_rows = req_local * qrows
    flat_ids = expert_ids.reshape(req_local, qrows * TOP)
    hits = (flat_ids[:, :, None] == jnp.arange(E, dtype=jnp.int32)[None, None, :]).astype(jnp.int32)
    ranks = jnp.sum((jnp.cumsum(hits, axis=1) - 1) * hits, axis=2)
    slot_of = ranks + jnp.arange(req_local, dtype=jnp.int32)[:, None] * capacity
    place_of = jnp.sum(hits * expert_slot[None, None, :], axis=2)
    target = (place_of * slots + slot_of).reshape(local_rows, TOP)
    columns = jnp.arange(E * slots, dtype=jnp.int32)
    matches = (target[:, :, None] == columns[None, None, :]).astype(jnp.float32)
    placement = jnp.sum(matches, axis=1).astype(jnp.bfloat16)
    routing_matrix = jnp.sum(matches * expert_weights.reshape(local_rows, TOP)[:, :, None], axis=1)
    gathered = head_gather(tokens[0])[None]
    gathered, placement, routing_matrix = lax.optimization_barrier(
        (gathered, placement, routing_matrix)
    )
    normed = normalize(gathered, attn_gain)
    qkv = jnp.dot(normed[0], w_qkv, preferred_element_type=jnp.float32)
    length = cache_len[0]
    positions = length + jnp.arange(new_len, dtype=jnp.int32)
    half_dim = HD // 2
    freqs = 10000.0 ** (-jnp.arange(half_dim, dtype=jnp.float32) / half_dim)
    angles = positions.astype(jnp.float32)[:, None] * freqs[None, :]
    cosine = jnp.cos(angles)
    sine_part = jnp.sin(angles)
    cosine = jnp.concatenate([cosine, cosine], axis=1)
    sine_signed = jnp.concatenate([-sine_part, sine_part], axis=1)
    outputs = [attention(cache_len, qkv, cosine, sine_signed, k_cache, v_cache)]
    attn_rows = head_scatter_sum(
        jnp.dot(outputs[0], w_out, preferred_element_type=jnp.float32).astype(jnp.bfloat16)
    )[None]
    middle = (tokens.astype(jnp.float32) + attn_rows).astype(jnp.bfloat16)
    normed_mid = normalize(middle, moe_gain)
    flat_mid = normed_mid.reshape(local_rows, width)
    devices = head_count * tok_count
    per_device = max(1, E // devices)
    copies = max(1, devices // E)
    unit_count = w_expert.shape[2] // per_device
    w_down = w_expert_down.reshape(per_device, unit_count, width)
    groups = E // per_device
    placement_parts = placement.reshape(local_rows, groups, per_device, slots)
    received = []
    for c in range(per_device):
        outgoing = lax.dot_general(
            placement_parts[:, :, c].reshape(local_rows, groups * slots),
            flat_mid,
            (((0,), (0,)), ((), ())),
            preferred_element_type=jnp.float32,
        ).astype(jnp.bfloat16)
        outgoing = outgoing.reshape(groups, 1, slots, width)
        if copies > 1:
            outgoing = jnp.broadcast_to(outgoing, (groups, copies, slots, width))
        outgoing = outgoing.reshape(devices, slots, width)
        received.append(
            lax.all_to_all(outgoing, ("head", "tok"), split_axis=0, concat_axis=0, tiled=True)
        )
    received[0], shared_in = lax.optimization_barrier((received[0], normed_mid))
    gathered_mid = head_gather(shared_in[0])
    routing_parts = routing_matrix.reshape(local_rows, groups, per_device, slots)
    routed = None
    for c in range(per_device):
        w_pair = w_expert[:, :, c * unit_count : (c + 1) * unit_count]
        gate_up = jnp.einsum(
            "gsd,dju->jgsu", received[c], w_pair, preferred_element_type=jnp.float32
        )
        hidden_part = (jax.nn.silu(gate_up[0]) * gate_up[1]).astype(jnp.bfloat16)
        expert_part = jnp.einsum(
            "gsu,ud->gsd", hidden_part, w_down[c], preferred_element_type=jnp.float32
        ).astype(jnp.bfloat16)
        if c == per_device - 1:
            expert_part, gathered_mid = lax.optimization_barrier((expert_part, gathered_mid))
        back = lax.all_to_all(expert_part, ("head", "tok"), split_axis=0, concat_axis=0, tiled=True)
        summed = jnp.sum(back.reshape(groups, copies, slots, width).astype(jnp.float32), axis=1)
        weights = routing_parts[:, :, c].reshape(local_rows, groups * slots)
        if copies == 1:
            rows_back = back.reshape(groups * slots, width)
            part = None
            for _ in range(3):
                piece = weights.astype(jnp.bfloat16)
                weights = weights - piece.astype(jnp.float32)
                term = jnp.dot(piece, rows_back, preferred_element_type=jnp.float32)
                part = term if part is None else part + term
        else:
            part = jnp.dot(
                weights,
                summed.reshape(groups * slots, width),
                precision=lax.Precision.HIGHEST,
                preferred_element_type=jnp.float32,
            )
        routed = part if routed is None else routed + part
    routed = routed.reshape(req_local, qrows, width)
    gate_up = jnp.einsum(
        "cd,djz->jcz",
        gathered_mid,
        w_shared,
        preferred_element_type=jnp.float32,
    )
    hidden_rows = (jax.nn.silu(gate_up[0]) * gate_up[1]).astype(jnp.bfloat16)
    shared_rows = head_scatter_sum(
        jnp.dot(hidden_rows, w_shared_down, preferred_element_type=jnp.float32).astype(
            jnp.bfloat16
        )
    )[None]
    layer_out = middle.astype(jnp.float32) + shared_rows + routed
    return layer_out.astype(jnp.bfloat16)


def solution(mesh):
    return jax.shard_map(
        body,
        mesh=mesh,
        in_specs=(
            P("tok", "head", None),
            P("tok"),
            P(),
            P(None, "head"),
            P("tok", None, "head"),
            P("tok", None, "head"),
            P("head", None),
            P(),
            P(None, None, "head"),
            P("head", None),
            P("tok", "head", None),
            P("tok", "head", None),
            P(),
            P(None, None, ("head", "tok")),
            P(("head", "tok"), None),
        ),
        out_specs=P("tok", "head", None),
        check_vma=False,
    )
```

```python
import math

import jax
import jax.numpy as jnp
from jax import lax
from jax.experimental import pallas as pl
from jax.experimental.pallas import tpu as pltpu
from jax.sharding import PartitionSpec as P

HD = 128
E = 64
TOP = 6


EPS = 1e-06
NEG_BIG = -1e30


def normalize(values, gain_vector):
    wide = values.astype(jnp.float32)
    factor = lax.rsqrt(jnp.mean(wide * wide, axis=-1, keepdims=True) + EPS)
    return (wide * factor * gain_vector).astype(jnp.bfloat16)


def rotary(vectors, positions):
    half_dim = vectors.shape[-1] // 2
    freqs = 10000.0 ** (-jnp.arange(half_dim, dtype=jnp.float32) / half_dim)
    angles = positions.astype(jnp.float32)[:, None] * freqs[None, :]
    cosine = jnp.cos(angles)[:, None, :]
    sine_part = jnp.sin(angles)[:, None, :]
    lower = vectors[..., :half_dim]
    upper = vectors[..., half_dim:]
    return jnp.concatenate(
        [lower * cosine - upper * sine_part, upper * cosine + lower * sine_part], axis=-1
    )


def attend(queries, keys_new, values_new, keys_old, values_old, length):
    factor = 1.0 / math.sqrt(queries.shape[-1])
    score_old = jnp.dot(queries, keys_old.T, preferred_element_type=jnp.float32) * factor
    score_new = jnp.dot(queries, keys_new.T, preferred_element_type=jnp.float32) * factor
    old_slots = jnp.arange(keys_old.shape[0], dtype=jnp.int32)
    live_old = (old_slots < length)[None, :]
    new_slots = jnp.arange(queries.shape[0], dtype=jnp.int32)
    live_new = new_slots[None, :] <= new_slots[:, None]
    row_max = jnp.maximum(
        jnp.max(jnp.where(live_old, score_old, NEG_BIG), axis=1),
        jnp.max(jnp.where(live_new, score_new, NEG_BIG), axis=1),
    )
    prob_old = jnp.where(live_old, jnp.exp(score_old - row_max[:, None]), 0.0)
    prob_new = jnp.where(live_new, jnp.exp(score_new - row_max[:, None]), 0.0)
    denom = jnp.sum(prob_old, axis=1) + jnp.sum(prob_new, axis=1)
    weighted = jnp.dot(
        prob_old.astype(jnp.bfloat16), values_old, preferred_element_type=jnp.float32
    )
    weighted = weighted + jnp.dot(
        prob_new.astype(jnp.bfloat16), values_new, preferred_element_type=jnp.float32
    )
    return (weighted / denom[:, None]).astype(jnp.bfloat16)


def rotate(block, cosine, sine_signed):
    half = block.shape[-1] // 2
    return block * cosine + pltpu.roll(block, half, 1) * sine_signed


def attention_kernel(
    len_ref, q_ref, kn_ref, vn_ref, cq_ref, sq_ref, ck_ref, sk_ref, ko_ref, vo_ref, o_ref
):
    rows = q_ref.shape[0]
    new_len = kn_ref.shape[0]
    cache_rows = ko_ref.shape[1]
    length = len_ref[0]
    start = pl.program_id(1) * rows

    def compute(mask_cache):
        factor = 1.0 / math.sqrt(q_ref.shape[-1])
        contract = (((1,), (1,)), ((), ()))
        queries = rotate(q_ref[...], cq_ref[...], sq_ref[...]).astype(jnp.bfloat16)
        keys_new = rotate(kn_ref[...], ck_ref[...], sk_ref[...]).astype(jnp.bfloat16)
        values_new = vn_ref[...].astype(jnp.bfloat16)
        score_old = (
            lax.dot_general(queries, ko_ref[0], contract, preferred_element_type=jnp.float32)
            * factor
        )
        score_new = (
            lax.dot_general(queries, keys_new, contract, preferred_element_type=jnp.float32)
            * factor
        )
        if mask_cache:
            live_old = lax.broadcasted_iota(jnp.int32, (rows, cache_rows), 1) < length
            score_old = jnp.where(live_old, score_old, NEG_BIG)
        new_cols = lax.broadcasted_iota(jnp.int32, (rows, new_len), 1)
        new_rows = lax.broadcasted_iota(jnp.int32, (rows, new_len), 0) + start
        score_new = jnp.where(new_cols <= new_rows, score_new, NEG_BIG)
        row_max = jnp.maximum(
            jnp.max(score_old, axis=1, keepdims=True), jnp.max(score_new, axis=1, keepdims=True)
        )
        prob_old = jnp.exp(score_old - row_max)
        prob_new = jnp.exp(score_new - row_max)
        denom = jnp.sum(prob_old, axis=1, keepdims=True) + jnp.sum(
            prob_new, axis=1, keepdims=True
        )
        weighted = jnp.dot(
            prob_old.astype(jnp.bfloat16), vo_ref[0], preferred_element_type=jnp.float32
        )
        weighted = weighted + jnp.dot(
            prob_new.astype(jnp.bfloat16), values_new, preferred_element_type=jnp.float32
        )
        o_ref[...] = (weighted / denom).astype(o_ref.dtype)

    @pl.when(length >= cache_rows)
    def _():
        compute(False)

    @pl.when(length < cache_rows)
    def _():
        compute(True)


def attention(length, qkv, cosine, sine_signed, k_cache, v_cache):
    new_len = qkv.shape[0]
    cache_rows = k_cache.shape[1]
    heads = qkv.shape[1] // (3 * HD)
    rows = min(512, new_len)
    grid_spec = pltpu.PrefetchScalarGridSpec(
        num_scalar_prefetch=1,
        grid=(heads, new_len // rows),
        in_specs=[
            pl.BlockSpec((rows, HD), lambda h, i, n: (i, 3 * h)),
            pl.BlockSpec((new_len, HD), lambda h, i, n: (0, 3 * h + 1)),
            pl.BlockSpec((new_len, HD), lambda h, i, n: (0, 3 * h + 2)),
            pl.BlockSpec((rows, HD), lambda h, i, n: (i, 0)),
            pl.BlockSpec((rows, HD), lambda h, i, n: (i, 0)),
            pl.BlockSpec((new_len, HD), lambda h, i, n: (0, 0)),
            pl.BlockSpec((new_len, HD), lambda h, i, n: (0, 0)),
            pl.BlockSpec((1, cache_rows, HD), lambda h, i, n: (0, 0, h)),
            pl.BlockSpec((1, cache_rows, HD), lambda h, i, n: (0, 0, h)),
        ],
        out_specs=pl.BlockSpec((rows, HD), lambda h, i, n: (i, h)),
    )
    return pl.pallas_call(
        attention_kernel,
        grid_spec=grid_spec,
        out_shape=jax.ShapeDtypeStruct((new_len, heads * HD), jnp.bfloat16),
        name="cached_attention",
    )(length, qkv, qkv, qkv, cosine, sine_signed, cosine, sine_signed, k_cache, v_cache)


def cross_perm(count, step):
    pairs = count // 2
    return [(j, ((j // 2 + step) % pairs) * 2 + j % 2) for j in range(count)]


def head_gather(block):
    count = lax.axis_size("head")
    pairs = count // 2
    index = lax.axis_index("head")
    pair, core = index // 2, index % 2
    pieces = [block] + [
        lax.ppermute(block, "head", cross_perm(count, step)) for step in range(1, pairs)
    ]
    stacked = jnp.stack(pieces)
    order = (pair - jnp.arange(pairs, dtype=jnp.int32)) % pairs
    mine = jnp.take(stacked, order, axis=0)
    partner = lax.ppermute(mine, "head", [(j, j ^ 1) for j in range(count)])
    first = jnp.where(core == 0, mine, partner)
    second = jnp.where(core == 0, partner, mine)
    return jnp.stack([first, second], axis=1).reshape((count * block.shape[0],) + block.shape[1:])


def head_scatter_sum(partial):
    count = lax.axis_size("head")
    pairs = count // 2
    index = lax.axis_index("head")
    pair, core = index // 2, index % 2
    blocks = partial.reshape((pairs, 2, partial.shape[0] // count) + partial.shape[1:])
    mine = jnp.where(core == 0, blocks[:, 0], blocks[:, 1])
    other = jnp.where(core == 0, blocks[:, 1], blocks[:, 0])
    received = lax.ppermute(other, "head", [(j, j ^ 1) for j in range(count)])
    chip_sum = mine.astype(jnp.float32) + received.astype(jnp.float32)
    result = jnp.take(chip_sum, pair, axis=0)
    for step in range(1, pairs):
        outgoing = jnp.take(chip_sum, (pair + step) % pairs, axis=0).astype(jnp.bfloat16)
        arrived = lax.ppermute(outgoing, "head", cross_perm(count, step))
        result = result + arrived.astype(jnp.float32)
    return result


def body(
    tokens,
    cache_len,
    attn_gain,
    w_qkv,
    k_cache,
    v_cache,
    w_out,
    moe_gain,
    w_shared,
    w_shared_down,
    expert_ids,
    expert_weights,
    expert_slot,
    w_expert,
    w_expert_down,
):
    req_local, qrows, width = tokens.shape
    head_count = lax.axis_size("head")
    tok_count = lax.axis_size("tok")
    new_len = qrows * head_count
    head_local = w_out.shape[0] // HD
    cache_rows = k_cache.shape[1]
    capacity = 2 * qrows * TOP // E
    slots = req_local * capacity
    local_rows = req_local * qrows
    flat_ids = expert_ids.reshape(req_local, qrows * TOP)
    hits = (flat_ids[:, :, None] == jnp.arange(E, dtype=jnp.int32)[None, None, :]).astype(jnp.int32)
    ranks = jnp.sum((jnp.cumsum(hits, axis=1) - 1) * hits, axis=2)
    slot_of = ranks + jnp.arange(req_local, dtype=jnp.int32)[:, None] * capacity
    place_of = jnp.sum(hits * expert_slot[None, None, :], axis=2)
    target = (place_of * slots + slot_of).reshape(local_rows, TOP)
    columns = jnp.arange(E * slots, dtype=jnp.int32)
    matches = (target[:, :, None] == columns[None, None, :]).astype(jnp.float32)
    placement = jnp.sum(matches, axis=1).astype(jnp.bfloat16)
    routing_matrix = jnp.sum(matches * expert_weights.reshape(local_rows, TOP)[:, :, None], axis=1)
    gathered = head_gather(tokens[0])[None]
    gathered, placement, routing_matrix = lax.optimization_barrier(
        (gathered, placement, routing_matrix)
    )
    normed = normalize(gathered, attn_gain)
    qkv = jnp.dot(normed[0], w_qkv, preferred_element_type=jnp.float32)
    length = cache_len[0]
    positions = length + jnp.arange(new_len, dtype=jnp.int32)
    half_dim = HD // 2
    freqs = 10000.0 ** (-jnp.arange(half_dim, dtype=jnp.float32) / half_dim)
    angles = positions.astype(jnp.float32)[:, None] * freqs[None, :]
    cosine = jnp.cos(angles)
    sine_part = jnp.sin(angles)
    cosine = jnp.concatenate([cosine, cosine], axis=1)
    sine_signed = jnp.concatenate([-sine_part, sine_part], axis=1)
    outputs = [attention(cache_len, qkv, cosine, sine_signed, k_cache, v_cache)]
    attn_rows = head_scatter_sum(
        jnp.dot(outputs[0], w_out, preferred_element_type=jnp.float32).astype(jnp.bfloat16)
    )[None]
    middle = (tokens.astype(jnp.float32) + attn_rows).astype(jnp.bfloat16)
    normed_mid = normalize(middle, moe_gain)
    flat_mid = normed_mid.reshape(local_rows, width)
    devices = head_count * tok_count
    per_device = max(1, E // devices)
    copies = max(1, devices // E)
    unit_count = w_expert.shape[2] // per_device
    w_down = w_expert_down.reshape(per_device, unit_count, width)
    groups = E // per_device
    placement_parts = placement.reshape(local_rows, groups, per_device, slots)
    received = []
    for c in range(per_device):
        outgoing = lax.dot_general(
            placement_parts[:, :, c].reshape(local_rows, groups * slots),
            flat_mid,
            (((0,), (0,)), ((), ())),
            preferred_element_type=jnp.float32,
        ).astype(jnp.bfloat16)
        outgoing = outgoing.reshape(groups, 1, slots, width)
        if copies > 1:
            outgoing = jnp.broadcast_to(outgoing, (groups, copies, slots, width))
        outgoing = outgoing.reshape(devices, slots, width)
        received.append(
            lax.all_to_all(outgoing, ("head", "tok"), split_axis=0, concat_axis=0, tiled=True)
        )
    received[0], shared_in = lax.optimization_barrier((received[0], normed_mid))
    gathered_mid = head_gather(shared_in[0])
    routing_parts = routing_matrix.reshape(local_rows, groups, per_device, slots)
    routed = None
    for c in range(per_device):
        w_pair = w_expert[:, :, c * unit_count : (c + 1) * unit_count]
        gate_up = jnp.einsum(
            "gsd,dju->jgsu", received[c], w_pair, preferred_element_type=jnp.float32
        )
        hidden_part = (jax.nn.silu(gate_up[0]) * gate_up[1]).astype(jnp.bfloat16)
        expert_part = jnp.einsum(
            "gsu,ud->gsd", hidden_part, w_down[c], preferred_element_type=jnp.float32
        ).astype(jnp.bfloat16)
        if c == per_device - 1:
            expert_part, gathered_mid = lax.optimization_barrier((expert_part, gathered_mid))
        back = lax.all_to_all(expert_part, ("head", "tok"), split_axis=0, concat_axis=0, tiled=True)
        summed = jnp.sum(back.reshape(groups, copies, slots, width).astype(jnp.float32), axis=1)
        part = jnp.dot(
            routing_parts[:, :, c].reshape(local_rows, groups * slots),
            summed.reshape(groups * slots, width),
            precision=lax.Precision.HIGHEST,
            preferred_element_type=jnp.float32,
        )
        routed = part if routed is None else routed + part
    routed = routed.reshape(req_local, qrows, width)
    gate_up = jnp.einsum(
        "cd,djz->jcz",
        gathered_mid,
        w_shared,
        preferred_element_type=jnp.float32,
    )
    hidden_rows = (jax.nn.silu(gate_up[0]) * gate_up[1]).astype(jnp.bfloat16)
    shared_rows = head_scatter_sum(
        jnp.dot(hidden_rows, w_shared_down, preferred_element_type=jnp.float32).astype(
            jnp.bfloat16
        )
    )[None]
    layer_out = middle.astype(jnp.float32) + shared_rows + routed
    return layer_out.astype(jnp.bfloat16)


def solution(mesh):
    return jax.shard_map(
        body,
        mesh=mesh,
        in_specs=(
            P("tok", "head", None),
            P("tok"),
            P(),
            P(None, "head"),
            P("tok", None, "head"),
            P("tok", None, "head"),
            P("head", None),
            P(),
            P(None, None, "head"),
            P("head", None),
            P("tok", "head", None),
            P("tok", "head", None),
            P(),
            P(None, None, ("head", "tok")),
            P(("head", "tok"), None),
        ),
        out_specs=P("tok", "head", None),
        check_vma=False,
    )
```
